32 devices in a mesh: row: 4 (over z), col: 8 (over y, x, core).
Axes of the slice: x: 2, y: 2, z: 4, core: 2. Of those that a mesh axis runs over, the one named last changes fastest.
Arguments:
- xn: bfloat16 [256, 2048], P('col', 'row'), may hold values from -6 to 6
- w_qkv: bfloat16 [2048, 6144], P('row', 'col'), may hold values from -0.125 to 0.125
- w_out: bfloat16 [2048, 2048], P('col', 'row'), may hold values from -0.125 to 0.125
- pool: bfloat16 [1024, 64, 4096], P('row', None, 'col'), may hold values from -136 to 136
- page_table: int32 [256, 64], P('row'), may hold values from 0 to 271
- lengths: int32 [256], P('row'), may hold values from 1 to 4096, 24576 in all
- mig_src: int32 [64], replicated, may hold values from 0 to 1023, as said below
- deal: int32 [256], replicated, may hold values from 0 to 255, each once
Outputs:
- attended: bfloat16 [256, 2048], P('col', 'row')
- landed: bfloat16 [64, 64, 4096], P('row', None, 'col')
The draws below stay inside these ranges and needn't reach their ends.
Inputs may be any that keep to these rules, and one draw needn't show every extreme that they name: `page_table`: page ids of a request refer to its own row block: below 256 its pool pages, from 256 its landing slots. `lengths`: the longest request has exactly 4096 cache tokens. `mig_src`: slot d belongs to row block d // 16; its source page lies in the pool pages of another row block. `deal`: a permutation of the requests.
All inputs are finite; a program needn't handle non-finite values. No bound on the sum of `lengths` on one device may be relied on, other than what follows from the above.
Results may differ from the reference program's by a relative error of at most 0.02.
Values may be sent and summed in bfloat16 or wider, within the bound.
No kernel may reach another device: no remote copies, remote signals or barrier semaphores. Data moves between devices by JAX's collectives and lax.ppermute only.
A program may use at most 128 MiB of HBM per device.

```python
import math
import jax
import jax.numpy as jnp
import numpy as np
from jax import lax

D = 2048
HEADS = 32
HEAD_DIM = 64
REQUESTS = 256
REQ_ROW = 64
PAGE = 64
MAXLEN = 4096
MAXP = 64
MEAN_LEN = 96
POOL_DEV = 256
LAND_DEV = 16
POOL = 1024
LANDING = 64


def draw_pool(key, part):
    shape = (POOL, PAGE, 2 * D)
    base = jnp.clip(jax.random.normal(jax.random.fold_in(key, 13), shape, jnp.float32), -6.0, 6.0)
    return base.astype(jnp.bfloat16)


def draw_mig_src(key, part):
    slots = jnp.arange(LANDING, dtype=jnp.int32)
    blocks = LANDING // LAND_DEV
    target = slots // LAND_DEV
    first_key, second_key = jax.random.split(jax.random.fold_in(key, 7))
    offset = jax.random.randint(first_key, (LANDING,), 1, blocks, dtype=jnp.int32)
    source_block = (target + offset) % blocks
    page_no = jax.random.randint(second_key, (LANDING,), 0, POOL_DEV, dtype=jnp.int32)
    return (source_block * POOL_DEV + page_no).astype(jnp.int32)


def touch_ends(result, rng, least, high):
    longest = result.shape.index(max(result.shape))
    spots = []
    for shift in (0, 1):
        where = [jax.random.randint(jax.random.fold_in(rng, axis), (), 0, length) for axis, length in enumerate(result.shape)]
        where[longest] = (where[longest] + shift) % result.shape[longest]
        spots.append(tuple(where))
    return result.at[spots[0]].set(least).at[spots[1]].set(high)


def levels(own_key, extent, cuts, low, high):
    level, own = 1.0, jax.random.fold_in(own_key, 6)
    for axis_at, blocks in cuts:
        heights = jnp.exp(jax.random.uniform(jax.random.fold_in(own, axis_at), (blocks,), jnp.float32, low / len(cuts), high / len(cuts)))
        level = level * jnp.repeat(heights, extent[axis_at] // blocks).reshape([-1 if axis == axis_at else 1 for axis in range(len(extent))])
    return level


def length_profile(number_of, total, limit, slope):
    weights = [(1 << 20) // math.isqrt(standing ** slope) + 1 for standing in range(2, number_of + 1)]
    spare, given = total - limit - (number_of - 1), [1] * (number_of - 1)
    while spare > 0:
        free = [i for i in range(number_of - 1) if given[i] < limit]
        mass, remaining = sum([weights[i] for i in free]), spare
        for i in free:
            more = min(limit - given[i], max(1, remaining * weights[i] // mass), spare)
            given[i] = given[i] + more
            spare = spare - more
    return np.array([limit] + given)


def ragged(stream_key, number_of, total, most, skew):
    if number_of == 2:
        one = jax.random.randint(stream_key, (), max(1, total - most), min(most, total - 1) + 1)
        return jnp.stack([one, total - one])
    sizes = jnp.asarray(length_profile(number_of, total, most, skew), jnp.int32)
    twos = (number_of - 1) // 2
    source_of, taker = sizes[1:1 + 2 * twos:2], sizes[2:2 + 2 * twos:2]
    room = jnp.minimum(source_of - 1, most - taker)
    passed = jax.random.randint(jax.random.fold_in(stream_key, 1), (twos,), 0, 1 << 20) % (room + 1)
    sizes = sizes.at[1:1 + 2 * twos:2].set(source_of - passed).at[2:2 + 2 * twos:2].set(taker + passed)
    return sizes[jax.random.permutation(jax.random.fold_in(stream_key, 2), number_of)]


def scatter_about(stream_key, extent, spread, most, cuts=(), kind=jnp.bfloat16):
    values = spread * jax.random.normal(stream_key, extent, jnp.float32)
    if cuts:
        values = values * levels(stream_key, extent, cuts, -0.22, 0.18)
    return jnp.clip(values, -most, most).astype(kind)


def setup_inputs(seed: int = 0) -> dict:
    arg_keys = jax.random.split(jax.random.key(seed), 9)
    return {
        "xn": scatter_about(arg_keys[0], (REQUESTS, D), 1.0, 6.0, ((0, 8), (1, 4))),
        "w_qkv": scatter_about(arg_keys[1], (D, 3 * D), D ** -0.5, 0.125, ((0, 4), (1, 8))),
        "w_out": scatter_about(arg_keys[2], (D, D), D ** -0.5, 0.125, ((0, 8), (1, 4))),
        "pool": draw_pool(jax.random.fold_in(arg_keys[8], 71), 0),
        "page_table": touch_ends(jax.random.randint(arg_keys[4], (REQUESTS, MAXP), 0, POOL_DEV + LAND_DEV), jax.random.fold_in(arg_keys[4], 1), 0, (POOL_DEV + LAND_DEV) - 1).astype(jnp.int32),
        "lengths": ragged(arg_keys[5], REQUESTS, MEAN_LEN * REQUESTS, MAXLEN, 2).astype(jnp.int32),
        "mig_src": draw_mig_src(jax.random.fold_in(arg_keys[8], 71), 0),
        "deal": jax.random.permutation(arg_keys[7], REQUESTS).astype(jnp.int32),
    }


theta_base = 130000.0
neg_large = -1.0e30


def rotate(values, positions):
    half = values.shape[-1] // 2
    freqs = theta_base ** (-(jnp.arange(half, dtype=jnp.float32) * 2.0 / values.shape[-1]))
    angles = positions.astype(jnp.float32)[:, None, None] * freqs[None, None, :]
    cosine = jnp.cos(angles)
    sine = jnp.sin(angles)
    first = values[..., :half]
    second = values[..., half:]
    return jnp.concatenate([first * cosine - second * sine, second * cosine + first * sine], axis=-1)


def reference(xn, w_qkv, w_out, pool, page_table, lengths, mig_src, deal):
    projected = jnp.dot(xn, w_qkv, preferred_element_type=jnp.float32)
    ordered = jnp.zeros_like(projected).at[deal].set(projected)
    ordered = ordered.reshape(REQUESTS, HEADS, 3, HEAD_DIM)
    query = rotate(ordered[:, :, 0], lengths).astype(jnp.bfloat16)
    key_new = rotate(ordered[:, :, 1], lengths).astype(jnp.bfloat16)
    value_new = ordered[:, :, 2].astype(jnp.bfloat16)
    landed = pool[mig_src]
    block_of = (jnp.arange(REQUESTS, dtype=jnp.int32) // REQ_ROW)[:, None]
    use_land = page_table >= POOL_DEV
    pool_ids = jnp.clip(block_of * POOL_DEV + page_table, 0, POOL - 1).astype(jnp.int32)
    land_ids = jnp.clip(block_of * LAND_DEV + page_table - POOL_DEV, 0, LANDING - 1).astype(jnp.int32)

    def one_request(items):
        q_one, k_one, v_one, p_ids, l_ids, l_use, length = items
        pages = jnp.where(l_use[:, None, None], landed[l_ids], pool[p_ids])
        pages = pages.reshape(MAXLEN, HEADS, 2, HEAD_DIM)
        keys = pages[:, :, 0].astype(jnp.float32)
        values = pages[:, :, 1].astype(jnp.float32)
        qf = q_one.astype(jnp.float32)
        scores = jnp.einsum("he,the->ht", qf, keys) * 0.125
        valid = jnp.arange(MAXLEN, dtype=jnp.int32)[None, :] < length
        scores = jnp.where(valid, scores, neg_large)
        score_new = jnp.sum(qf * k_one.astype(jnp.float32), axis=-1) * 0.125
        top = jnp.maximum(jnp.max(scores, axis=1), score_new)
        expo = jnp.where(valid, jnp.exp(scores - top[:, None]), 0.0)
        expo_new = jnp.exp(score_new - top)
        total = jnp.sum(expo, axis=1) + expo_new
        weights = lax.optimization_barrier(expo.astype(jnp.bfloat16)).astype(jnp.float32)
        weight_new = lax.optimization_barrier(expo_new.astype(jnp.bfloat16)).astype(jnp.float32)
        numer = jnp.einsum("ht,the->he", weights, values) + weight_new[:, None] * v_one.astype(jnp.float32)
        return (numer / total[:, None]).astype(jnp.bfloat16)

    mixed = lax.map(one_request, (query, key_new, value_new, pool_ids, land_ids, use_land, lengths))
    mixed = mixed.reshape(REQUESTS, D)[deal]
    attended = jnp.dot(mixed, w_out, preferred_element_type=jnp.float32).astype(jnp.bfloat16)
    return attended, landed
```

```python
import functools

import jax
import jax.numpy as jnp
from jax import lax
from jax.experimental import pallas as pl
from jax.experimental.pallas import tpu as pltpu
from jax.sharding import PartitionSpec as P

HEAD_DIM = 64
PAGE = 64


theta_base = 130000.0
neg_large = -1e30


def rotate(values, positions):
    half = values.shape[-1] // 2
    freqs = theta_base ** (-(jnp.arange(half, dtype=jnp.float32) * 2.0 / values.shape[-1]))
    angles = positions.astype(jnp.float32)[:, None, None] * freqs[None, None, :]
    cosine = jnp.cos(angles)
    sine = jnp.sin(angles)
    first = values[..., :half]
    second = values[..., half:]
    return jnp.concatenate(
        [first * cosine - second * sine, second * cosine + first * sine], axis=-1
    )


def paged_kernel(tbl, lens, qrow_ref, snew_ref, vrow_ref, pool_ref, land_ref,
                 out_ref, pages, scores, sems):
    i = pl.program_id(0)
    reqs = pl.num_programs(0)
    pool_n = pool_ref.shape[0]
    land_n = land_ref.shape[0]
    maxp = pages.shape[1]

    def start_request(r, slot):
        count = (lens[r] + PAGE - 1) // PAGE

        def body(j, carry):
            p = tbl[r * maxp + j]

            @pl.when(p < pool_n)
            def _():
                src = jnp.clip(p, 0, pool_n - 1)
                pltpu.make_async_copy(
                    pool_ref.at[src], pages.at[slot, j], sems.at[slot, j]
                ).start()

            @pl.when(p >= pool_n)
            def _():
                src = jnp.clip(p - pool_n, 0, land_n - 1)
                pltpu.make_async_copy(
                    land_ref.at[src], pages.at[slot, j], sems.at[slot, j]
                ).start()

            return carry

        lax.fori_loop(0, count, body, 0)

    @pl.when(i == 0)
    def _():
        start_request(0, 0)

    @pl.when(i + 1 < reqs)
    def _():
        start_request(i + 1, (i + 1) % 2)

    slot = i % 2
    length = lens[i]
    count = (length + PAGE - 1) // PAGE
    qrow = qrow_ref[0]
    rows = qrow.shape[0]
    pos = lax.broadcasted_iota(jnp.int32, (rows, PAGE), 1)

    def score_body(j, top):
        pltpu.make_async_copy(pool_ref.at[0], pages.at[slot, j], sems.at[slot, j]).wait()
        page = pages[slot, j]
        s = lax.dot_general(
            qrow, page, (((1,), (1,)), ((), ())), preferred_element_type=jnp.float32
        ) * 0.125
        s = jnp.where(j * PAGE + pos < length, s, neg_large)
        scores[j] = s
        return jnp.maximum(top, s)

    top = lax.fori_loop(0, count, score_body, jnp.full((rows, PAGE), neg_large, jnp.float32))
    snew = snew_ref[0][:, :1]
    top = jnp.maximum(jnp.max(top, axis=1, keepdims=True), snew)

    def value_body(j, carry):
        total, numer = carry
        s = scores[j]
        e = jnp.where(j * PAGE + pos < length, jnp.exp(s - top), 0.0)
        w = e.astype(jnp.bfloat16)
        numer = numer + jnp.dot(w, pages[slot, j], preferred_element_type=jnp.float32)
        return total + e, numer

    lanes = qrow.shape[1]
    total, numer = lax.fori_loop(
        0, count, value_body,
        (jnp.zeros((rows, PAGE), jnp.float32), jnp.zeros((rows, lanes), jnp.float32)),
    )
    e_new = jnp.exp(snew - top)
    total = jnp.sum(total, axis=1, keepdims=True) + e_new
    w_new = e_new.astype(jnp.bfloat16).astype(jnp.float32)
    numer = numer + w_new * vrow_ref[0]
    out_ref[0] = (numer / total).astype(out_ref.dtype)


def attend(query, key_new, value_new, table, lens, pool, landed):
    req_count, heads_here, _ = query.shape
    lanes = pool.shape[2]
    maxp = table.shape[1]
    rows = 8
    qf = query.astype(jnp.float32)
    score_new = jnp.sum(qf * key_new.astype(jnp.float32), axis=-1) * 0.125
    eye = jnp.eye(rows, heads_here, dtype=jnp.float32)
    zeros = jnp.zeros_like(qf)
    qrow = (eye[None, :, :, None, None] *
            jnp.stack([qf, zeros], axis=2)[:, None, :, :, :]).reshape(req_count, rows, lanes)
    qrow = qrow.astype(jnp.bfloat16)
    vf = value_new.astype(jnp.float32)
    vrow = (eye[None, :, :, None, None] *
            jnp.stack([zeros, vf], axis=2)[:, None, :, :, :]).reshape(req_count, rows, lanes)
    snew = jnp.zeros((req_count, rows, 128), jnp.float32) + jnp.pad(
        score_new, ((0, 0), (0, rows - heads_here)))[:, :, None]

    grid_spec = pltpu.PrefetchScalarGridSpec(
        num_scalar_prefetch=2,
        grid=(req_count,),
        in_specs=[
            pl.BlockSpec((1, rows, lanes), lambda i, t, l: (i, 0, 0)),
            pl.BlockSpec((1, rows, 128), lambda i, t, l: (i, 0, 0)),
            pl.BlockSpec((1, rows, lanes), lambda i, t, l: (i, 0, 0)),
            pl.BlockSpec(memory_space=pl.ANY),
            pl.BlockSpec(memory_space=pl.ANY),
        ],
        out_specs=pl.BlockSpec((1, rows, lanes), lambda i, t, l: (i, 0, 0)),
        scratch_shapes=[
            pltpu.VMEM((2, maxp, PAGE, lanes), jnp.bfloat16),
            pltpu.VMEM((maxp, rows, PAGE), jnp.float32),
            pltpu.SemaphoreType.DMA((2, maxp)),
        ],
    )
    out = pl.pallas_call(
        paged_kernel,
        grid_spec=grid_spec,
        out_shape=jax.ShapeDtypeStruct((req_count, rows, lanes), jnp.bfloat16),
        compiler_params=pltpu.CompilerParams(
            dimension_semantics=("arbitrary",), vmem_limit_bytes=48 * 1024 * 1024
        ),
    )(table.reshape(-1), lens, qrow, snew, vrow, pool, landed)
    out = out[:, :heads_here].reshape(req_count, heads_here, heads_here, 2, HEAD_DIM)
    picked = jnp.stack([out[:, h, h, 1] for h in range(heads_here)], axis=1)
    return picked


def on_device(xn, w_qkv, w_out, pool, page_table, lengths, mig_src, deal):
    heads_here = w_out.shape[0] // HEAD_DIM
    rows_all = xn.shape[0] * lax.axis_size("col")
    row_count = lax.axis_size("row")
    req_row = rows_all // row_count
    inverse = jnp.zeros((rows_all,), jnp.int32).at[deal].set(jnp.arange(rows_all, dtype=jnp.int32))
    gathered = lax.all_gather(xn, "col", axis=0, tiled=True)
    chosen = inverse
    projected = lax.psum_scatter(
        jnp.dot(jnp.take(gathered, chosen, axis=0), w_qkv, preferred_element_type=jnp.float32),
        "row",
        scatter_dimension=0,
        tiled=True,
    )
    projected = projected.reshape(req_row, heads_here, 3, HEAD_DIM)
    query = rotate(projected[:, :, 0], lengths).astype(jnp.bfloat16)
    key_new = rotate(projected[:, :, 1], lengths).astype(jnp.bfloat16)
    value_new = projected[:, :, 2].astype(jnp.bfloat16)
    my_row = lax.axis_index("row")
    pool_dev = pool.shape[0]
    land_dev = mig_src.shape[0] // row_count
    source_row = mig_src // pool_dev
    local_page = jnp.clip(mig_src - my_row * pool_dev, 0, pool_dev - 1)
    outgoing = jnp.where(
        (source_row == my_row)[:, None, None],
        jnp.take(pool, local_page, axis=0),
        jnp.zeros((), jnp.bfloat16),
    )
    outgoing = outgoing.reshape(row_count, land_dev, pool.shape[1], pool.shape[2])
    received = lax.all_to_all(outgoing, "row", split_axis=0, concat_axis=0, tiled=True)
    my_sources = lax.dynamic_slice_in_dim(source_row, my_row * land_dev, land_dev)
    landed = received[my_sources, jnp.arange(land_dev)]
    mixed = attend(query, key_new, value_new, page_table, lengths, pool, landed)
    mixed = mixed.reshape(req_row, heads_here * HEAD_DIM)
    mixed_all = lax.all_gather(mixed, "row", axis=0, tiled=True)
    chosen = deal
    attended = lax.psum_scatter(
        jnp.dot(
            jnp.take(mixed_all, chosen, axis=0), w_out, preferred_element_type=jnp.float32
        ).astype(jnp.bfloat16),
        "col",
        scatter_dimension=0,
        tiled=True,
    )
    return (attended, landed)


def solution(mesh):
    placed = (
        P("col", "row"),
        P("row", "col"),
        P("col", "row"),
        P("row", None, "col"),
        P("row", None),
        P("row"),
        P(),
        P(),
    )
    return jax.shard_map(
        on_device,
        mesh=mesh,
        in_specs=placed,
        out_specs=(P("col", "row"), P("row", None, "col")),
        check_vma=False,
    )
```

```python
import functools

import jax
import jax.numpy as jnp
from jax import lax
from jax.experimental import pallas as pl
from jax.experimental.pallas import tpu as pltpu
from jax.sharding import PartitionSpec as P

HEAD_DIM = 64
PAGE = 64


theta_base = 130000.0
neg_large = -1e30


def rotate(values, positions):
    half = values.shape[-1] // 2
    freqs = theta_base ** (-(jnp.arange(half, dtype=jnp.float32) * 2.0 / values.shape[-1]))
    angles = positions.astype(jnp.float32)[:, None, None] * freqs[None, None, :]
    cosine = jnp.cos(angles)
    sine = jnp.sin(angles)
    first = values[..., :half]
    second = values[..., half:]
    return jnp.concatenate(
        [first * cosine - second * sine, second * cosine + first * sine], axis=-1
    )


def paged_kernel(flat, starts, lens, qrow_ref, snew_ref, vrow_ref, pool_ref, land_ref,
                 out_ref, ring, scores, sems):
    reqs = qrow_ref.shape[0]
    rows, lanes = qrow_ref.shape[1], qrow_ref.shape[2]
    pool_n = pool_ref.shape[0]
    land_n = land_ref.shape[0]
    ring_n = ring.shape[0]
    total_pages = starts[reqs]
    pos = lax.broadcasted_iota(jnp.int32, (rows, PAGE), 1)

    def issue(f, carry):
        p = flat[f]
        slot = f % ring_n

        @pl.when(p < pool_n)
        def _():
            src = jnp.clip(p, 0, pool_n - 1)
            pltpu.make_async_copy(pool_ref.at[src], ring.at[slot], sems.at[slot]).start()

        @pl.when(p >= pool_n)
        def _():
            src = jnp.clip(p - pool_n, 0, land_n - 1)
            pltpu.make_async_copy(land_ref.at[src], ring.at[slot], sems.at[slot]).start()

        return carry

    def request(r, issued):
        start = starts[r]
        count = starts[r + 1] - start
        limit = jnp.minimum(total_pages, start + ring_n)
        lax.fori_loop(issued, limit, issue, 0)
        issued = jnp.maximum(issued, limit)
        length = lens[r]
        qrow = qrow_ref[r]

        def score_body(j, top):
            slot = (start + j) % ring_n
            pltpu.make_async_copy(pool_ref.at[0], ring.at[slot], sems.at[slot]).wait()
            s = lax.dot_general(
                qrow, ring[slot], (((1,), (1,)), ((), ())),
                preferred_element_type=jnp.float32,
            ) * 0.125
            s = jnp.where(j * PAGE + pos < length, s, neg_large)
            scores[j] = s
            return jnp.maximum(top, s)

        top = lax.fori_loop(0, count, score_body,
                            jnp.full((rows, PAGE), neg_large, jnp.float32))
        snew = snew_ref[r][:, :1]
        top = jnp.maximum(jnp.max(top, axis=1, keepdims=True), snew)

        def value_body(j, carry):
            total, numer = carry
            slot = (start + j) % ring_n
            e = jnp.where(j * PAGE + pos < length, jnp.exp(scores[j] - top), 0.0)
            w = e.astype(jnp.bfloat16)
            numer = numer + jnp.dot(w, ring[slot], preferred_element_type=jnp.float32)
            return total + e, numer

        total, numer = lax.fori_loop(
            0, count, value_body,
            (jnp.zeros((rows, PAGE), jnp.float32), jnp.zeros((rows, lanes), jnp.float32)),
        )
        e_new = jnp.exp(snew - top)
        total = jnp.sum(total, axis=1, keepdims=True) + e_new
        w_new = e_new.astype(jnp.bfloat16).astype(jnp.float32)
        numer = numer + w_new * vrow_ref[r]
        out_ref[r] = (numer / total).astype(out_ref.dtype)
        return issued

    lax.fori_loop(0, reqs, request, 0)


def attend(query, key_new, value_new, table, lens, pool, landed):
    req_count, heads_here, _ = query.shape
    lanes = pool.shape[2]
    maxp = table.shape[1]
    rows = 8
    qf = query.astype(jnp.float32)
    score_new = jnp.sum(qf * key_new.astype(jnp.float32), axis=-1) * 0.125
    eye = jnp.eye(rows, heads_here, dtype=jnp.float32)
    zeros = jnp.zeros_like(qf)
    qrow = (eye[None, :, :, None, None] *
            jnp.stack([qf, zeros], axis=2)[:, None, :, :, :]).reshape(req_count, rows, lanes)
    qrow = qrow.astype(jnp.bfloat16)
    vf = value_new.astype(jnp.float32)
    vrow = (eye[None, :, :, None, None] *
            jnp.stack([zeros, vf], axis=2)[:, None, :, :, :]).reshape(req_count, rows, lanes)
    snew = jnp.zeros((req_count, rows, 128), jnp.float32) + jnp.pad(
        score_new, ((0, 0), (0, rows - heads_here)))[:, :, None]

    counts = (lens + PAGE - 1) // PAGE
    starts = jnp.concatenate([jnp.zeros((1,), jnp.int32), jnp.cumsum(counts).astype(jnp.int32)])
    flat_n = req_count * maxp
    mark = jnp.zeros((flat_n,), jnp.int32).at[starts[:-1]].add(1, mode="drop")
    owner = jnp.clip(jnp.cumsum(mark) - 1, 0, req_count - 1)
    within = jnp.clip(jnp.arange(flat_n, dtype=jnp.int32) - starts[owner], 0, maxp - 1)
    flat = table.reshape(-1)[owner * maxp + within]

    full = lambda shape: pl.BlockSpec(shape, lambda i, *_: (0,) * len(shape))
    grid_spec = pltpu.PrefetchScalarGridSpec(
        num_scalar_prefetch=3,
        grid=(1,),
        in_specs=[
            full((req_count, rows, lanes)),
            full((req_count, rows, 128)),
            full((req_count, rows, lanes)),
            pl.BlockSpec(memory_space=pl.ANY),
            pl.BlockSpec(memory_space=pl.ANY),
        ],
        out_specs=full((req_count, rows, lanes)),
        scratch_shapes=[
            pltpu.VMEM((2 * maxp, PAGE, lanes), jnp.bfloat16),
            pltpu.VMEM((maxp, rows, PAGE), jnp.float32),
            pltpu.SemaphoreType.DMA((2 * maxp,)),
        ],
    )
    out = pl.pallas_call(
        paged_kernel,
        grid_spec=grid_spec,
        out_shape=jax.ShapeDtypeStruct((req_count, rows, lanes), jnp.bfloat16),
        compiler_params=pltpu.CompilerParams(
            dimension_semantics=("arbitrary",), vmem_limit_bytes=48 * 1024 * 1024
        ),
    )(flat, starts, lens, qrow, snew, vrow, pool, landed)
    out = out[:, :heads_here].reshape(req_count, heads_here, heads_here, 2, HEAD_DIM)
    picked = jnp.stack([out[:, h, h, 1] for h in range(heads_here)], axis=1)
    return picked


def on_device(xn, w_qkv, w_out, pool, page_table, lengths, mig_src, deal):
    heads_here = w_out.shape[0] // HEAD_DIM
    rows_all = xn.shape[0] * lax.axis_size("col")
    row_count = lax.axis_size("row")
    req_row = rows_all // row_count
    inverse = jnp.zeros((rows_all,), jnp.int32).at[deal].set(jnp.arange(rows_all, dtype=jnp.int32))
    gathered = lax.all_gather(xn, "col", axis=0, tiled=True)
    chosen = inverse
    projected = lax.psum_scatter(
        jnp.dot(jnp.take(gathered, chosen, axis=0), w_qkv, preferred_element_type=jnp.float32),
        "row",
        scatter_dimension=0,
        tiled=True,
    )
    projected = projected.reshape(req_row, heads_here, 3, HEAD_DIM)
    query = rotate(projected[:, :, 0], lengths).astype(jnp.bfloat16)
    key_new = rotate(projected[:, :, 1], lengths).astype(jnp.bfloat16)
    value_new = projected[:, :, 2].astype(jnp.bfloat16)
    my_row = lax.axis_index("row")
    pool_dev = pool.shape[0]
    land_dev = mig_src.shape[0] // row_count
    source_row = mig_src // pool_dev
    local_page = jnp.clip(mig_src - my_row * pool_dev, 0, pool_dev - 1)
    outgoing = jnp.where(
        (source_row == my_row)[:, None, None],
        jnp.take(pool, local_page, axis=0),
        jnp.zeros((), jnp.bfloat16),
    )
    outgoing = outgoing.reshape(row_count, land_dev, pool.shape[1], pool.shape[2])
    received = lax.all_to_all(outgoing, "row", split_axis=0, concat_axis=0, tiled=True)
    my_sources = lax.dynamic_slice_in_dim(source_row, my_row * land_dev, land_dev)
    landed = received[my_sources, jnp.arange(land_dev)]
    mixed = attend(query, key_new, value_new, page_table, lengths, pool, landed)
    mixed = mixed.reshape(req_row, heads_here * HEAD_DIM)
    mixed_all = lax.all_gather(mixed, "row", axis=0, tiled=True)
    chosen = deal
    attended = lax.psum_scatter(
        jnp.dot(
            jnp.take(mixed_all, chosen, axis=0), w_out, preferred_element_type=jnp.float32
        ).astype(jnp.bfloat16),
        "col",
        scatter_dimension=0,
        tiled=True,
    )
    return (attended, landed)


def solution(mesh):
    placed = (
        P("col", "row"),
        P("row", "col"),
        P("col", "row"),
        P("row", None, "col"),
        P("row", None),
        P("row"),
        P(),
        P(),
    )
    return jax.shard_map(
        on_device,
        mesh=mesh,
        in_specs=placed,
        out_specs=(P("col", "row"), P("row", None, "col")),
        check_vma=False,
    )
```

```python
import functools

import jax
import jax.numpy as jnp
from jax import lax
from jax.experimental import pallas as pl
from jax.experimental.pallas import tpu as pltpu
from jax.sharding import PartitionSpec as P

HEAD_DIM = 64
PAGE = 64


theta_base = 130000.0
neg_large = -1e30


def rotate(values, positions):
    half = values.shape[-1] // 2
    freqs = theta_base ** (-(jnp.arange(half, dtype=jnp.float32) * 2.0 / values.shape[-1]))
    angles = positions.astype(jnp.float32)[:, None, None] * freqs[None, None, :]
    cosine = jnp.cos(angles)
    sine = jnp.sin(angles)
    first = values[..., :half]
    second = values[..., half:]
    return jnp.concatenate(
        [first * cosine - second * sine, second * cosine + first * sine], axis=-1
    )


def issue_pages(flat, tbl, src_ref, ring, sems, lo, hi, shift):
    n = src_ref.shape[0]
    ring_n = ring.shape[0]

    def issue(f, carry):
        p = jnp.clip(tbl[flat[f]] - shift, 0, n - 1)
        slot = f % ring_n
        pltpu.make_async_copy(src_ref.at[p], ring.at[slot], sems.at[slot]).start()
        return carry

    lax.fori_loop(lo, hi, issue, 0)


def page_scores(flat, src_ref, ring, sems, scores, qrow, start, count, length, maxp):
    rows = qrow.shape[0]
    ring_n = ring.shape[0]
    pos = lax.broadcasted_iota(jnp.int32, (rows, PAGE), 1)

    def body(k, top):
        slot = (start + k) % ring_n
        pltpu.make_async_copy(src_ref.at[0], ring.at[slot], sems.at[slot]).wait()
        j = flat[start + k] % maxp
        s = lax.dot_general(
            qrow, ring[slot], (((1,), (1,)), ((), ())),
            preferred_element_type=jnp.float32,
        ) * 0.125
        s = jnp.where(j * PAGE + pos < length, s, neg_large)
        scores[k] = s
        return jnp.maximum(top, s)

    top = lax.fori_loop(0, count, body, jnp.full((rows, PAGE), neg_large, jnp.float32))
    return jnp.max(top, axis=1, keepdims=True)


def page_values(flat, ring, scores, top, start, count, length, maxp, lanes):
    rows = top.shape[0]
    ring_n = ring.shape[0]
    pos = lax.broadcasted_iota(jnp.int32, (rows, PAGE), 1)

    def body(k, carry):
        total, numer = carry
        slot = (start + k) % ring_n
        j = flat[start + k] % maxp
        e = jnp.where(j * PAGE + pos < length, jnp.exp(scores[k] - top), 0.0)
        w = e.astype(jnp.bfloat16)
        numer = numer + jnp.dot(w, ring[slot], preferred_element_type=jnp.float32)
        return total + e, numer

    total, numer = lax.fori_loop(
        0, count, body,
        (jnp.zeros((rows, PAGE), jnp.float32), jnp.zeros((rows, lanes), jnp.float32)),
    )
    return jnp.sum(total, axis=1, keepdims=True), numer


def pool_kernel(flat, starts, tbl, lens, qrow_ref, snew_ref, vrow_ref, pool_ref,
                out_ref, m_ref, l_ref, n_ref, ring, scores, sems):
    reqs, rows, lanes = qrow_ref.shape
    maxp = scores.shape[0]
    ring_n = ring.shape[0]
    total_pages = starts[reqs]

    def request(r, issued):
        start = starts[r]
        count = starts[r + 1] - start
        limit = jnp.minimum(total_pages, start + ring_n)
        issue_pages(flat, tbl, pool_ref, ring, sems, issued, limit, 0)
        issued = jnp.maximum(issued, limit)
        length = lens[r]
        snew = snew_ref[r][:, :1]
        top = page_scores(flat, pool_ref, ring, sems, scores, qrow_ref[r], start, count,
                          length, maxp)
        top = jnp.maximum(top, snew)
        total, numer = page_values(flat, ring, scores, top, start, count, length, maxp, lanes)
        e_new = jnp.exp(snew - top)
        w_new = e_new.astype(jnp.bfloat16).astype(jnp.float32)
        out_ref[r] = ((numer + w_new * vrow_ref[r]) / (total + e_new)).astype(out_ref.dtype)
        m_ref[r] = jnp.broadcast_to(top, (rows, 128))
        l_ref[r] = jnp.broadcast_to(total, (rows, 128))
        n_ref[r] = numer
        return issued

    lax.fori_loop(0, reqs, request, 0)


def land_kernel(flat, starts, tbl, lens, listed, listed_n, qrow_ref, snew_ref, vrow_ref,
                m_ref, l_ref, n_ref, prev_ref, land_ref, pool_n_ref, out_ref, ring, scores, sems):
    reqs, rows, lanes = qrow_ref.shape
    maxp = scores.shape[0]
    ring_n = ring.shape[0]
    pool_n = pool_n_ref.shape[0]
    total_pages = starts[reqs]
    out_ref[...] = prev_ref[...]

    def request(k, issued):
        r = listed[k]
        start = starts[r]
        count = starts[r + 1] - start
        limit = jnp.minimum(total_pages, start + ring_n)
        issue_pages(flat, tbl, land_ref, ring, sems, issued, limit, pool_n)
        issued = jnp.maximum(issued, limit)
        length = lens[r]
        snew = snew_ref[r][:, :1]
        top_a = m_ref[r][:, :1]
        top_b = page_scores(flat, land_ref, ring, sems, scores, qrow_ref[r], start, count,
                            length, maxp)
        top = jnp.maximum(top_a, top_b)
        total, numer = page_values(flat, ring, scores, top, start, count, length, maxp, lanes)
        scale = jnp.exp(top_a - top)
        e_new = jnp.exp(snew - top)
        w_new = e_new.astype(jnp.bfloat16).astype(jnp.float32)
        total = total + l_ref[r][:, :1] * scale + e_new
        numer = numer + n_ref[r] * scale + w_new * vrow_ref[r]
        out_ref[r] = (numer / total).astype(out_ref.dtype)
        return issued

    lax.fori_loop(0, listed_n[0], request, 0)


def page_lists(table, lens, pool_n):
    req_count, maxp = table.shape
    flat_n = req_count * maxp
    counts = (lens + PAGE - 1) // PAGE
    valid = jnp.arange(maxp, dtype=jnp.int32)[None, :] < counts[:, None]
    landing = table >= pool_n
    entry = (jnp.arange(req_count, dtype=jnp.int32)[:, None] * maxp
             + jnp.arange(maxp, dtype=jnp.int32)[None, :])
    lists = []
    for chosen in (valid & ~landing, valid & landing):
        chosen_i = chosen.astype(jnp.int32)
        per_req = jnp.sum(chosen_i, axis=1)
        starts = jnp.concatenate(
            [jnp.zeros((1,), jnp.int32), jnp.cumsum(per_req).astype(jnp.int32)])
        rank = jnp.cumsum(chosen_i, axis=1) - 1
        where = jnp.where(chosen, starts[:-1, None] + rank, flat_n)
        flat = jnp.zeros((flat_n,), jnp.int32).at[where.reshape(-1)].set(
            entry.reshape(-1), mode="drop")
        lists.append((flat, starts, per_req))
    return lists


def attend(query, key_new, value_new, table, lens, pool, landed_fn):
    req_count, heads_here, _ = query.shape
    lanes = pool.shape[2]
    maxp = table.shape[1]
    pool_n = pool.shape[0]
    rows = 8
    qf = query.astype(jnp.float32)
    score_new = jnp.sum(qf * key_new.astype(jnp.float32), axis=-1) * 0.125
    eye = jnp.eye(rows, heads_here, dtype=jnp.float32)
    zeros = jnp.zeros_like(qf)
    qrow = (eye[None, :, :, None, None] *
            jnp.stack([qf, zeros], axis=2)[:, None, :, :, :]).reshape(req_count, rows, lanes)
    qrow = qrow.astype(jnp.bfloat16)
    vf = value_new.astype(jnp.float32)
    vrow = (eye[None, :, :, None, None] *
            jnp.stack([zeros, vf], axis=2)[:, None, :, :, :]).reshape(req_count, rows, lanes)
    snew = jnp.zeros((req_count, rows, 128), jnp.float32) + jnp.pad(
        score_new, ((0, 0), (0, rows - heads_here)))[:, :, None]
    (flat_a, starts_a, _), (flat_b, starts_b, per_b) = page_lists(table, lens, pool_n)
    tbl = table.reshape(-1)

    full = lambda shape: pl.BlockSpec(shape, lambda i, *_: (0,) * len(shape))
    big = (req_count, rows, lanes)
    small = (req_count, rows, 128)
    scratch = [
        pltpu.VMEM((2 * maxp, PAGE, lanes), jnp.bfloat16),
        pltpu.VMEM((maxp, rows, PAGE), jnp.float32),
        pltpu.SemaphoreType.DMA((2 * maxp,)),
    ]
    params = pltpu.CompilerParams(
        dimension_semantics=("arbitrary",), vmem_limit_bytes=48 * 1024 * 1024)
    out_a, m_a, l_a, n_a = pl.pallas_call(
        pool_kernel,
        grid_spec=pltpu.PrefetchScalarGridSpec(
            num_scalar_prefetch=4,
            grid=(1,),
            in_specs=[full(big), full(small), full(big), pl.BlockSpec(memory_space=pl.ANY)],
            out_specs=[full(big), full(small), full(small), full(big)],
            scratch_shapes=scratch,
        ),
        out_shape=[
            jax.ShapeDtypeStruct(big, jnp.bfloat16),
            jax.ShapeDtypeStruct(small, jnp.float32),
            jax.ShapeDtypeStruct(small, jnp.float32),
            jax.ShapeDtypeStruct(big, jnp.float32),
        ],
        compiler_params=params,
    )(flat_a, starts_a, tbl, lens, qrow, snew, vrow, pool)

    landed = landed_fn()
    has_b = per_b > 0
    slot_b = jnp.where(has_b, jnp.cumsum(has_b.astype(jnp.int32)) - 1, req_count)
    listed = jnp.zeros((req_count,), jnp.int32).at[slot_b].set(
        jnp.arange(req_count, dtype=jnp.int32), mode="drop")
    listed_n = jnp.sum(has_b.astype(jnp.int32)).reshape(1)
    out = pl.pallas_call(
        land_kernel,
        grid_spec=pltpu.PrefetchScalarGridSpec(
            num_scalar_prefetch=6,
            grid=(1,),
            in_specs=[full(big), full(small), full(big), full(small), full(small), full(big),
                      full(big), pl.BlockSpec(memory_space=pl.ANY),
                      pl.BlockSpec(memory_space=pl.ANY)],
            out_specs=full(big),
            scratch_shapes=scratch,
        ),
        out_shape=jax.ShapeDtypeStruct(big, jnp.bfloat16),
        compiler_params=params,
    )(flat_b, starts_b, tbl, lens, listed, listed_n, qrow, snew, vrow, m_a, l_a, n_a, out_a,
      landed, pool)
    out = out[:, :heads_here].reshape(req_count, heads_here, heads_here, 2, HEAD_DIM)
    picked = jnp.stack([out[:, h, h, 1] for h in range(heads_here)], axis=1)
    return picked, landed


def on_device(xn, w_qkv, w_out, pool, page_table, lengths, mig_src, deal):
    heads_here = w_out.shape[0] // HEAD_DIM
    rows_all = xn.shape[0] * lax.axis_size("col")
    row_count = lax.axis_size("row")
    req_row = rows_all // row_count
    inverse = jnp.zeros((rows_all,), jnp.int32).at[deal].set(jnp.arange(rows_all, dtype=jnp.int32))
    gathered = lax.all_gather(xn, "col", axis=0, tiled=True)
    chosen = inverse
    projected = lax.psum_scatter(
        jnp.dot(jnp.take(gathered, chosen, axis=0), w_qkv, preferred_element_type=jnp.float32),
        "row",
        scatter_dimension=0,
        tiled=True,
    )
    projected = projected.reshape(req_row, heads_here, 3, HEAD_DIM)
    query = rotate(projected[:, :, 0], lengths).astype(jnp.bfloat16)
    key_new = rotate(projected[:, :, 1], lengths).astype(jnp.bfloat16)
    value_new = projected[:, :, 2].astype(jnp.bfloat16)
    def migrate():
        my_row = lax.axis_index("row")
        pool_dev = pool.shape[0]
        land_dev = mig_src.shape[0] // row_count
        source_row = mig_src // pool_dev
        local_page = jnp.clip(mig_src - my_row * pool_dev, 0, pool_dev - 1)
        outgoing = jnp.where(
            (source_row == my_row)[:, None, None],
            jnp.take(pool, local_page, axis=0),
            jnp.zeros((), jnp.bfloat16),
        )
        outgoing = outgoing.reshape(row_count, land_dev, pool.shape[1], pool.shape[2])
        received = lax.all_to_all(outgoing, "row", split_axis=0, concat_axis=0, tiled=True)
        my_sources = lax.dynamic_slice_in_dim(source_row, my_row * land_dev, land_dev)
        landed = received[my_sources, jnp.arange(land_dev)]
        return landed

    mixed, landed = attend(query, key_new, value_new, page_table, lengths, pool, migrate)
    mixed = mixed.reshape(req_row, heads_here * HEAD_DIM)
    mixed_all = lax.all_gather(mixed, "row", axis=0, tiled=True)
    chosen = deal
    attended = lax.psum_scatter(
        jnp.dot(
            jnp.take(mixed_all, chosen, axis=0), w_out, preferred_element_type=jnp.float32
        ).astype(jnp.bfloat16),
        "col",
        scatter_dimension=0,
        tiled=True,
    )
    return (attended, landed)


def solution(mesh):
    placed = (
        P("col", "row"),
        P("row", "col"),
        P("col", "row"),
        P("row", None, "col"),
        P("row", None),
        P("row"),
        P(),
        P(),
    )
    return jax.shard_map(
        on_device,
        mesh=mesh,
        in_specs=placed,
        out_specs=(P("col", "row"), P("row", None, "col")),
        check_vma=False,
    )
```

```python
import functools

import jax
import jax.numpy as jnp
from jax import lax
from jax.experimental import pallas as pl
from jax.experimental.pallas import tpu as pltpu
from jax.sharding import PartitionSpec as P

HEAD_DIM = 64
PAGE = 64


theta_base = 130000.0
neg_large = -1e30


def rotate(values, positions):
    half = values.shape[-1] // 2
    freqs = theta_base ** (-(jnp.arange(half, dtype=jnp.float32) * 2.0 / values.shape[-1]))
    angles = positions.astype(jnp.float32)[:, None, None] * freqs[None, None, :]
    cosine = jnp.cos(angles)
    sine = jnp.sin(angles)
    first = values[..., :half]
    second = values[..., half:]
    return jnp.concatenate(
        [first * cosine - second * sine, second * cosine + first * sine], axis=-1
    )


def issue_pages(flat, tbl, src_ref, ring, sems, lo, hi, shift):
    n = src_ref.shape[0]
    ring_n = ring.shape[0]

    def issue(f, carry):
        p = jnp.clip(tbl[flat[f]] - shift, 0, n - 1)
        slot = f % ring_n
        pltpu.make_async_copy(src_ref.at[p], ring.at[slot], sems.at[slot]).start()
        return carry

    lax.fori_loop(lo, hi, issue, 0)


def page_scores(flat, src_ref, ring, sems, scores, qrow, start, count, length, maxp):
    rows = qrow.shape[0]
    ring_n = ring.shape[0]
    pos = lax.broadcasted_iota(jnp.int32, (rows, PAGE), 1)

    def body(k, top):
        slot = (start + k) % ring_n
        pltpu.make_async_copy(src_ref.at[0], ring.at[slot], sems.at[slot]).wait()
        j = flat[start + k] % maxp
        s = lax.dot_general(
            qrow, ring[slot], (((1,), (1,)), ((), ())),
            preferred_element_type=jnp.float32,
        ) * 0.125
        s = jnp.where(j * PAGE + pos < length, s, neg_large)
        scores[k] = s
        return jnp.maximum(top, s)

    top = lax.fori_loop(0, count, body, jnp.full((rows, PAGE), neg_large, jnp.float32))
    return jnp.max(top, axis=1, keepdims=True)


def page_values(flat, ring, scores, top, start, count, length, maxp, lanes):
    rows = top.shape[0]
    ring_n = ring.shape[0]
    pos = lax.broadcasted_iota(jnp.int32, (rows, PAGE), 1)

    def body(k, carry):
        total, numer = carry
        slot = (start + k) % ring_n
        j = flat[start + k] % maxp
        e = jnp.where(j * PAGE + pos < length, jnp.exp(scores[k] - top), 0.0)
        w = e.astype(jnp.bfloat16)
        numer = numer + jnp.dot(w, ring[slot], preferred_element_type=jnp.float32)
        return total + e, numer

    total, numer = lax.fori_loop(
        0, count, body,
        (jnp.zeros((rows, PAGE), jnp.float32), jnp.zeros((rows, lanes), jnp.float32)),
    )
    return jnp.sum(total, axis=1, keepdims=True), numer


def build_list(tbl, lens, pool_n, maxp, reqs, flat, starts, listed, landing):
    def req(r, carry):
        n, nl = carry
        starts[r] = n
        count = (lens[r] + PAGE - 1) // PAGE

        def page(j, n):
            e = r * maxp + j
            flat[n] = e
            keep = (tbl[e] >= pool_n) if landing else (tbl[e] < pool_n)
            return n + keep.astype(jnp.int32)

        n2 = lax.fori_loop(0, count, page, n)
        listed[nl] = r
        return n2, nl + (n2 > n).astype(jnp.int32)

    n, nl = lax.fori_loop(0, reqs, req, (0, 0))
    starts[reqs] = n
    return n, nl


def pool_kernel(tbl, lens, qrow_ref, snew_ref, vrow_ref, pool_ref,
                out_ref, m_ref, l_ref, n_ref, ring, scores, sems, flat, starts, listed):
    reqs, rows, lanes = qrow_ref.shape
    maxp = scores.shape[0]
    ring_n = ring.shape[0]
    total_pages, _ = build_list(tbl, lens, pool_ref.shape[0], maxp, reqs, flat, starts,
                                listed, False)

    def request(r, issued):
        start = starts[r]
        count = starts[r + 1] - start
        limit = jnp.minimum(total_pages, start + ring_n)
        issue_pages(flat, tbl, pool_ref, ring, sems, issued, limit, 0)
        issued = jnp.maximum(issued, limit)
        length = lens[r]
        snew = snew_ref[r][:, :1]
        top = page_scores(flat, pool_ref, ring, sems, scores, qrow_ref[r], start, count,
                          length, maxp)
        top = jnp.maximum(top, snew)
        total, numer = page_values(flat, ring, scores, top, start, count, length, maxp, lanes)
        e_new = jnp.exp(snew - top)
        w_new = e_new.astype(jnp.bfloat16).astype(jnp.float32)
        out_ref[r] = ((numer + w_new * vrow_ref[r]) / (total + e_new)).astype(out_ref.dtype)
        m_ref[r] = jnp.broadcast_to(top, (rows, 128))
        l_ref[r] = jnp.broadcast_to(total, (rows, 128))
        n_ref[r] = numer
        return issued

    lax.fori_loop(0, reqs, request, 0)


def land_kernel(tbl, lens, qrow_ref, snew_ref, vrow_ref, m_ref, l_ref, n_ref, prev_ref,
                land_ref, pool_n_ref, out_ref, ring, scores, sems, flat, starts, listed):
    reqs, rows, lanes = qrow_ref.shape
    maxp = scores.shape[0]
    ring_n = ring.shape[0]
    pool_n = pool_n_ref.shape[0]
    total_pages, listed_n = build_list(tbl, lens, pool_n, maxp, reqs, flat, starts,
                                       listed, True)
    out_ref[...] = prev_ref[...]

    def request(k, issued):
        r = listed[k]
        start = starts[r]
        count = starts[r + 1] - start
        limit = jnp.minimum(total_pages, start + ring_n)
        issue_pages(flat, tbl, land_ref, ring, sems, issued, limit, pool_n)
        issued = jnp.maximum(issued, limit)
        length = lens[r]
        snew = snew_ref[r][:, :1]
        top_a = m_ref[r][:, :1]
        top_b = page_scores(flat, land_ref, ring, sems, scores, qrow_ref[r], start, count,
                            length, maxp)
        top = jnp.maximum(top_a, top_b)
        total, numer = page_values(flat, ring, scores, top, start, count, length, maxp, lanes)
        scale = jnp.exp(top_a - top)
        e_new = jnp.exp(snew - top)
        w_new = e_new.astype(jnp.bfloat16).astype(jnp.float32)
        total = total + l_ref[r][:, :1] * scale + e_new
        numer = numer + n_ref[r] * scale + w_new * vrow_ref[r]
        out_ref[r] = (numer / total).astype(out_ref.dtype)
        return issued

    lax.fori_loop(0, listed_n, request, 0)


def attend(query, key_new, value_new, table, lens, pool, landed_fn):
    req_count, heads_here, _ = query.shape
    lanes = pool.shape[2]
    maxp = table.shape[1]
    pool_n = pool.shape[0]
    rows = 8
    qf = query.astype(jnp.float32)
    score_new = jnp.sum(qf * key_new.astype(jnp.float32), axis=-1) * 0.125
    eye = jnp.eye(rows, heads_here, dtype=jnp.float32)
    zeros = jnp.zeros_like(qf)
    qrow = (eye[None, :, :, None, None] *
            jnp.stack([qf, zeros], axis=2)[:, None, :, :, :]).reshape(req_count, rows, lanes)
    qrow = qrow.astype(jnp.bfloat16)
    vf = value_new.astype(jnp.float32)
    vrow = (eye[None, :, :, None, None] *
            jnp.stack([zeros, vf], axis=2)[:, None, :, :, :]).reshape(req_count, rows, lanes)
    snew = jnp.zeros((req_count, rows, 128), jnp.float32) + jnp.pad(
        score_new, ((0, 0), (0, rows - heads_here)))[:, :, None]
    tbl = table.reshape(-1)

    full = lambda shape: pl.BlockSpec(shape, lambda i, *_: (0,) * len(shape))
    big = (req_count, rows, lanes)
    small = (req_count, rows, 128)
    scratch = [
        pltpu.VMEM((2 * maxp, PAGE, lanes), jnp.bfloat16),
        pltpu.VMEM((maxp, rows, PAGE), jnp.float32),
        pltpu.SemaphoreType.DMA((2 * maxp,)),
        pltpu.SMEM((req_count * maxp,), jnp.int32),
        pltpu.SMEM((req_count + 1,), jnp.int32),
        pltpu.SMEM((req_count,), jnp.int32),
    ]
    params = pltpu.CompilerParams(
        dimension_semantics=("arbitrary",), vmem_limit_bytes=48 * 1024 * 1024)
    out_a, m_a, l_a, n_a = pl.pallas_call(
        pool_kernel,
        grid_spec=pltpu.PrefetchScalarGridSpec(
            num_scalar_prefetch=2,
            grid=(1,),
            in_specs=[full(big), full(small), full(big), pl.BlockSpec(memory_space=pl.ANY)],
            out_specs=[full(big), full(small), full(small), full(big)],
            scratch_shapes=scratch,
        ),
        out_shape=[
            jax.ShapeDtypeStruct(big, jnp.bfloat16),
            jax.ShapeDtypeStruct(small, jnp.float32),
            jax.ShapeDtypeStruct(small, jnp.float32),
            jax.ShapeDtypeStruct(big, jnp.float32),
        ],
        compiler_params=params,
    )(tbl, lens, qrow, snew, vrow, pool)

    landed = landed_fn()
    out = pl.pallas_call(
        land_kernel,
        grid_spec=pltpu.PrefetchScalarGridSpec(
            num_scalar_prefetch=2,
            grid=(1,),
            in_specs=[full(big), full(small), full(big), full(small), full(small), full(big),
                      full(big), pl.BlockSpec(memory_space=pl.ANY),
                      pl.BlockSpec(memory_space=pl.ANY)],
            out_specs=full(big),
            scratch_shapes=scratch,
        ),
        out_shape=jax.ShapeDtypeStruct(big, jnp.bfloat16),
        compiler_params=params,
    )(tbl, lens, qrow, snew, vrow, m_a, l_a, n_a, out_a, landed, pool)
    out = out[:, :heads_here].reshape(req_count, heads_here, heads_here, 2, HEAD_DIM)
    picked = jnp.stack([out[:, h, h, 1] for h in range(heads_here)], axis=1)
    return picked, landed


def on_device(xn, w_qkv, w_out, pool, page_table, lengths, mig_src, deal):
    heads_here = w_out.shape[0] // HEAD_DIM
    rows_all = xn.shape[0] * lax.axis_size("col")
    row_count = lax.axis_size("row")
    req_row = rows_all // row_count
    inverse = jnp.zeros((rows_all,), jnp.int32).at[deal].set(jnp.arange(rows_all, dtype=jnp.int32))
    gathered = lax.all_gather(xn, "col", axis=0, tiled=True)
    chosen = inverse
    partial = jnp.dot(jnp.take(gathered, chosen, axis=0), w_qkv,
                      preferred_element_type=jnp.float32)
    parts = lax.all_to_all(partial, "row", split_axis=0, concat_axis=0, tiled=True)
    projected = jnp.sum(parts.reshape(row_count, req_row, -1), axis=0)
    projected = projected.reshape(req_row, heads_here, 3, HEAD_DIM)
    query = rotate(projected[:, :, 0], lengths).astype(jnp.bfloat16)
    key_new = rotate(projected[:, :, 1], lengths).astype(jnp.bfloat16)
    value_new = projected[:, :, 2].astype(jnp.bfloat16)
    def migrate():
        my_row = lax.axis_index("row")
        pool_dev = pool.shape[0]
        land_dev = mig_src.shape[0] // row_count
        source_row = mig_src // pool_dev
        local_page = jnp.clip(mig_src - my_row * pool_dev, 0, pool_dev - 1)
        outgoing = jnp.where(
            (source_row == my_row)[:, None, None],
            jnp.take(pool, local_page, axis=0),
            jnp.zeros((), jnp.bfloat16),
        )
        outgoing = outgoing.reshape(row_count, land_dev, pool.shape[1], pool.shape[2])
        outgoing, _ = lax.optimization_barrier((outgoing, projected))
        received = lax.all_to_all(outgoing, "row", split_axis=0, concat_axis=0, tiled=True)
        my_sources = lax.dynamic_slice_in_dim(source_row, my_row * land_dev, land_dev)
        landed = received[my_sources, jnp.arange(land_dev)]
        return landed

    mixed, landed = attend(query, key_new, value_new, page_table, lengths, pool, migrate)
    mixed = mixed.reshape(req_row, heads_here * HEAD_DIM)
    mixed_all = lax.all_gather(mixed, "row", axis=0, tiled=True)
    chosen = deal
    col_count = lax.axis_size("col")
    partial = jnp.dot(
        jnp.take(mixed_all, chosen, axis=0), w_out, preferred_element_type=jnp.float32
    ).astype(jnp.bfloat16)
    parts = lax.all_to_all(partial, "col", split_axis=0, concat_axis=0, tiled=True)
    attended = jnp.sum(
        parts.reshape(col_count, rows_all // col_count, -1).astype(jnp.float32), axis=0
    ).astype(jnp.bfloat16)
    return (attended, landed)


def solution(mesh):
    placed = (
        P("col", "row"),
        P("row", "col"),
        P("col", "row"),
        P("row", None, "col"),
        P("row", None),
        P("row"),
        P(),
        P(),
    )
    return jax.shard_map(
        on_device,
        mesh=mesh,
        in_specs=placed,
        out_specs=(P("col", "row"), P("row", None, "col")),
        check_vma=False,
    )
```

```python
import functools

import jax
import jax.numpy as jnp
from jax import lax
from jax.experimental import pallas as pl
from jax.experimental.pallas import tpu as pltpu
from jax.sharding import PartitionSpec as P

HEAD_DIM = 64
PAGE = 64


theta_base = 130000.0
neg_large = -1e30


def rotate(values, positions):
    half = values.shape[-1] // 2
    freqs = theta_base ** (-(jnp.arange(half, dtype=jnp.float32) * 2.0 / values.shape[-1]))
    angles = positions.astype(jnp.float32)[:, None, None] * freqs[None, None, :]
    cosine = jnp.cos(angles)
    sine = jnp.sin(angles)
    first = values[..., :half]
    second = values[..., half:]
    return jnp.concatenate(
        [first * cosine - second * sine, second * cosine + first * sine], axis=-1
    )


def issue_pages(flat, tbl, src_ref, ring, sems, lo, hi, shift):
    n = src_ref.shape[0]
    ring_n = ring.shape[0]

    def issue(f, carry):
        p = jnp.clip(tbl[flat[f]] - shift, 0, n - 1)
        slot = f % ring_n
        pltpu.make_async_copy(src_ref.at[p], ring.at[slot], sems.at[slot]).start()
        return carry

    lax.fori_loop(lo, hi, issue, 0)


def page_scores(flat, src_ref, ring, sems, scores, qrow, start, count, length, maxp):
    rows = qrow.shape[0]
    ring_n = ring.shape[0]
    pos = lax.broadcasted_iota(jnp.int32, (rows, PAGE), 1)

    def body(k, top):
        slot = (start + k) % ring_n
        pltpu.make_async_copy(src_ref.at[0], ring.at[slot], sems.at[slot]).wait()
        j = flat[start + k] % maxp
        s = lax.dot_general(
            qrow, ring[slot], (((1,), (1,)), ((), ())),
            preferred_element_type=jnp.float32,
        ) * 0.125
        s = jnp.where(j * PAGE + pos < length, s, neg_large)
        scores[k] = s
        return jnp.maximum(top, s)

    top = lax.fori_loop(0, count, body, jnp.full((rows, PAGE), neg_large, jnp.float32))
    return jnp.max(top, axis=1, keepdims=True)


def page_values(flat, ring, scores, top, start, count, length, maxp, lanes):
    rows = top.shape[0]
    ring_n = ring.shape[0]
    pos = lax.broadcasted_iota(jnp.int32, (rows, PAGE), 1)

    def body(k, carry):
        total, numer = carry
        slot = (start + k) % ring_n
        j = flat[start + k] % maxp
        e = jnp.where(j * PAGE + pos < length, jnp.exp(scores[k] - top), 0.0)
        w = e.astype(jnp.bfloat16)
        numer = numer + jnp.dot(w, ring[slot], preferred_element_type=jnp.float32)
        return total + e, numer

    total, numer = lax.fori_loop(
        0, count, body,
        (jnp.zeros((rows, PAGE), jnp.float32), jnp.zeros((rows, lanes), jnp.float32)),
    )
    return jnp.sum(total, axis=1, keepdims=True), numer


def build_list(tbl, lens, pool_n, maxp, reqs, flat, starts, listed, landing):
    def req(r, carry):
        n, nl = carry
        starts[r] = n
        count = (lens[r] + PAGE - 1) // PAGE

        def page(j, n):
            e = r * maxp + j
            flat[n] = e
            keep = (tbl[e] >= pool_n) if landing else (tbl[e] < pool_n)
            return n + keep.astype(jnp.int32)

        n2 = lax.fori_loop(0, count, page, n)
        listed[nl] = r
        return n2, nl + (n2 > n).astype(jnp.int32)

    n, nl = lax.fori_loop(0, reqs, req, (0, 0))
    starts[reqs] = n
    return n, nl


def pool_kernel(tbl, lens, qrow_ref, snew_ref, vrow_ref, pool_ref,
                out_ref, m_ref, l_ref, n_ref, ring, scores, sems, flat, starts, listed):
    reqs, rows, lanes = qrow_ref.shape
    maxp = scores.shape[0]
    ring_n = ring.shape[0]
    total_pages, _ = build_list(tbl, lens, pool_ref.shape[0], maxp, reqs, flat, starts,
                                listed, False)

    def request(r, issued):
        start = starts[r]
        count = starts[r + 1] - start
        limit = jnp.minimum(total_pages, start + ring_n)
        issue_pages(flat, tbl, pool_ref, ring, sems, issued, limit, 0)
        issued = jnp.maximum(issued, limit)
        length = lens[r]
        snew = snew_ref[r][:, :1]
        top = page_scores(flat, pool_ref, ring, sems, scores, qrow_ref[r], start, count,
                          length, maxp)
        top = jnp.maximum(top, snew)
        total, numer = page_values(flat, ring, scores, top, start, count, length, maxp, lanes)
        e_new = jnp.exp(snew - top)
        w_new = e_new.astype(jnp.bfloat16).astype(jnp.float32)
        out_ref[r] = ((numer + w_new * vrow_ref[r]) / (total + e_new)).astype(out_ref.dtype)
        m_ref[r] = jnp.broadcast_to(top, (rows, 128))
        l_ref[r] = jnp.broadcast_to(total, (rows, 128))
        n_ref[r] = numer
        return issued

    lax.fori_loop(0, reqs, request, 0)


def land_kernel(tbl, lens, qrow_ref, snew_ref, vrow_ref, m_ref, l_ref, n_ref, prev_ref,
                land_ref, pool_n_ref, out_ref, ring, scores, sems, flat, starts, listed):
    reqs, rows, lanes = qrow_ref.shape
    maxp = scores.shape[0]
    ring_n = ring.shape[0]
    pool_n = pool_n_ref.shape[0]
    total_pages, listed_n = build_list(tbl, lens, pool_n, maxp, reqs, flat, starts,
                                       listed, True)
    out_ref[...] = prev_ref[...]

    def request(k, issued):
        r = listed[k]
        start = starts[r]
        count = starts[r + 1] - start
        limit = jnp.minimum(total_pages, start + ring_n)
        issue_pages(flat, tbl, land_ref, ring, sems, issued, limit, pool_n)
        issued = jnp.maximum(issued, limit)
        length = lens[r]
        snew = snew_ref[r][:, :1]
        top_a = m_ref[r][:, :1]
        top_b = page_scores(flat, land_ref, ring, sems, scores, qrow_ref[r], start, count,
                            length, maxp)
        top = jnp.maximum(top_a, top_b)
        total, numer = page_values(flat, ring, scores, top, start, count, length, maxp, lanes)
        scale = jnp.exp(top_a - top)
        e_new = jnp.exp(snew - top)
        w_new = e_new.astype(jnp.bfloat16).astype(jnp.float32)
        total = total + l_ref[r][:, :1] * scale + e_new
        numer = numer + n_ref[r] * scale + w_new * vrow_ref[r]
        out_ref[r] = (numer / total).astype(out_ref.dtype)
        return issued

    lax.fori_loop(0, listed_n, request, 0)


def attend(query, key_new, value_new, table, lens, pool, landed_fn):
    req_count, heads_here, _ = query.shape
    lanes = pool.shape[2]
    maxp = table.shape[1]
    pool_n = pool.shape[0]
    rows = 8
    qf = query.astype(jnp.float32)
    score_new = jnp.sum(qf * key_new.astype(jnp.float32), axis=-1) * 0.125
    eye = jnp.eye(rows, heads_here, dtype=jnp.float32)
    zeros = jnp.zeros_like(qf)
    qrow = (eye[None, :, :, None, None] *
            jnp.stack([qf, zeros], axis=2)[:, None, :, :, :]).reshape(req_count, rows, lanes)
    qrow = qrow.astype(jnp.bfloat16)
    vf = value_new.astype(jnp.float32)
    vrow = (eye[None, :, :, None, None] *
            jnp.stack([zeros, vf], axis=2)[:, None, :, :, :]).reshape(req_count, rows, lanes)
    snew = jnp.zeros((req_count, rows, 128), jnp.float32) + jnp.pad(
        score_new, ((0, 0), (0, rows - heads_here)))[:, :, None]
    tbl = table.reshape(-1)

    full = lambda shape: pl.BlockSpec(shape, lambda i, *_: (0,) * len(shape))
    big = (req_count, rows, lanes)
    small = (req_count, rows, 128)
    scratch = [
        pltpu.VMEM((2 * maxp, PAGE, lanes), jnp.bfloat16),
        pltpu.VMEM((maxp, rows, PAGE), jnp.float32),
        pltpu.SemaphoreType.DMA((2 * maxp,)),
        pltpu.SMEM((req_count * maxp,), jnp.int32),
        pltpu.SMEM((req_count + 1,), jnp.int32),
        pltpu.SMEM((req_count,), jnp.int32),
    ]
    params = pltpu.CompilerParams(
        dimension_semantics=("arbitrary",), vmem_limit_bytes=48 * 1024 * 1024)
    out_a, m_a, l_a, n_a = pl.pallas_call(
        pool_kernel,
        grid_spec=pltpu.PrefetchScalarGridSpec(
            num_scalar_prefetch=2,
            grid=(1,),
            in_specs=[full(big), full(small), full(big), pl.BlockSpec(memory_space=pl.ANY)],
            out_specs=[full(big), full(small), full(small), full(big)],
            scratch_shapes=scratch,
        ),
        out_shape=[
            jax.ShapeDtypeStruct(big, jnp.bfloat16),
            jax.ShapeDtypeStruct(small, jnp.float32),
            jax.ShapeDtypeStruct(small, jnp.float32),
            jax.ShapeDtypeStruct(big, jnp.float32),
        ],
        compiler_params=params,
    )(tbl, lens, qrow, snew, vrow, pool)

    landed = landed_fn(out_a)
    out = pl.pallas_call(
        land_kernel,
        grid_spec=pltpu.PrefetchScalarGridSpec(
            num_scalar_prefetch=2,
            grid=(1,),
            in_specs=[full(big), full(small), full(big), full(small), full(small), full(big),
                      full(big), pl.BlockSpec(memory_space=pl.ANY),
                      pl.BlockSpec(memory_space=pl.ANY)],
            out_specs=full(big),
            scratch_shapes=scratch,
        ),
        out_shape=jax.ShapeDtypeStruct(big, jnp.bfloat16),
        compiler_params=params,
    )(tbl, lens, qrow, snew, vrow, m_a, l_a, n_a, out_a, landed, pool)
    out = out[:, :heads_here].reshape(req_count, heads_here, heads_here, 2, HEAD_DIM)
    picked = jnp.stack([out[:, h, h, 1] for h in range(heads_here)], axis=1)
    return picked, landed


def migration_plan(pool, mig_src, row_count):
    pool_dev = pool.shape[0]
    land_all = mig_src.shape[0]
    land_dev = land_all // row_count
    src_row = jnp.clip(mig_src // pool_dev, 0, row_count - 1)
    local_page = jnp.clip(mig_src - src_row * pool_dev, 0, pool_dev - 1)
    dst_row = jnp.arange(land_all, dtype=jnp.int32) // land_dev
    onehot = (src_row[:, None] == jnp.arange(row_count, dtype=jnp.int32)[None, :]).astype(jnp.int32)
    csum = jnp.cumsum(onehot.reshape(row_count, land_dev, row_count), axis=1)
    csum = csum.reshape(land_all, row_count)
    rank = jnp.sum(csum * onehot, axis=1) - 1
    return dict(src_row=src_row, local_page=local_page, dst_row=dst_row, rank=rank,
                most=jnp.max(csum), land_dev=land_dev, first=max(1, land_dev // 2))


def outgoing_pages(pool, plan, row_count, lo, size):
    my_row = lax.axis_index("row")
    rank = plan["rank"]
    sel = (plan["src_row"] == my_row) & (rank >= lo) & (rank < lo + size)
    where = jnp.where(sel, plan["dst_row"] * size + (rank - lo), row_count * size)
    idx = jnp.zeros((row_count * size,), jnp.int32).at[where].set(plan["local_page"], mode="drop")
    return jnp.take(pool, idx, axis=0).reshape(row_count, size, pool.shape[1], pool.shape[2])


def migrate_first(pool, mig_src, row_count):
    plan = migration_plan(pool, mig_src, row_count)
    sent = outgoing_pages(pool, plan, row_count, 0, plan["first"])
    return lax.all_to_all(sent, "row", split_axis=0, concat_axis=0, tiled=True)


def migrate_rest(pool, mig_src, row_count, first_recv, dep):
    plan = migration_plan(pool, mig_src, row_count)
    land_dev, k1 = plan["land_dev"], plan["first"]
    my_row = lax.axis_index("row")
    mine = my_row * land_dev + jnp.arange(land_dev, dtype=jnp.int32)
    src_mine = plan["src_row"][mine]
    rank_mine = plan["rank"][mine]
    pool_dep, _ = lax.optimization_barrier((pool, dep))
    sizes = [0] + [b for b in (1, 2, 4, 8, 16, 32, 64) if b < land_dev - k1]
    sizes = sizes + [land_dev - k1] if land_dev > k1 else sizes

    def branch(size):
        def run(pool_b, recv1):
            if size == 0:
                both = recv1
            else:
                sent = outgoing_pages(pool_b, plan, row_count, k1, size)
                recv2 = lax.all_to_all(sent, "row", split_axis=0, concat_axis=0, tiled=True)
                both = jnp.concatenate([recv1, recv2], axis=1)
            width = k1 + size
            flat = both.reshape(row_count * width, both.shape[2], both.shape[3])
            return jnp.take(flat, src_mine * width + jnp.clip(rank_mine, 0, width - 1), axis=0)
        return run

    need = jnp.maximum(plan["most"] - k1, 0)
    index = jnp.sum((jnp.array(sizes, jnp.int32) < need).astype(jnp.int32))
    return lax.switch(index, [branch(b) for b in sizes], pool_dep, first_recv)


def on_device(xn, w_qkv, w_out, pool, page_table, lengths, mig_src, deal):
    heads_here = w_out.shape[0] // HEAD_DIM
    rows_all = xn.shape[0] * lax.axis_size("col")
    row_count = lax.axis_size("row")
    req_row = rows_all // row_count
    inverse = jnp.zeros((rows_all,), jnp.int32).at[deal].set(jnp.arange(rows_all, dtype=jnp.int32))
    gathered = lax.all_gather(xn, "col", axis=0, tiled=True)
    chosen = inverse
    partial = jnp.dot(jnp.take(gathered, chosen, axis=0), w_qkv,
                      preferred_element_type=jnp.float32)
    parts = lax.all_to_all(partial, "row", split_axis=0, concat_axis=0, tiled=True)
    projected = jnp.sum(parts.reshape(row_count, req_row, -1), axis=0)
    projected = projected.reshape(req_row, heads_here, 3, HEAD_DIM)
    query = rotate(projected[:, :, 0], lengths).astype(jnp.bfloat16)
    key_new = rotate(projected[:, :, 1], lengths).astype(jnp.bfloat16)
    value_new = projected[:, :, 2].astype(jnp.bfloat16)
    first = migrate_first(pool, mig_src, row_count)
    mixed, landed = attend(query, key_new, value_new, page_table, lengths, pool,
                           lambda dep: migrate_rest(pool, mig_src, row_count, first, dep))
    mixed = mixed.reshape(req_row, heads_here * HEAD_DIM)
    mixed_all = lax.all_gather(mixed, "row", axis=0, tiled=True)
    chosen = deal
    col_count = lax.axis_size("col")
    partial = jnp.dot(
        jnp.take(mixed_all, chosen, axis=0), w_out, preferred_element_type=jnp.float32
    ).astype(jnp.bfloat16)
    parts = lax.all_to_all(partial, "col", split_axis=0, concat_axis=0, tiled=True)
    attended = jnp.sum(
        parts.reshape(col_count, rows_all // col_count, -1).astype(jnp.float32), axis=0
    ).astype(jnp.bfloat16)
    return (attended, landed)


def solution(mesh):
    placed = (
        P("col", "row"),
        P("row", "col"),
        P("col", "row"),
        P("row", None, "col"),
        P("row", None),
        P("row"),
        P(),
        P(),
    )
    return jax.shard_map(
        on_device,
        mesh=mesh,
        in_specs=placed,
        out_specs=(P("col", "row"), P("row", None, "col")),
        check_vma=False,
    )
```

```python
import functools

import jax
import jax.numpy as jnp
from jax import lax
from jax.experimental import pallas as pl
from jax.experimental.pallas import tpu as pltpu
from jax.sharding import PartitionSpec as P

HEAD_DIM = 64
PAGE = 64


theta_base = 130000.0
neg_large = -1e30


def rotate(values, positions):
    half = values.shape[-1] // 2
    freqs = theta_base ** (-(jnp.arange(half, dtype=jnp.float32) * 2.0 / values.shape[-1]))
    angles = positions.astype(jnp.float32)[:, None, None] * freqs[None, None, :]
    cosine = jnp.cos(angles)
    sine = jnp.sin(angles)
    first = values[..., :half]
    second = values[..., half:]
    return jnp.concatenate(
        [first * cosine - second * sine, second * cosine + first * sine], axis=-1
    )


def issue_pages(flat, tbl, src_ref, ring, sems, lo, hi, shift):
    n = src_ref.shape[0]
    ring_n = ring.shape[0]

    def issue(f, carry):
        p = jnp.clip(tbl[flat[f]] - shift, 0, n - 1)
        slot = f % ring_n
        pltpu.make_async_copy(src_ref.at[p], ring.at[slot], sems.at[slot]).start()
        return carry

    lax.fori_loop(lo, hi, issue, 0)


def page_scores(flat, src_ref, ring, sems, scores, qrow, start, count, length, maxp):
    rows = qrow.shape[0]
    ring_n = ring.shape[0]
    pos = lax.broadcasted_iota(jnp.int32, (rows, PAGE), 1)

    def one(k):
        slot = (start + k) % ring_n
        pltpu.make_async_copy(src_ref.at[0], ring.at[slot], sems.at[slot]).wait()
        j = flat[start + k] % maxp
        s = lax.dot_general(
            qrow, ring[slot], (((1,), (1,)), ((), ())),
            preferred_element_type=jnp.float32,
        ) * 0.125
        s = jnp.where(j * PAGE + pos < length, s, neg_large)
        scores[k] = s
        return s

    def two(k2, top):
        s0 = one(2 * k2)
        s1 = one(2 * k2 + 1)
        return jnp.maximum(top, jnp.maximum(s0, s1))

    top = lax.fori_loop(0, count // 2, two, jnp.full((rows, PAGE), neg_large, jnp.float32))
    top = lax.fori_loop(count // 2 * 2, count, lambda k, t: jnp.maximum(t, one(k)), top)
    return jnp.max(top, axis=1, keepdims=True)


def page_values(flat, ring, scores, top, start, count, length, maxp, lanes):
    rows = top.shape[0]
    ring_n = ring.shape[0]
    pos = lax.broadcasted_iota(jnp.int32, (rows, PAGE), 1)

    def one(k):
        slot = (start + k) % ring_n
        j = flat[start + k] % maxp
        e = jnp.where(j * PAGE + pos < length, jnp.exp(scores[k] - top), 0.0)
        w = e.astype(jnp.bfloat16)
        return e, jnp.dot(w, ring[slot], preferred_element_type=jnp.float32)

    def two(k2, carry):
        total, numer = carry
        e0, n0 = one(2 * k2)
        e1, n1 = one(2 * k2 + 1)
        return total + (e0 + e1), numer + (n0 + n1)

    def single(k, carry):
        total, numer = carry
        e0, n0 = one(k)
        return total + e0, numer + n0

    init = (jnp.zeros((rows, PAGE), jnp.float32), jnp.zeros((rows, lanes), jnp.float32))
    carry = lax.fori_loop(0, count // 2, two, init)
    total, numer = lax.fori_loop(count // 2 * 2, count, single, carry)
    return jnp.sum(total, axis=1, keepdims=True), numer


def build_list(tbl, lens, pool_n, maxp, reqs, flat, starts, listed, landing):
    def req(r, carry):
        n, nl = carry
        starts[r] = n
        count = (lens[r] + PAGE - 1) // PAGE

        def page(j, n):
            e = r * maxp + j
            flat[n] = e
            keep = (tbl[e] >= pool_n) if landing else (tbl[e] < pool_n)
            return n + keep.astype(jnp.int32)

        n2 = lax.fori_loop(0, count, page, n)
        listed[nl] = r
        return n2, nl + (n2 > n).astype(jnp.int32)

    n, nl = lax.fori_loop(0, reqs, req, (0, 0))
    starts[reqs] = n
    return n, nl


def pool_kernel(tbl, lens, qrow_ref, snew_ref, pool_ref,
                m_ref, l_ref, n_ref, ring, scores, sems, flat, starts, listed):
    reqs, rows, lanes = qrow_ref.shape
    maxp = scores.shape[0]
    ring_n = ring.shape[0]
    total_pages, _ = build_list(tbl, lens, pool_ref.shape[0], maxp, reqs, flat, starts,
                                listed, False)

    def request(r, issued):
        start = starts[r]
        count = starts[r + 1] - start
        limit = jnp.minimum(total_pages, start + ring_n)
        issue_pages(flat, tbl, pool_ref, ring, sems, issued, limit, 0)
        issued = jnp.maximum(issued, limit)
        length = lens[r]
        snew = snew_ref[r][:, :1]
        top = page_scores(flat, pool_ref, ring, sems, scores, qrow_ref[r], start, count,
                          length, maxp)
        top = jnp.maximum(top, snew)
        total, numer = page_values(flat, ring, scores, top, start, count, length, maxp, lanes)
        m_ref[r] = jnp.broadcast_to(top, (rows, 128))
        l_ref[r] = jnp.broadcast_to(total, (rows, 128))
        n_ref[r] = numer
        return issued

    lax.fori_loop(0, reqs, request, 0)


def land_kernel(tbl, lens, qrow_ref, m_in, l_in, n_in, land_ref, pool_n_ref,
                m_ref, l_ref, n_ref, ring, scores, sems, flat, starts, listed):
    reqs, rows, lanes = qrow_ref.shape
    maxp = scores.shape[0]
    ring_n = ring.shape[0]
    pool_n = pool_n_ref.shape[0]
    total_pages, listed_n = build_list(tbl, lens, pool_n, maxp, reqs, flat, starts,
                                       listed, True)
    m_ref[...] = m_in[...]
    l_ref[...] = l_in[...]
    n_ref[...] = n_in[...]

    def request(k, issued):
        r = listed[k]
        start = starts[r]
        count = starts[r + 1] - start
        limit = jnp.minimum(total_pages, start + ring_n)
        issue_pages(flat, tbl, land_ref, ring, sems, issued, limit, pool_n)
        issued = jnp.maximum(issued, limit)
        length = lens[r]
        top_a = m_in[r][:, :1]
        top_b = page_scores(flat, land_ref, ring, sems, scores, qrow_ref[r], start, count,
                            length, maxp)
        top = jnp.maximum(top_a, top_b)
        total, numer = page_values(flat, ring, scores, top, start, count, length, maxp, lanes)
        scale = jnp.exp(top_a - top)
        m_ref[r] = jnp.broadcast_to(top, (rows, 128))
        l_ref[r] = jnp.broadcast_to(total + l_in[r][:, :1] * scale, (rows, 128))
        n_ref[r] = numer + n_in[r] * scale
        return issued

    lax.fori_loop(0, listed_n, request, 0)


def attend(query, key_new, value_new, table, lens, pool, landed_fn):
    req_count, heads_here, _ = query.shape
    lanes = pool.shape[2]
    maxp = table.shape[1]
    pool_n = pool.shape[0]
    rows = 8
    qf = query.astype(jnp.float32)
    score_new = jnp.sum(qf * key_new.astype(jnp.float32), axis=-1) * 0.125
    eye = jnp.eye(rows, heads_here, dtype=jnp.float32)
    zeros = jnp.zeros_like(qf)
    qrow = (eye[None, :, :, None, None] *
            jnp.stack([qf, zeros], axis=2)[:, None, :, :, :]).reshape(req_count, rows, lanes)
    qrow = qrow.astype(jnp.bfloat16)
    vf = value_new.astype(jnp.float32)
    snew = jnp.zeros((req_count, rows, 128), jnp.float32) + jnp.pad(
        score_new, ((0, 0), (0, rows - heads_here)))[:, :, None]
    tbl = table.reshape(-1)

    full = lambda shape: pl.BlockSpec(shape, lambda i, *_: (0,) * len(shape))
    big = (req_count, rows, lanes)
    small = (req_count, rows, 128)
    scratch = [
        pltpu.VMEM((2 * maxp, PAGE, lanes), jnp.bfloat16),
        pltpu.VMEM((maxp, rows, PAGE), jnp.float32),
        pltpu.SemaphoreType.DMA((2 * maxp,)),
        pltpu.SMEM((req_count * maxp,), jnp.int32),
        pltpu.SMEM((req_count + 1,), jnp.int32),
        pltpu.SMEM((req_count,), jnp.int32),
    ]
    params = pltpu.CompilerParams(
        dimension_semantics=("arbitrary",), vmem_limit_bytes=48 * 1024 * 1024)
    state = [
        jax.ShapeDtypeStruct(small, jnp.float32),
        jax.ShapeDtypeStruct(small, jnp.float32),
        jax.ShapeDtypeStruct(big, jnp.float32),
    ]
    m_a, l_a, n_a = pl.pallas_call(
        pool_kernel,
        grid_spec=pltpu.PrefetchScalarGridSpec(
            num_scalar_prefetch=2,
            grid=(1,),
            in_specs=[full(big), full(small), pl.BlockSpec(memory_space=pl.ANY)],
            out_specs=[full(small), full(small), full(big)],
            scratch_shapes=scratch,
        ),
        out_shape=state,
        compiler_params=params,
    )(tbl, lens, qrow, snew, pool)

    landed = landed_fn(n_a)
    m_b, l_b, n_b = pl.pallas_call(
        land_kernel,
        grid_spec=pltpu.PrefetchScalarGridSpec(
            num_scalar_prefetch=2,
            grid=(1,),
            in_specs=[full(big), full(small), full(small), full(big),
                      pl.BlockSpec(memory_space=pl.ANY), pl.BlockSpec(memory_space=pl.ANY)],
            out_specs=[full(small), full(small), full(big)],
            scratch_shapes=scratch,
        ),
        out_shape=state,
        compiler_params=params,
    )(tbl, lens, qrow, m_a, l_a, n_a, landed, pool)
    top = m_b[:, :heads_here, :1]
    e_new = jnp.exp(score_new[:, :, None] - top)
    w_new = e_new.astype(jnp.bfloat16).astype(jnp.float32)
    numer = n_b[:, :heads_here].reshape(req_count, heads_here, heads_here, 2, HEAD_DIM)
    numer = jnp.stack([numer[:, h, h, 1] for h in range(heads_here)], axis=1)
    picked = ((numer + w_new * vf) / (l_b[:, :heads_here, :1] + e_new)).astype(jnp.bfloat16)
    return picked, landed


def migration_plan(pool, mig_src, row_count):
    pool_dev = pool.shape[0]
    land_all = mig_src.shape[0]
    land_dev = land_all // row_count
    src_row = jnp.clip(mig_src // pool_dev, 0, row_count - 1)
    local_page = jnp.clip(mig_src - src_row * pool_dev, 0, pool_dev - 1)
    dst_row = jnp.arange(land_all, dtype=jnp.int32) // land_dev
    onehot = (src_row[:, None] == jnp.arange(row_count, dtype=jnp.int32)[None, :]).astype(jnp.int32)
    csum = jnp.cumsum(onehot.reshape(row_count, land_dev, row_count), axis=1)
    csum = csum.reshape(land_all, row_count)
    rank = jnp.sum(csum * onehot, axis=1) - 1
    return dict(src_row=src_row, local_page=local_page, dst_row=dst_row, rank=rank,
                most=jnp.max(csum), land_dev=land_dev, first=max(1, (land_dev * 5 + 7) // 8))


def outgoing_pages(pool, plan, row_count, lo, size):
    my_row = lax.axis_index("row")
    rank = plan["rank"]
    sel = (plan["src_row"] == my_row) & (rank >= lo) & (rank < lo + size)
    where = jnp.where(sel, plan["dst_row"] * size + (rank - lo), row_count * size)
    idx = jnp.zeros((row_count * size,), jnp.int32).at[where].set(plan["local_page"], mode="drop")
    return jnp.take(pool, idx, axis=0).reshape(row_count, size, pool.shape[1], pool.shape[2])


def migrate_first(pool, mig_src, row_count):
    plan = migration_plan(pool, mig_src, row_count)
    sent = outgoing_pages(pool, plan, row_count, 0, plan["first"])
    return lax.all_to_all(sent, "row", split_axis=0, concat_axis=0, tiled=True)


def migrate_rest(pool, mig_src, row_count, first_recv, dep):
    plan = migration_plan(pool, mig_src, row_count)
    land_dev, k1 = plan["land_dev"], plan["first"]
    my_row = lax.axis_index("row")
    mine = my_row * land_dev + jnp.arange(land_dev, dtype=jnp.int32)
    src_mine = plan["src_row"][mine]
    rank_mine = plan["rank"][mine]
    pool_dep, _ = lax.optimization_barrier((pool, dep))
    sizes = [0, land_dev - k1] if land_dev > k1 else [0]

    def branch(size):
        def run(pool_b, recv1):
            if size == 0:
                both = recv1
            else:
                sent = outgoing_pages(pool_b, plan, row_count, k1, size)
                recv2 = lax.all_to_all(sent, "row", split_axis=0, concat_axis=0, tiled=True)
                both = jnp.concatenate([recv1, recv2], axis=1)
            width = k1 + size
            flat = both.reshape(row_count * width, both.shape[2], both.shape[3])
            return jnp.take(flat, src_mine * width + jnp.clip(rank_mine, 0, width - 1), axis=0)
        return run

    need = jnp.maximum(plan["most"] - k1, 0)
    index = jnp.sum((jnp.array(sizes, jnp.int32) < need).astype(jnp.int32))
    return lax.switch(index, [branch(b) for b in sizes], pool_dep, first_recv)


def on_device(xn, w_qkv, w_out, pool, page_table, lengths, mig_src, deal):
    heads_here = w_out.shape[0] // HEAD_DIM
    rows_all = xn.shape[0] * lax.axis_size("col")
    row_count = lax.axis_size("row")
    req_row = rows_all // row_count
    inverse = jnp.zeros((rows_all,), jnp.int32).at[deal].set(jnp.arange(rows_all, dtype=jnp.int32))
    gathered = lax.all_gather(xn, "col", axis=0, tiled=True)
    chosen = inverse
    partial = jnp.dot(jnp.take(gathered, chosen, axis=0), w_qkv,
                      preferred_element_type=jnp.float32)
    parts = lax.all_to_all(partial, "row", split_axis=0, concat_axis=0, tiled=True)
    projected = jnp.sum(parts.reshape(row_count, req_row, -1), axis=0)
    projected = projected.reshape(req_row, heads_here, 3, HEAD_DIM)
    query = rotate(projected[:, :, 0], lengths).astype(jnp.bfloat16)
    key_new = rotate(projected[:, :, 1], lengths).astype(jnp.bfloat16)
    value_new = projected[:, :, 2].astype(jnp.bfloat16)
    first = migrate_first(pool, mig_src, row_count)
    mixed, landed = attend(query, key_new, value_new, page_table, lengths, pool,
                           lambda dep: migrate_rest(pool, mig_src, row_count, first, dep))
    mixed = mixed.reshape(req_row, heads_here * HEAD_DIM)
    mixed_all = lax.all_gather(mixed, "row", axis=0, tiled=True)
    chosen = deal
    col_count = lax.axis_size("col")
    partial = jnp.dot(
        jnp.take(mixed_all, chosen, axis=0), w_out, preferred_element_type=jnp.float32
    ).astype(jnp.bfloat16)
    parts = lax.all_to_all(partial, "col", split_axis=0, concat_axis=0, tiled=True)
    attended = jnp.sum(
        parts.reshape(col_count, rows_all // col_count, -1).astype(jnp.float32), axis=0
    ).astype(jnp.bfloat16)
    return (attended, landed)


def solution(mesh):
    placed = (
        P("col", "row"),
        P("row", "col"),
        P("col", "row"),
        P("row", None, "col"),
        P("row", None),
        P("row"),
        P(),
        P(),
    )
    return jax.shard_map(
        on_device,
        mesh=mesh,
        in_specs=placed,
        out_specs=(P("col", "row"), P("row", None, "col")),
        check_vma=False,
    )
```

```python
import functools

import jax
import jax.numpy as jnp
from jax import lax
from jax.experimental import pallas as pl
from jax.experimental.pallas import tpu as pltpu
from jax.sharding import PartitionSpec as P

HEAD_DIM = 64
PAGE = 64


theta_base = 130000.0
neg_large = -1e30


def rotate(values, positions):
    half = values.shape[-1] // 2
    freqs = theta_base ** (-(jnp.arange(half, dtype=jnp.float32) * 2.0 / values.shape[-1]))
    angles = positions.astype(jnp.float32)[:, None, None] * freqs[None, None, :]
    cosine = jnp.cos(angles)
    sine = jnp.sin(angles)
    first = values[..., :half]
    second = values[..., half:]
    return jnp.concatenate(
        [first * cosine - second * sine, second * cosine + first * sine], axis=-1
    )


def page_scores(page_of, flat, scores, qrow, start, count, length, maxp):
    rows = qrow.shape[0]
    pos = lax.broadcasted_iota(jnp.int32, (rows, PAGE), 1)

    def one(k):
        j = flat[start + k] % maxp
        s = lax.dot_general(
            qrow, page_of(start + k), (((1,), (1,)), ((), ())),
            preferred_element_type=jnp.float32,
        ) * 0.125
        s = jnp.where(j * PAGE + pos < length, s, neg_large)
        scores[k] = s
        return s

    def two(k2, top):
        s0 = one(2 * k2)
        s1 = one(2 * k2 + 1)
        return jnp.maximum(top, jnp.maximum(s0, s1))

    top = lax.fori_loop(0, count // 2, two, jnp.full((rows, PAGE), neg_large, jnp.float32))
    top = lax.fori_loop(count // 2 * 2, count, lambda k, t: jnp.maximum(t, one(k)), top)
    return jnp.max(top, axis=1, keepdims=True)


def page_values(page_of, flat, scores, top, start, count, length, maxp, lanes):
    rows = top.shape[0]
    pos = lax.broadcasted_iota(jnp.int32, (rows, PAGE), 1)

    def one(k):
        j = flat[start + k] % maxp
        e = jnp.where(j * PAGE + pos < length, jnp.exp(scores[k] - top), 0.0)
        w = e.astype(jnp.bfloat16)
        return e, jnp.dot(w, page_of(start + k), preferred_element_type=jnp.float32)

    def two(k2, carry):
        total, numer = carry
        e0, n0 = one(2 * k2)
        e1, n1 = one(2 * k2 + 1)
        return total + (e0 + e1), numer + (n0 + n1)

    def single(k, carry):
        total, numer = carry
        e0, n0 = one(k)
        return total + e0, numer + n0

    init = (jnp.zeros((rows, PAGE), jnp.float32), jnp.zeros((rows, lanes), jnp.float32))
    carry = lax.fori_loop(0, count // 2, two, init)
    total, numer = lax.fori_loop(count // 2 * 2, count, single, carry)
    return jnp.sum(total, axis=1, keepdims=True), numer


def build_list(tbl, lens, pool_n, maxp, reqs, flat, starts, listed, landing):
    def req(r, carry):
        n, nl = carry
        starts[r] = n
        count = (lens[r] + PAGE - 1) // PAGE

        def page(j, n):
            e = r * maxp + j
            flat[n] = e
            keep = (tbl[e] >= pool_n) if landing else (tbl[e] < pool_n)
            return n + keep.astype(jnp.int32)

        n2 = lax.fori_loop(0, count, page, n)
        listed[nl] = r
        return n2, nl + (n2 > n).astype(jnp.int32)

    n, nl = lax.fori_loop(0, reqs, req, (0, 0))
    starts[reqs] = n
    return n, nl


def pool_kernel(tbl, lens, qrow_ref, snew_ref, pool_ref,
                m_ref, l_ref, n_ref, scores, flat, starts, listed):
    reqs, rows, lanes = qrow_ref.shape
    maxp = scores.shape[0]
    pool_n = pool_ref.shape[0]
    build_list(tbl, lens, pool_n, maxp, reqs, flat, starts, listed, False)
    page_of = lambda f: pool_ref[jnp.clip(tbl[flat[f]], 0, pool_n - 1)]

    def request(r, carry):
        start = starts[r]
        count = starts[r + 1] - start
        length = lens[r]
        snew = snew_ref[r][:, :1]
        top = page_scores(page_of, flat, scores, qrow_ref[r], start, count, length, maxp)
        top = jnp.maximum(top, snew)
        total, numer = page_values(page_of, flat, scores, top, start, count, length, maxp,
                                   lanes)
        m_ref[r] = jnp.broadcast_to(top, (rows, 128))
        l_ref[r] = jnp.broadcast_to(total, (rows, 128))
        n_ref[r] = numer
        return carry

    lax.fori_loop(0, reqs, request, 0)


def land_kernel(tbl, lens, qrow_ref, m_in, l_in, n_in, land_ref, pool_n_ref,
                m_ref, l_ref, n_ref, scores, flat, starts, listed):
    reqs, rows, lanes = qrow_ref.shape
    maxp = scores.shape[0]
    pool_n = pool_n_ref.shape[0]
    land_n = land_ref.shape[0]
    _, listed_n = build_list(tbl, lens, pool_n, maxp, reqs, flat, starts, listed, True)
    m_ref[...] = m_in[...]
    l_ref[...] = l_in[...]
    n_ref[...] = n_in[...]
    page_of = lambda f: land_ref[jnp.clip(tbl[flat[f]] - pool_n, 0, land_n - 1)]

    def request(k, carry):
        r = listed[k]
        start = starts[r]
        count = starts[r + 1] - start
        length = lens[r]
        top_a = m_in[r][:, :1]
        top_b = page_scores(page_of, flat, scores, qrow_ref[r], start, count, length, maxp)
        top = jnp.maximum(top_a, top_b)
        total, numer = page_values(page_of, flat, scores, top, start, count, length, maxp,
                                   lanes)
        scale = jnp.exp(top_a - top)
        m_ref[r] = jnp.broadcast_to(top, (rows, 128))
        l_ref[r] = jnp.broadcast_to(total + l_in[r][:, :1] * scale, (rows, 128))
        n_ref[r] = numer + n_in[r] * scale
        return carry

    lax.fori_loop(0, listed_n, request, 0)


def attend(query, key_new, value_new, table, lens, pool, landed_fn):
    req_count, heads_here, _ = query.shape
    lanes = pool.shape[2]
    maxp = table.shape[1]
    pool_n = pool.shape[0]
    rows = 8
    qf = query.astype(jnp.float32)
    score_new = jnp.sum(qf * key_new.astype(jnp.float32), axis=-1) * 0.125
    eye = jnp.eye(rows, heads_here, dtype=jnp.float32)
    zeros = jnp.zeros_like(qf)
    qrow = (eye[None, :, :, None, None] *
            jnp.stack([qf, zeros], axis=2)[:, None, :, :, :]).reshape(req_count, rows, lanes)
    qrow = qrow.astype(jnp.bfloat16)
    vf = value_new.astype(jnp.float32)
    snew = jnp.zeros((req_count, rows, 128), jnp.float32) + jnp.pad(
        score_new, ((0, 0), (0, rows - heads_here)))[:, :, None]
    tbl = table.reshape(-1)

    full = lambda shape: pl.BlockSpec(shape, lambda i, *_: (0,) * len(shape))
    big = (req_count, rows, lanes)
    small = (req_count, rows, 128)
    scratch = [
        pltpu.VMEM((maxp, rows, PAGE), jnp.float32),
        pltpu.SMEM((req_count * maxp,), jnp.int32),
        pltpu.SMEM((req_count + 1,), jnp.int32),
        pltpu.SMEM((req_count,), jnp.int32),
    ]
    params = pltpu.CompilerParams(
        dimension_semantics=("arbitrary",), vmem_limit_bytes=60 * 1024 * 1024)
    state = [
        jax.ShapeDtypeStruct(small, jnp.float32),
        jax.ShapeDtypeStruct(small, jnp.float32),
        jax.ShapeDtypeStruct(big, jnp.float32),
    ]
    m_a, l_a, n_a = pl.pallas_call(
        pool_kernel,
        grid_spec=pltpu.PrefetchScalarGridSpec(
            num_scalar_prefetch=2,
            grid=(1,),
            in_specs=[full(big), full(small), pl.BlockSpec(memory_space=pltpu.VMEM)],
            out_specs=[full(small), full(small), full(big)],
            scratch_shapes=scratch,
        ),
        out_shape=state,
        compiler_params=params,
    )(tbl, lens, qrow, snew, pool)

    landed = landed_fn(n_a)
    m_b, l_b, n_b = pl.pallas_call(
        land_kernel,
        grid_spec=pltpu.PrefetchScalarGridSpec(
            num_scalar_prefetch=2,
            grid=(1,),
            in_specs=[full(big), full(small), full(small), full(big),
                      pl.BlockSpec(memory_space=pltpu.VMEM), pl.BlockSpec(memory_space=pl.ANY)],
            out_specs=[full(small), full(small), full(big)],
            scratch_shapes=scratch,
        ),
        out_shape=state,
        compiler_params=params,
    )(tbl, lens, qrow, m_a, l_a, n_a, landed, pool)
    top = m_b[:, :heads_here, :1]
    e_new = jnp.exp(score_new[:, :, None] - top)
    w_new = e_new.astype(jnp.bfloat16).astype(jnp.float32)
    numer = n_b[:, :heads_here].reshape(req_count, heads_here, heads_here, 2, HEAD_DIM)
    numer = jnp.stack([numer[:, h, h, 1] for h in range(heads_here)], axis=1)
    picked = ((numer + w_new * vf) / (l_b[:, :heads_here, :1] + e_new)).astype(jnp.bfloat16)
    return picked, landed


def migration_plan(pool, mig_src, row_count):
    pool_dev = pool.shape[0]
    land_all = mig_src.shape[0]
    land_dev = land_all // row_count
    src_row = jnp.clip(mig_src // pool_dev, 0, row_count - 1)
    local_page = jnp.clip(mig_src - src_row * pool_dev, 0, pool_dev - 1)
    dst_row = jnp.arange(land_all, dtype=jnp.int32) // land_dev
    onehot = (src_row[:, None] == jnp.arange(row_count, dtype=jnp.int32)[None, :]).astype(jnp.int32)
    csum = jnp.cumsum(onehot.reshape(row_count, land_dev, row_count), axis=1)
    csum = csum.reshape(land_all, row_count)
    rank = jnp.sum(csum * onehot, axis=1) - 1
    return dict(src_row=src_row, local_page=local_page, dst_row=dst_row, rank=rank,
                most=jnp.max(csum), land_dev=land_dev, first=max(1, (land_dev * 5 + 7) // 8))


def outgoing_pages(pool, plan, row_count, lo, size):
    my_row = lax.axis_index("row")
    rank = plan["rank"]
    sel = (plan["src_row"] == my_row) & (rank >= lo) & (rank < lo + size)
    where = jnp.where(sel, plan["dst_row"] * size + (rank - lo), row_count * size)
    idx = jnp.zeros((row_count * size,), jnp.int32).at[where].set(plan["local_page"], mode="drop")
    return jnp.take(pool, idx, axis=0).reshape(row_count, size, pool.shape[1], pool.shape[2])


def migrate_first(pool, mig_src, row_count):
    plan = migration_plan(pool, mig_src, row_count)
    sent = outgoing_pages(pool, plan, row_count, 0, plan["first"])
    return lax.all_to_all(sent, "row", split_axis=0, concat_axis=0, tiled=True)


def migrate_rest(pool, mig_src, row_count, first_recv, dep):
    plan = migration_plan(pool, mig_src, row_count)
    land_dev, k1 = plan["land_dev"], plan["first"]
    my_row = lax.axis_index("row")
    mine = my_row * land_dev + jnp.arange(land_dev, dtype=jnp.int32)
    src_mine = plan["src_row"][mine]
    rank_mine = plan["rank"][mine]
    pool_dep, _ = lax.optimization_barrier((pool, dep))
    sizes = [0, land_dev - k1] if land_dev > k1 else [0]

    def branch(size):
        def run(pool_b, recv1):
            if size == 0:
                both = recv1
            else:
                sent = outgoing_pages(pool_b, plan, row_count, k1, size)
                recv2 = lax.all_to_all(sent, "row", split_axis=0, concat_axis=0, tiled=True)
                both = jnp.concatenate([recv1, recv2], axis=1)
            width = k1 + size
            flat = both.reshape(row_count * width, both.shape[2], both.shape[3])
            return jnp.take(flat, src_mine * width + jnp.clip(rank_mine, 0, width - 1), axis=0)
        return run

    need = jnp.maximum(plan["most"] - k1, 0)
    index = jnp.sum((jnp.array(sizes, jnp.int32) < need).astype(jnp.int32))
    return lax.switch(index, [branch(b) for b in sizes], pool_dep, first_recv)


def on_device(xn, w_qkv, w_out, pool, page_table, lengths, mig_src, deal):
    heads_here = w_out.shape[0] // HEAD_DIM
    rows_all = xn.shape[0] * lax.axis_size("col")
    row_count = lax.axis_size("row")
    req_row = rows_all // row_count
    inverse = jnp.zeros((rows_all,), jnp.int32).at[deal].set(jnp.arange(rows_all, dtype=jnp.int32))
    gathered = lax.all_gather(xn, "col", axis=0, tiled=True)
    chosen = inverse
    partial = jnp.dot(jnp.take(gathered, chosen, axis=0), w_qkv,
                      preferred_element_type=jnp.float32).astype(jnp.bfloat16)
    parts = lax.all_to_all(partial, "row", split_axis=0, concat_axis=0, tiled=True)
    projected = jnp.sum(parts.reshape(row_count, req_row, -1).astype(jnp.float32), axis=0)
    projected = projected.reshape(req_row, heads_here, 3, HEAD_DIM)
    query = rotate(projected[:, :, 0], lengths).astype(jnp.bfloat16)
    key_new = rotate(projected[:, :, 1], lengths).astype(jnp.bfloat16)
    value_new = projected[:, :, 2].astype(jnp.bfloat16)
    first = migrate_first(pool, mig_src, row_count)
    mixed, landed = attend(query, key_new, value_new, page_table, lengths, pool,
                           lambda dep: migrate_rest(pool, mig_src, row_count, first, dep))
    mixed = mixed.reshape(req_row, heads_here * HEAD_DIM)
    mixed_all = lax.all_gather(mixed, "row", axis=0, tiled=True)
    chosen = deal
    col_count = lax.axis_size("col")
    partial = jnp.dot(
        jnp.take(mixed_all, chosen, axis=0), w_out, preferred_element_type=jnp.float32
    ).astype(jnp.bfloat16)
    parts = lax.all_to_all(partial, "col", split_axis=0, concat_axis=0, tiled=True)
    attended = jnp.sum(
        parts.reshape(col_count, rows_all // col_count, -1).astype(jnp.float32), axis=0
    ).astype(jnp.bfloat16)
    return (attended, landed)


def solution(mesh):
    placed = (
        P("col", "row"),
        P("row", "col"),
        P("col", "row"),
        P("row", None, "col"),
        P("row", None),
        P("row"),
        P(),
        P(),
    )
    return jax.shard_map(
        on_device,
        mesh=mesh,
        in_specs=placed,
        out_specs=(P("col", "row"), P("row", None, "col")),
        check_vma=False,
    )
```

```python
import functools

import jax
import jax.numpy as jnp
from jax import lax
from jax.experimental import pallas as pl
from jax.experimental.pallas import tpu as pltpu
from jax.sharding import PartitionSpec as P

HEAD_DIM = 64
PAGE = 64


theta_base = 130000.0
neg_large = -1e30


def rotate(values, positions):
    half = values.shape[-1] // 2
    freqs = theta_base ** (-(jnp.arange(half, dtype=jnp.float32) * 2.0 / values.shape[-1]))
    angles = positions.astype(jnp.float32)[:, None, None] * freqs[None, None, :]
    cosine = jnp.cos(angles)
    sine = jnp.sin(angles)
    first = values[..., :half]
    second = values[..., half:]
    return jnp.concatenate(
        [first * cosine - second * sine, second * cosine + first * sine], axis=-1
    )


def page_scores(page_of, flat, scores, qrow, start, count, length, maxp):
    rows = qrow.shape[0]
    pos = lax.broadcasted_iota(jnp.int32, (rows, PAGE), 1)

    def one(k):
        j = flat[start + k] % maxp
        s = lax.dot_general(
            qrow, page_of(start + k), (((1,), (1,)), ((), ())),
            preferred_element_type=jnp.float32,
        ) * 0.125
        s = jnp.where(j * PAGE + pos < length, s, neg_large)
        scores[k] = s
        return s

    def two(k2, top):
        s0 = one(2 * k2)
        s1 = one(2 * k2 + 1)
        return jnp.maximum(top, jnp.maximum(s0, s1))

    top = lax.fori_loop(0, count // 2, two, jnp.full((rows, PAGE), neg_large, jnp.float32))
    top = lax.fori_loop(count // 2 * 2, count, lambda k, t: jnp.maximum(t, one(k)), top)
    return jnp.max(top, axis=1, keepdims=True)


def page_values(page_of, flat, scores, top, start, count, length, maxp, lanes):
    rows = top.shape[0]
    pos = lax.broadcasted_iota(jnp.int32, (rows, PAGE), 1)

    def one(k):
        j = flat[start + k] % maxp
        e = jnp.where(j * PAGE + pos < length, jnp.exp(scores[k] - top), 0.0)
        w = e.astype(jnp.bfloat16)
        return e, jnp.dot(w, page_of(start + k), preferred_element_type=jnp.float32)

    def two(k2, carry):
        total, numer = carry
        e0, n0 = one(2 * k2)
        e1, n1 = one(2 * k2 + 1)
        return total + (e0 + e1), numer + (n0 + n1)

    def single(k, carry):
        total, numer = carry
        e0, n0 = one(k)
        return total + e0, numer + n0

    init = (jnp.zeros((rows, PAGE), jnp.float32), jnp.zeros((rows, lanes), jnp.float32))
    carry = lax.fori_loop(0, count // 2, two, init)
    total, numer = lax.fori_loop(count // 2 * 2, count, single, carry)
    return jnp.sum(total, axis=1, keepdims=True), numer


def build_list(tbl, lens, pool_n, maxp, reqs, flat, starts, listed, landing):
    def req(r, carry):
        n, nl = carry
        starts[r] = n
        count = (lens[r] + PAGE - 1) // PAGE

        def page(j, n):
            e = r * maxp + j
            flat[n] = e
            keep = (tbl[e] >= pool_n) if landing else (tbl[e] < pool_n)
            return n + keep.astype(jnp.int32)

        n2 = lax.fori_loop(0, count, page, n)
        listed[nl] = r
        return n2, nl + (n2 > n).astype(jnp.int32)

    n, nl = lax.fori_loop(0, reqs, req, (0, 0))
    starts[reqs] = n
    return n, nl


def query_rows(qwide_ref, r, rows):
    lanes = qwide_ref.shape[2]
    wide = jnp.broadcast_to(qwide_ref[r], (rows, lanes))
    head = lax.broadcasted_iota(jnp.int32, (rows, lanes), 0)
    lane = lax.broadcasted_iota(jnp.int32, (rows, lanes), 1)
    return jnp.where(head == lane // 128, wide, 0.0).astype(jnp.bfloat16)


def pool_kernel(tbl, lens, qrow_ref, snew_ref, pool_ref,
                m_ref, l_ref, n_ref, scores, flat, starts, listed):
    reqs, rows, lanes = snew_ref.shape[0], snew_ref.shape[1], pool_ref.shape[2]
    maxp = scores.shape[0]
    pool_n = pool_ref.shape[0]
    build_list(tbl, lens, pool_n, maxp, reqs, flat, starts, listed, False)
    page_of = lambda f: pool_ref[jnp.clip(tbl[flat[f]], 0, pool_n - 1)]

    def request(r, carry):
        start = starts[r]
        count = starts[r + 1] - start
        length = lens[r]
        snew = snew_ref[r][:, :1]
        top = page_scores(page_of, flat, scores, query_rows(qrow_ref, r, rows), start, count,
                          length, maxp)
        top = jnp.maximum(top, snew)
        total, numer = page_values(page_of, flat, scores, top, start, count, length, maxp,
                                   lanes)
        m_ref[r] = jnp.broadcast_to(top, (rows, 128))
        l_ref[r] = jnp.broadcast_to(total, (rows, 128))
        n_ref[r] = numer
        return carry

    lax.fori_loop(0, reqs, request, 0)


def land_kernel(tbl, lens, qrow_ref, m_in, l_in, n_in, land_ref, pool_n_ref,
                m_ref, l_ref, n_ref, scores, flat, starts, listed):
    reqs, rows, lanes = m_in.shape[0], m_in.shape[1], land_ref.shape[2]
    maxp = scores.shape[0]
    pool_n = pool_n_ref.shape[0]
    land_n = land_ref.shape[0]
    _, listed_n = build_list(tbl, lens, pool_n, maxp, reqs, flat, starts, listed, True)
    m_ref[...] = m_in[...]
    l_ref[...] = l_in[...]
    n_ref[...] = n_in[...]
    page_of = lambda f: land_ref[jnp.clip(tbl[flat[f]] - pool_n, 0, land_n - 1)]

    def request(k, carry):
        r = listed[k]
        start = starts[r]
        count = starts[r + 1] - start
        length = lens[r]
        top_a = m_in[r][:, :1]
        top_b = page_scores(page_of, flat, scores, query_rows(qrow_ref, r, rows), start, count,
                            length, maxp)
        top = jnp.maximum(top_a, top_b)
        total, numer = page_values(page_of, flat, scores, top, start, count, length, maxp,
                                   lanes)
        scale = jnp.exp(top_a - top)
        m_ref[r] = jnp.broadcast_to(top, (rows, 128))
        l_ref[r] = jnp.broadcast_to(total + l_in[r][:, :1] * scale, (rows, 128))
        n_ref[r] = numer + n_in[r] * scale
        return carry

    lax.fori_loop(0, listed_n, request, 0)


def attend(qk, value_new, table, lens, pool, landed_fn):
    req_count = qk.shape[0]
    lanes = pool.shape[2]
    heads_here = lanes // (2 * HEAD_DIM)
    maxp = table.shape[1]
    pool_n = pool.shape[0]
    rows = 8
    lane = jnp.arange(lanes, dtype=jnp.int32)
    qwide = jnp.where((lane % 128 < HEAD_DIM)[None, :], qk.astype(jnp.float32), 0.0)
    qwide = qwide.reshape(req_count, 1, lanes)
    grouped = qk.astype(jnp.float32).reshape(req_count, heads_here, 2 * HEAD_DIM)
    score_new = jnp.sum(grouped[..., :HEAD_DIM] * grouped[..., HEAD_DIM:], axis=-1) * 0.125
    vf = value_new.astype(jnp.float32).reshape(req_count, heads_here, HEAD_DIM)
    snew = jnp.zeros((req_count, rows, 128), jnp.float32) + jnp.pad(
        score_new, ((0, 0), (0, rows - heads_here)))[:, :, None]
    tbl = table.reshape(-1)

    full = lambda shape: pl.BlockSpec(shape, lambda i, *_: (0,) * len(shape))
    big = (req_count, rows, lanes)
    small = (req_count, rows, 128)
    wide = (req_count, 1, lanes)
    scratch = [
        pltpu.VMEM((maxp, rows, PAGE), jnp.float32),
        pltpu.SMEM((req_count * maxp,), jnp.int32),
        pltpu.SMEM((req_count + 1,), jnp.int32),
        pltpu.SMEM((req_count,), jnp.int32),
    ]
    params = pltpu.CompilerParams(
        dimension_semantics=("arbitrary",), vmem_limit_bytes=60 * 1024 * 1024)
    state = [
        jax.ShapeDtypeStruct(small, jnp.float32),
        jax.ShapeDtypeStruct(small, jnp.float32),
        jax.ShapeDtypeStruct(big, jnp.float32),
    ]
    m_a, l_a, n_a = pl.pallas_call(
        pool_kernel,
        grid_spec=pltpu.PrefetchScalarGridSpec(
            num_scalar_prefetch=2,
            grid=(1,),
            in_specs=[full(wide), full(small), pl.BlockSpec(memory_space=pltpu.VMEM)],
            out_specs=[full(small), full(small), full(big)],
            scratch_shapes=scratch,
        ),
        out_shape=state,
        compiler_params=params,
    )(tbl, lens, qwide, snew, pool)

    landed = landed_fn(n_a)
    m_b, l_b, n_b = pl.pallas_call(
        land_kernel,
        grid_spec=pltpu.PrefetchScalarGridSpec(
            num_scalar_prefetch=2,
            grid=(1,),
            in_specs=[full(wide), full(small), full(small), full(big),
                      pl.BlockSpec(memory_space=pltpu.VMEM), pl.BlockSpec(memory_space=pl.ANY)],
            out_specs=[full(small), full(small), full(big)],
            scratch_shapes=scratch,
        ),
        out_shape=state,
        compiler_params=params,
    )(tbl, lens, qwide, m_a, l_a, n_a, landed, pool)
    top = m_b[:, :heads_here, :1]
    e_new = jnp.exp(score_new[:, :, None] - top)
    w_new = e_new.astype(jnp.bfloat16).astype(jnp.float32)
    numer = n_b[:, :heads_here].reshape(req_count, heads_here, heads_here, 2, HEAD_DIM)
    numer = jnp.stack([numer[:, h, h, 1] for h in range(heads_here)], axis=1)
    picked = ((numer + w_new * vf) / (l_b[:, :heads_here, :1] + e_new)).astype(jnp.bfloat16)
    return picked, landed


def migration_plan(pool, mig_src, row_count):
    pool_dev = pool.shape[0]
    land_all = mig_src.shape[0]
    land_dev = land_all // row_count
    src_row = jnp.clip(mig_src // pool_dev, 0, row_count - 1)
    local_page = jnp.clip(mig_src - src_row * pool_dev, 0, pool_dev - 1)
    dst_row = jnp.arange(land_all, dtype=jnp.int32) // land_dev
    onehot = (src_row[:, None] == jnp.arange(row_count, dtype=jnp.int32)[None, :]).astype(jnp.int32)
    csum = jnp.cumsum(onehot.reshape(row_count, land_dev, row_count), axis=1)
    csum = csum.reshape(land_all, row_count)
    rank = jnp.sum(csum * onehot, axis=1) - 1
    return dict(src_row=src_row, local_page=local_page, dst_row=dst_row, rank=rank,
                most=jnp.max(csum), land_dev=land_dev, first=max(1, (land_dev * 5 + 7) // 8))


def outgoing_pages(pool, plan, row_count, lo, size):
    my_row = lax.axis_index("row")
    rank = plan["rank"]
    sel = (plan["src_row"] == my_row) & (rank >= lo) & (rank < lo + size)
    where = jnp.where(sel, plan["dst_row"] * size + (rank - lo), row_count * size)
    idx = jnp.zeros((row_count * size,), jnp.int32).at[where].set(plan["local_page"], mode="drop")
    return jnp.take(pool, idx, axis=0).reshape(row_count, size, pool.shape[1], pool.shape[2])


def migrate_first(pool, mig_src, row_count):
    plan = migration_plan(pool, mig_src, row_count)
    sent = outgoing_pages(pool, plan, row_count, 0, plan["first"])
    return lax.all_to_all(sent, "row", split_axis=0, concat_axis=0, tiled=True)


def migrate_rest(pool, mig_src, row_count, first_recv, dep):
    plan = migration_plan(pool, mig_src, row_count)
    land_dev, k1 = plan["land_dev"], plan["first"]
    my_row = lax.axis_index("row")
    mine = my_row * land_dev + jnp.arange(land_dev, dtype=jnp.int32)
    src_mine = plan["src_row"][mine]
    rank_mine = plan["rank"][mine]
    pool_dep, _ = lax.optimization_barrier((pool, dep))
    sizes = [0, land_dev - k1] if land_dev > k1 else [0]

    def branch(size):
        def run(pool_b, recv1):
            if size == 0:
                both = recv1
            else:
                sent = outgoing_pages(pool_b, plan, row_count, k1, size)
                recv2 = lax.all_to_all(sent, "row", split_axis=0, concat_axis=0, tiled=True)
                both = jnp.concatenate([recv1, recv2], axis=1)
            width = k1 + size
            flat = both.reshape(row_count * width, both.shape[2], both.shape[3])
            return jnp.take(flat, src_mine * width + jnp.clip(rank_mine, 0, width - 1), axis=0)
        return run

    need = jnp.maximum(plan["most"] - k1, 0)
    index = jnp.sum((jnp.array(sizes, jnp.int32) < need).astype(jnp.int32))
    return lax.switch(index, [branch(b) for b in sizes], pool_dep, first_recv)


def on_device(xn, w_qkv, w_out, pool, page_table, lengths, mig_src, deal):
    heads_here = w_out.shape[0] // HEAD_DIM
    rows_all = xn.shape[0] * lax.axis_size("col")
    row_count = lax.axis_size("row")
    req_row = rows_all // row_count
    inverse = jnp.zeros((rows_all,), jnp.int32).at[deal].set(jnp.arange(rows_all, dtype=jnp.int32))
    gathered = lax.all_gather(xn, "col", axis=0, tiled=True)
    chosen = inverse
    heads3 = w_qkv.reshape(w_qkv.shape[0], heads_here, 3, HEAD_DIM)
    w_perm = jnp.concatenate(
        [heads3[:, :, :2].reshape(w_qkv.shape[0], -1), heads3[:, :, 2].reshape(w_qkv.shape[0], -1)],
        axis=1)
    partial = jnp.dot(jnp.take(gathered, chosen, axis=0), w_perm,
                      preferred_element_type=jnp.float32).astype(jnp.bfloat16)
    parts = lax.all_to_all(partial, "row", split_axis=0, concat_axis=0, tiled=True)
    projected = jnp.sum(parts.reshape(row_count, req_row, -1).astype(jnp.float32), axis=0)
    qk_lanes = heads_here * 2 * HEAD_DIM
    x = projected[:, :qk_lanes]
    lane = jnp.arange(qk_lanes, dtype=jnp.int32)
    within = lane % HEAD_DIM
    half = HEAD_DIM // 2
    freqs = theta_base ** (-(jnp.arange(half, dtype=jnp.float32) * 2.0 / HEAD_DIM))
    angles = lengths.astype(jnp.float32)[:, None] * freqs[within % half][None, :]
    cosine = jnp.cos(angles)
    sine = jnp.sin(angles)
    ahead = jnp.roll(x, -half, axis=1)
    behind = jnp.roll(x, half, axis=1)
    rotated = jnp.where((within < half)[None, :], x * cosine - ahead * sine,
                        x * cosine + behind * sine)
    qk = rotated.astype(jnp.bfloat16)
    value_new = projected[:, qk_lanes:].astype(jnp.bfloat16)
    first = migrate_first(pool, mig_src, row_count)
    mixed, landed = attend(qk, value_new, page_table, lengths, pool,
                           lambda dep: migrate_rest(pool, mig_src, row_count, first, dep))
    mixed = mixed.reshape(req_row, heads_here * HEAD_DIM)
    mixed_all = lax.all_gather(mixed, "row", axis=0, tiled=True)
    chosen = deal
    col_count = lax.axis_size("col")
    partial = jnp.dot(
        jnp.take(mixed_all, chosen, axis=0), w_out, preferred_element_type=jnp.float32
    ).astype(jnp.bfloat16)
    parts = lax.all_to_all(partial, "col", split_axis=0, concat_axis=0, tiled=True)
    attended = jnp.sum(
        parts.reshape(col_count, rows_all // col_count, -1).astype(jnp.float32), axis=0
    ).astype(jnp.bfloat16)
    return (attended, landed)


def solution(mesh):
    placed = (
        P("col", "row"),
        P("row", "col"),
        P("col", "row"),
        P("row", None, "col"),
        P("row", None),
        P("row"),
        P(),
        P(),
    )
    return jax.shard_map(
        on_device,
        mesh=mesh,
        in_specs=placed,
        out_specs=(P("col", "row"), P("row", None, "col")),
        check_vma=False,
    )
```

```python
import functools

import jax
import jax.numpy as jnp
from jax import lax
from jax.experimental import pallas as pl
from jax.experimental.pallas import tpu as pltpu
from jax.sharding import PartitionSpec as P

HEAD_DIM = 64
PAGE = 64


theta_base = 130000.0
neg_large = -1e30


def rotate(values, positions):
    half = values.shape[-1] // 2
    freqs = theta_base ** (-(jnp.arange(half, dtype=jnp.float32) * 2.0 / values.shape[-1]))
    angles = positions.astype(jnp.float32)[:, None, None] * freqs[None, None, :]
    cosine = jnp.cos(angles)
    sine = jnp.sin(angles)
    first = values[..., :half]
    second = values[..., half:]
    return jnp.concatenate(
        [first * cosine - second * sine, second * cosine + first * sine], axis=-1
    )


def page_scores(page_of, flat, scores, qrow, start, count, length, maxp):
    rows = qrow.shape[0]
    pos = lax.broadcasted_iota(jnp.int32, (rows, PAGE), 1)

    def one(k):
        j = flat[start + k] % maxp
        s = lax.dot_general(
            qrow, page_of(start + k), (((1,), (1,)), ((), ())),
            preferred_element_type=jnp.float32,
        ) * 0.125
        s = jnp.where(j * PAGE + pos < length, s, neg_large)
        scores[k] = s
        return s

    def two(k2, top):
        s0 = one(2 * k2)
        s1 = one(2 * k2 + 1)
        return jnp.maximum(top, jnp.maximum(s0, s1))

    top = lax.fori_loop(0, count // 2, two, jnp.full((rows, PAGE), neg_large, jnp.float32))
    top = lax.fori_loop(count // 2 * 2, count, lambda k, t: jnp.maximum(t, one(k)), top)
    return jnp.max(top, axis=1, keepdims=True)


def page_values(page_of, flat, scores, top, start, count, length, maxp, lanes):
    rows = top.shape[0]
    pos = lax.broadcasted_iota(jnp.int32, (rows, PAGE), 1)

    def one(k):
        j = flat[start + k] % maxp
        e = jnp.where(j * PAGE + pos < length, jnp.exp(scores[k] - top), 0.0)
        w = e.astype(jnp.bfloat16)
        return e, jnp.dot(w, page_of(start + k), preferred_element_type=jnp.float32)

    def two(k2, carry):
        total, numer = carry
        e0, n0 = one(2 * k2)
        e1, n1 = one(2 * k2 + 1)
        return total + (e0 + e1), numer + (n0 + n1)

    def single(k, carry):
        total, numer = carry
        e0, n0 = one(k)
        return total + e0, numer + n0

    init = (jnp.zeros((rows, PAGE), jnp.float32), jnp.zeros((rows, lanes), jnp.float32))
    carry = lax.fori_loop(0, count // 2, two, init)
    total, numer = lax.fori_loop(count // 2 * 2, count, single, carry)
    return jnp.sum(total, axis=1, keepdims=True), numer


def build_list(tbl, lens, pool_n, maxp, reqs, flat, starts, listed, landing):
    def req(r, carry):
        n, nl = carry
        starts[r] = n
        count = (lens[r] + PAGE - 1) // PAGE

        def page(j, n):
            e = r * maxp + j
            flat[n] = e
            keep = (tbl[e] >= pool_n) if landing else (tbl[e] < pool_n)
            return n + keep.astype(jnp.int32)

        n2 = lax.fori_loop(0, count, page, n)
        listed[nl] = r
        return n2, nl + (n2 > n).astype(jnp.int32)

    n, nl = lax.fori_loop(0, reqs, req, (0, 0))
    starts[reqs] = n
    return n, nl


def query_rows(qwide_ref, r, rows):
    lanes = qwide_ref.shape[2]
    wide = jnp.broadcast_to(qwide_ref[r], (rows, lanes))
    head = lax.broadcasted_iota(jnp.int32, (rows, lanes), 0)
    lane = lax.broadcasted_iota(jnp.int32, (rows, lanes), 1)
    return jnp.where(head == lane // 128, wide, 0.0).astype(jnp.bfloat16)


def pool_kernel(tbl, lens, x_ref, cos_ref, sin_ref, pool_ref,
                m_ref, l_ref, n_ref, qrow_ref, snew_ref, scores, flat, starts, listed):
    reqs, rows, lanes = m_ref.shape[0], m_ref.shape[1], pool_ref.shape[2]
    half = HEAD_DIM // 2
    lane = lax.broadcasted_iota(jnp.int32, (1, lanes), 1)
    first_half = lane % HEAD_DIM < half
    head = lax.broadcasted_iota(jnp.int32, (rows, lanes), 0)
    lane8 = lax.broadcasted_iota(jnp.int32, (rows, lanes), 1)
    own_q = (head == lane8 // 128) & (lane8 % 128 < HEAD_DIM)

    def rotate_row(r):
        x = x_ref[r]
        ahead = pltpu.roll(x, lanes - half, 1)
        behind = pltpu.roll(x, half, 1)
        c = cos_ref[r]
        s = sin_ref[r]
        rot = jnp.where(first_half, x * c - ahead * s, x * c + behind * s)
        qk = rot.astype(jnp.bfloat16).astype(jnp.float32)
        keys = pltpu.roll(qk, lanes - HEAD_DIM, 1)
        prod = jnp.where(own_q, jnp.broadcast_to(qk * keys, (rows, lanes)), 0.0)
        snew = jnp.sum(prod, axis=1, keepdims=True) * 0.125
        qrow_ref[r] = jnp.where(lane % 128 < HEAD_DIM, qk, 0.0)
        snew_ref[r] = jnp.broadcast_to(snew, (rows, 128))
        return snew

    def prep(r, carry):
        rotate_row(r)
        return carry

    lax.fori_loop(0, reqs, prep, 0)
    maxp = scores.shape[0]
    pool_n = pool_ref.shape[0]
    build_list(tbl, lens, pool_n, maxp, reqs, flat, starts, listed, False)
    page_of = lambda f: pool_ref[jnp.clip(tbl[flat[f]], 0, pool_n - 1)]

    def request(r, carry):
        start = starts[r]
        count = starts[r + 1] - start
        length = lens[r]
        snew = snew_ref[r][:, :1]
        top = page_scores(page_of, flat, scores, query_rows(qrow_ref, r, rows), start, count,
                          length, maxp)
        top = jnp.maximum(top, snew)
        total, numer = page_values(page_of, flat, scores, top, start, count, length, maxp,
                                   lanes)
        m_ref[r] = jnp.broadcast_to(top, (rows, 128))
        l_ref[r] = jnp.broadcast_to(total, (rows, 128))
        n_ref[r] = numer
        return carry

    lax.fori_loop(0, reqs, request, 0)


def land_kernel(tbl, lens, qrow_ref, m_in, l_in, n_in, land_ref, pool_n_ref,
                m_ref, l_ref, n_ref, scores, flat, starts, listed):
    reqs, rows, lanes = m_in.shape[0], m_in.shape[1], land_ref.shape[2]
    maxp = scores.shape[0]
    pool_n = pool_n_ref.shape[0]
    land_n = land_ref.shape[0]
    _, listed_n = build_list(tbl, lens, pool_n, maxp, reqs, flat, starts, listed, True)
    m_ref[...] = m_in[...]
    l_ref[...] = l_in[...]
    n_ref[...] = n_in[...]
    page_of = lambda f: land_ref[jnp.clip(tbl[flat[f]] - pool_n, 0, land_n - 1)]

    def request(k, carry):
        r = listed[k]
        start = starts[r]
        count = starts[r + 1] - start
        length = lens[r]
        top_a = m_in[r][:, :1]
        top_b = page_scores(page_of, flat, scores, query_rows(qrow_ref, r, rows), start, count,
                            length, maxp)
        top = jnp.maximum(top_a, top_b)
        total, numer = page_values(page_of, flat, scores, top, start, count, length, maxp,
                                   lanes)
        scale = jnp.exp(top_a - top)
        m_ref[r] = jnp.broadcast_to(top, (rows, 128))
        l_ref[r] = jnp.broadcast_to(total + l_in[r][:, :1] * scale, (rows, 128))
        n_ref[r] = numer + n_in[r] * scale
        return carry

    lax.fori_loop(0, listed_n, request, 0)


def attend(xqk, value_new, table, lens, pool, landed_fn):
    req_count = xqk.shape[0]
    lanes = pool.shape[2]
    heads_here = lanes // (2 * HEAD_DIM)
    maxp = table.shape[1]
    pool_n = pool.shape[0]
    rows = 8
    lane = jnp.arange(lanes, dtype=jnp.int32)
    half = HEAD_DIM // 2
    freqs = theta_base ** (-(jnp.arange(half, dtype=jnp.float32) * 2.0 / HEAD_DIM))
    angles = lens.astype(jnp.float32)[:, None] * freqs[lane % HEAD_DIM % half][None, :]
    cosine = jnp.cos(angles).reshape(req_count, 1, lanes)
    sine = jnp.sin(angles).reshape(req_count, 1, lanes)
    xqk = xqk.reshape(req_count, 1, lanes)
    vf = value_new.astype(jnp.float32).reshape(req_count, heads_here, HEAD_DIM)
    tbl = table.reshape(-1)

    full = lambda shape: pl.BlockSpec(shape, lambda i, *_: (0,) * len(shape))
    big = (req_count, rows, lanes)
    small = (req_count, rows, 128)
    wide = (req_count, 1, lanes)
    scratch = [
        pltpu.VMEM((maxp, rows, PAGE), jnp.float32),
        pltpu.SMEM((req_count * maxp,), jnp.int32),
        pltpu.SMEM((req_count + 1,), jnp.int32),
        pltpu.SMEM((req_count,), jnp.int32),
    ]
    params = pltpu.CompilerParams(
        dimension_semantics=("arbitrary",), vmem_limit_bytes=60 * 1024 * 1024)
    state = [
        jax.ShapeDtypeStruct(small, jnp.float32),
        jax.ShapeDtypeStruct(small, jnp.float32),
        jax.ShapeDtypeStruct(big, jnp.float32),
    ]
    m_a, l_a, n_a, qwide, snew = pl.pallas_call(
        pool_kernel,
        grid_spec=pltpu.PrefetchScalarGridSpec(
            num_scalar_prefetch=2,
            grid=(1,),
            in_specs=[full(wide), full(wide), full(wide), pl.BlockSpec(memory_space=pltpu.VMEM)],
            out_specs=[full(small), full(small), full(big), full(wide), full(small)],
            scratch_shapes=scratch,
        ),
        out_shape=state + [jax.ShapeDtypeStruct(wide, jnp.float32),
                           jax.ShapeDtypeStruct(small, jnp.float32)],
        compiler_params=params,
    )(tbl, lens, xqk, cosine, sine, pool)
    score_new = snew[:, :heads_here, 0]

    landed = landed_fn(n_a)
    m_b, l_b, n_b = pl.pallas_call(
        land_kernel,
        grid_spec=pltpu.PrefetchScalarGridSpec(
            num_scalar_prefetch=2,
            grid=(1,),
            in_specs=[full(wide), full(small), full(small), full(big),
                      pl.BlockSpec(memory_space=pltpu.VMEM), pl.BlockSpec(memory_space=pl.ANY)],
            out_specs=[full(small), full(small), full(big)],
            scratch_shapes=scratch,
        ),
        out_shape=state,
        compiler_params=params,
    )(tbl, lens, qwide, m_a, l_a, n_a, landed, pool)
    top = m_b[:, :heads_here, :1]
    e_new = jnp.exp(score_new[:, :, None] - top)
    w_new = e_new.astype(jnp.bfloat16).astype(jnp.float32)
    numer = n_b[:, :heads_here].reshape(req_count, heads_here, heads_here, 2, HEAD_DIM)
    numer = jnp.stack([numer[:, h, h, 1] for h in range(heads_here)], axis=1)
    picked = ((numer + w_new * vf) / (l_b[:, :heads_here, :1] + e_new)).astype(jnp.bfloat16)
    return picked, landed


def migration_plan(pool, mig_src, row_count):
    pool_dev = pool.shape[0]
    land_all = mig_src.shape[0]
    land_dev = land_all // row_count
    src_row = jnp.clip(mig_src // pool_dev, 0, row_count - 1)
    local_page = jnp.clip(mig_src - src_row * pool_dev, 0, pool_dev - 1)
    dst_row = jnp.arange(land_all, dtype=jnp.int32) // land_dev
    onehot = (src_row[:, None] == jnp.arange(row_count, dtype=jnp.int32)[None, :]).astype(jnp.int32)
    csum = jnp.cumsum(onehot.reshape(row_count, land_dev, row_count), axis=1)
    csum = csum.reshape(land_all, row_count)
    rank = jnp.sum(csum * onehot, axis=1) - 1
    return dict(src_row=src_row, local_page=local_page, dst_row=dst_row, rank=rank,
                most=jnp.max(csum), land_dev=land_dev, first=max(1, (land_dev * 5 + 7) // 8))


def outgoing_pages(pool, plan, row_count, lo, size):
    my_row = lax.axis_index("row")
    rank = plan["rank"]
    sel = (plan["src_row"] == my_row) & (rank >= lo) & (rank < lo + size)
    where = jnp.where(sel, plan["dst_row"] * size + (rank - lo), row_count * size)
    idx = jnp.zeros((row_count * size,), jnp.int32).at[where].set(plan["local_page"], mode="drop")
    return jnp.take(pool, idx, axis=0).reshape(row_count, size, pool.shape[1], pool.shape[2])


def migrate_first(pool, mig_src, row_count):
    plan = migration_plan(pool, mig_src, row_count)
    sent = outgoing_pages(pool, plan, row_count, 0, plan["first"])
    return lax.all_to_all(sent, "row", split_axis=0, concat_axis=0, tiled=True)


def migrate_rest(pool, mig_src, row_count, first_recv, dep):
    plan = migration_plan(pool, mig_src, row_count)
    land_dev, k1 = plan["land_dev"], plan["first"]
    my_row = lax.axis_index("row")
    mine = my_row * land_dev + jnp.arange(land_dev, dtype=jnp.int32)
    src_mine = plan["src_row"][mine]
    rank_mine = plan["rank"][mine]
    pool_dep, _ = lax.optimization_barrier((pool, dep))
    sizes = [0, land_dev - k1] if land_dev > k1 else [0]

    def branch(size):
        def run(pool_b, recv1):
            if size == 0:
                both = recv1
            else:
                sent = outgoing_pages(pool_b, plan, row_count, k1, size)
                recv2 = lax.all_to_all(sent, "row", split_axis=0, concat_axis=0, tiled=True)
                both = jnp.concatenate([recv1, recv2], axis=1)
            width = k1 + size
            flat = both.reshape(row_count * width, both.shape[2], both.shape[3])
            return jnp.take(flat, src_mine * width + jnp.clip(rank_mine, 0, width - 1), axis=0)
        return run

    need = jnp.maximum(plan["most"] - k1, 0)
    index = jnp.sum((jnp.array(sizes, jnp.int32) < need).astype(jnp.int32))
    return lax.switch(index, [branch(b) for b in sizes], pool_dep, first_recv)


def on_device(xn, w_qkv, w_out, pool, page_table, lengths, mig_src, deal):
    heads_here = w_out.shape[0] // HEAD_DIM
    rows_all = xn.shape[0] * lax.axis_size("col")
    row_count = lax.axis_size("row")
    req_row = rows_all // row_count
    inverse = jnp.zeros((rows_all,), jnp.int32).at[deal].set(jnp.arange(rows_all, dtype=jnp.int32))
    gathered = lax.all_gather(xn, "col", axis=0, tiled=True)
    chosen = inverse
    heads3 = w_qkv.reshape(w_qkv.shape[0], heads_here, 3, HEAD_DIM)
    w_perm = jnp.concatenate(
        [heads3[:, :, :2].reshape(w_qkv.shape[0], -1), heads3[:, :, 2].reshape(w_qkv.shape[0], -1)],
        axis=1)
    partial = jnp.dot(jnp.take(gathered, chosen, axis=0), w_perm,
                      preferred_element_type=jnp.float32).astype(jnp.bfloat16)
    parts = lax.all_to_all(partial, "row", split_axis=0, concat_axis=0, tiled=True)
    projected = jnp.sum(parts.reshape(row_count, req_row, -1).astype(jnp.float32), axis=0)
    qk_lanes = heads_here * 2 * HEAD_DIM
    value_new = projected[:, qk_lanes:].astype(jnp.bfloat16)
    first = migrate_first(pool, mig_src, row_count)
    mixed, landed = attend(projected[:, :qk_lanes], value_new, page_table, lengths, pool,
                           lambda dep: migrate_rest(pool, mig_src, row_count, first, dep))
    mixed = mixed.reshape(req_row, heads_here * HEAD_DIM)
    mixed_all = lax.all_gather(mixed, "row", axis=0, tiled=True)
    chosen = deal
    col_count = lax.axis_size("col")
    partial = jnp.dot(
        jnp.take(mixed_all, chosen, axis=0), w_out, preferred_element_type=jnp.float32
    ).astype(jnp.bfloat16)
    parts = lax.all_to_all(partial, "col", split_axis=0, concat_axis=0, tiled=True)
    attended = jnp.sum(
        parts.reshape(col_count, rows_all // col_count, -1).astype(jnp.float32), axis=0
    ).astype(jnp.bfloat16)
    return (attended, landed)


def solution(mesh):
    placed = (
        P("col", "row"),
        P("row", "col"),
        P("col", "row"),
        P("row", None, "col"),
        P("row", None),
        P("row"),
        P(),
        P(),
    )
    return jax.shard_map(
        on_device,
        mesh=mesh,
        in_specs=placed,
        out_specs=(P("col", "row"), P("row", None, "col")),
        check_vma=False,
    )
```

```python
import functools

import jax
import jax.numpy as jnp
from jax import lax
from jax.experimental import pallas as pl
from jax.experimental.pallas import tpu as pltpu
from jax.sharding import PartitionSpec as P

HEAD_DIM = 64
PAGE = 64


theta_base = 130000.0
neg_large = -1e30


def rotate(values, positions):
    half = values.shape[-1] // 2
    freqs = theta_base ** (-(jnp.arange(half, dtype=jnp.float32) * 2.0 / values.shape[-1]))
    angles = positions.astype(jnp.float32)[:, None, None] * freqs[None, None, :]
    cosine = jnp.cos(angles)
    sine = jnp.sin(angles)
    first = values[..., :half]
    second = values[..., half:]
    return jnp.concatenate(
        [first * cosine - second * sine, second * cosine + first * sine], axis=-1
    )


def page_scores(page_of, flat, scores, qrow, start, count, length, maxp):
    rows = qrow.shape[0]
    pos = lax.broadcasted_iota(jnp.int32, (rows, PAGE), 1)

    def one(k):
        j = flat[start + k] % maxp
        s = lax.dot_general(
            qrow, page_of(start + k), (((1,), (1,)), ((), ())),
            preferred_element_type=jnp.float32,
        ) * 0.125
        s = jnp.where(j * PAGE + pos < length, s, neg_large)
        scores[k] = s
        return s

    def two(k2, top):
        s0 = one(2 * k2)
        s1 = one(2 * k2 + 1)
        return jnp.maximum(top, jnp.maximum(s0, s1))

    top = lax.fori_loop(0, count // 2, two, jnp.full((rows, PAGE), neg_large, jnp.float32))
    top = lax.fori_loop(count // 2 * 2, count, lambda k, t: jnp.maximum(t, one(k)), top)
    return jnp.max(top, axis=1, keepdims=True)


def page_values(page_of, flat, scores, top, start, count, length, maxp, lanes):
    rows = top.shape[0]
    pos = lax.broadcasted_iota(jnp.int32, (rows, PAGE), 1)

    def one(k):
        j = flat[start + k] % maxp
        e = jnp.where(j * PAGE + pos < length, jnp.exp(scores[k] - top), 0.0)
        w = e.astype(jnp.bfloat16)
        return e, jnp.dot(w, page_of(start + k), preferred_element_type=jnp.float32)

    def two(k2, carry):
        total, numer = carry
        e0, n0 = one(2 * k2)
        e1, n1 = one(2 * k2 + 1)
        return total + (e0 + e1), numer + (n0 + n1)

    def single(k, carry):
        total, numer = carry
        e0, n0 = one(k)
        return total + e0, numer + n0

    init = (jnp.zeros((rows, PAGE), jnp.float32), jnp.zeros((rows, lanes), jnp.float32))
    carry = lax.fori_loop(0, count // 2, two, init)
    total, numer = lax.fori_loop(count // 2 * 2, count, single, carry)
    return jnp.sum(total, axis=1, keepdims=True), numer


def build_list(tbl, lens, pool_n, maxp, reqs, flat, starts, listed, landing):
    def req(r, carry):
        n, nl = carry
        starts[r] = n
        count = (lens[r] + PAGE - 1) // PAGE

        def page(j, n):
            e = r * maxp + j
            flat[n] = e
            keep = (tbl[e] >= pool_n) if landing else (tbl[e] < pool_n)
            return n + keep.astype(jnp.int32)

        n2 = lax.fori_loop(0, count, page, n)
        listed[nl] = r
        return n2, nl + (n2 > n).astype(jnp.int32)

    n, nl = lax.fori_loop(0, reqs, req, (0, 0))
    starts[reqs] = n
    return n, nl


def query_rows(qwide_ref, r, rows):
    lanes = qwide_ref.shape[2]
    wide = jnp.broadcast_to(qwide_ref[r], (rows, lanes))
    head = lax.broadcasted_iota(jnp.int32, (rows, lanes), 0)
    lane = lax.broadcasted_iota(jnp.int32, (rows, lanes), 1)
    return jnp.where(head == lane // 128, wide, 0.0).astype(jnp.bfloat16)


def pool_kernel(tbl, lens, x_ref, cos_ref, sin_ref, pool_ref,
                m_ref, l_ref, n_ref, qrow_ref, snew_ref, scores, flat, starts, listed):
    reqs, rows, lanes = m_ref.shape[0], m_ref.shape[1], pool_ref.shape[2]
    half = HEAD_DIM // 2
    lane = lax.broadcasted_iota(jnp.int32, (1, lanes), 1)
    first_half = lane % HEAD_DIM < half
    head = lax.broadcasted_iota(jnp.int32, (rows, lanes), 0)
    lane8 = lax.broadcasted_iota(jnp.int32, (rows, lanes), 1)
    own_q = (head == lane8 // 128) & (lane8 % 128 < HEAD_DIM)

    def rotate_row(r):
        x = x_ref[r]
        ahead = pltpu.roll(x, lanes - half, 1)
        behind = pltpu.roll(x, half, 1)
        c = cos_ref[r]
        s = sin_ref[r]
        rot = jnp.where(first_half, x * c - ahead * s, x * c + behind * s)
        qk = rot.astype(jnp.bfloat16).astype(jnp.float32)
        keys = pltpu.roll(qk, lanes - HEAD_DIM, 1)
        prod = jnp.where(own_q, jnp.broadcast_to(qk * keys, (rows, lanes)), 0.0)
        snew = jnp.sum(prod, axis=1, keepdims=True) * 0.125
        qrow_ref[r] = jnp.where(lane % 128 < HEAD_DIM, qk, 0.0)
        snew_ref[r] = jnp.broadcast_to(snew, (rows, 128))
        return snew

    def prep(r, carry):
        rotate_row(r)
        return carry

    lax.fori_loop(0, reqs, prep, 0)
    maxp = scores.shape[0]
    pool_n = pool_ref.shape[0]
    build_list(tbl, lens, pool_n, maxp, reqs, flat, starts, listed, False)
    page_of = lambda f: pool_ref[jnp.clip(tbl[flat[f]], 0, pool_n - 1)]

    def request(r, carry):
        start = starts[r]
        count = starts[r + 1] - start
        length = lens[r]
        snew = snew_ref[r][:, :1]
        top = page_scores(page_of, flat, scores, query_rows(qrow_ref, r, rows), start, count,
                          length, maxp)
        top = jnp.maximum(top, snew)
        total, numer = page_values(page_of, flat, scores, top, start, count, length, maxp,
                                   lanes)
        m_ref[r] = jnp.broadcast_to(top, (rows, 128))
        l_ref[r] = jnp.broadcast_to(total, (rows, 128))
        n_ref[r] = numer
        return carry

    lax.fori_loop(0, reqs, request, 0)


def land_kernel(tbl, lens, qrow_ref, m_in, l_in, n_in, land_ref, pool_n_ref,
                m_ref, l_ref, n_ref, scores, flat, starts, listed):
    reqs, rows, lanes = m_in.shape[0], m_in.shape[1], land_ref.shape[2]
    maxp = scores.shape[0]
    pool_n = pool_n_ref.shape[0]
    land_n = land_ref.shape[0]
    _, listed_n = build_list(tbl, lens, pool_n, maxp, reqs, flat, starts, listed, True)
    m_ref[...] = m_in[...]
    l_ref[...] = l_in[...]
    n_ref[...] = n_in[...]
    page_of = lambda f: land_ref[jnp.clip(tbl[flat[f]] - pool_n, 0, land_n - 1)]

    def request(k, carry):
        r = listed[k]
        start = starts[r]
        count = starts[r + 1] - start
        length = lens[r]
        top_a = m_in[r][:, :1]
        top_b = page_scores(page_of, flat, scores, query_rows(qrow_ref, r, rows), start, count,
                            length, maxp)
        top = jnp.maximum(top_a, top_b)
        total, numer = page_values(page_of, flat, scores, top, start, count, length, maxp,
                                   lanes)
        scale = jnp.exp(top_a - top)
        m_ref[r] = jnp.broadcast_to(top, (rows, 128))
        l_ref[r] = jnp.broadcast_to(total + l_in[r][:, :1] * scale, (rows, 128))
        n_ref[r] = numer + n_in[r] * scale
        return carry

    lax.fori_loop(0, listed_n, request, 0)


def attend(xqk, value_new, table, lens, pool, landed_fn):
    req_count = xqk.shape[0]
    lanes = pool.shape[2]
    heads_here = lanes // (2 * HEAD_DIM)
    maxp = table.shape[1]
    pool_n = pool.shape[0]
    rows = 8
    lane = jnp.arange(lanes, dtype=jnp.int32)
    half = HEAD_DIM // 2
    freqs = theta_base ** (-(jnp.arange(half, dtype=jnp.float32) * 2.0 / HEAD_DIM))
    angles = lens.astype(jnp.float32)[:, None] * freqs[None, :]
    cosine = jnp.tile(jnp.cos(angles), (1, lanes // half)).reshape(req_count, 1, lanes)
    sine = jnp.tile(jnp.sin(angles), (1, lanes // half)).reshape(req_count, 1, lanes)
    xqk = xqk.reshape(req_count, 1, lanes)
    vf = value_new.astype(jnp.float32).reshape(req_count, heads_here, HEAD_DIM)
    tbl = table.reshape(-1)

    full = lambda shape: pl.BlockSpec(shape, lambda i, *_: (0,) * len(shape))
    big = (req_count, rows, lanes)
    small = (req_count, rows, 128)
    wide = (req_count, 1, lanes)
    scratch = [
        pltpu.VMEM((maxp, rows, PAGE), jnp.float32),
        pltpu.SMEM((req_count * maxp,), jnp.int32),
        pltpu.SMEM((req_count + 1,), jnp.int32),
        pltpu.SMEM((req_count,), jnp.int32),
    ]
    params = pltpu.CompilerParams(
        dimension_semantics=("arbitrary",), vmem_limit_bytes=60 * 1024 * 1024)
    state = [
        jax.ShapeDtypeStruct(small, jnp.float32),
        jax.ShapeDtypeStruct(small, jnp.float32),
        jax.ShapeDtypeStruct(big, jnp.float32),
    ]
    m_a, l_a, n_a, qwide, snew = pl.pallas_call(
        pool_kernel,
        grid_spec=pltpu.PrefetchScalarGridSpec(
            num_scalar_prefetch=2,
            grid=(1,),
            in_specs=[full(wide), full(wide), full(wide), pl.BlockSpec(memory_space=pltpu.VMEM)],
            out_specs=[full(small), full(small), full(big), full(wide), full(small)],
            scratch_shapes=scratch,
        ),
        out_shape=state + [jax.ShapeDtypeStruct(wide, jnp.float32),
                           jax.ShapeDtypeStruct(small, jnp.float32)],
        compiler_params=params,
    )(tbl, lens, xqk, cosine, sine, pool)
    score_new = snew[:, :heads_here, 0]

    landed = landed_fn(n_a)
    m_b, l_b, n_b = pl.pallas_call(
        land_kernel,
        grid_spec=pltpu.PrefetchScalarGridSpec(
            num_scalar_prefetch=2,
            grid=(1,),
            in_specs=[full(wide), full(small), full(small), full(big),
                      pl.BlockSpec(memory_space=pltpu.VMEM), pl.BlockSpec(memory_space=pl.ANY)],
            out_specs=[full(small), full(small), full(big)],
            scratch_shapes=scratch,
        ),
        out_shape=state,
        compiler_params=params,
    )(tbl, lens, qwide, m_a, l_a, n_a, landed, pool)
    top = m_b[:, :heads_here, :1]
    e_new = jnp.exp(score_new[:, :, None] - top)
    w_new = e_new.astype(jnp.bfloat16).astype(jnp.float32)
    numer = n_b[:, :heads_here].reshape(req_count, heads_here, heads_here, 2, HEAD_DIM)
    numer = jnp.stack([numer[:, h, h, 1] for h in range(heads_here)], axis=1)
    picked = ((numer + w_new * vf) / (l_b[:, :heads_here, :1] + e_new)).astype(jnp.bfloat16)
    return picked, landed


def migration_plan(pool, mig_src, row_count):
    pool_dev = pool.shape[0]
    land_all = mig_src.shape[0]
    land_dev = land_all // row_count
    src_row = jnp.clip(mig_src // pool_dev, 0, row_count - 1)
    local_page = jnp.clip(mig_src - src_row * pool_dev, 0, pool_dev - 1)
    dst_row = jnp.arange(land_all, dtype=jnp.int32) // land_dev
    onehot = (src_row[:, None] == jnp.arange(row_count, dtype=jnp.int32)[None, :]).astype(jnp.int32)
    csum = jnp.cumsum(onehot.reshape(row_count, land_dev, row_count), axis=1)
    csum = csum.reshape(land_all, row_count)
    rank = jnp.sum(csum * onehot, axis=1) - 1
    return dict(src_row=src_row, local_page=local_page, dst_row=dst_row, rank=rank,
                most=jnp.max(csum), land_dev=land_dev, first=max(1, (land_dev * 5 + 7) // 8))


def outgoing_pages(pool, plan, row_count, lo, size):
    my_row = lax.axis_index("row")
    rank = plan["rank"]
    sel = (plan["src_row"] == my_row) & (rank >= lo) & (rank < lo + size)
    where = jnp.where(sel, plan["dst_row"] * size + (rank - lo), row_count * size)
    idx = jnp.zeros((row_count * size,), jnp.int32).at[where].set(plan["local_page"], mode="drop")
    return jnp.take(pool, idx, axis=0).reshape(row_count, size, pool.shape[1], pool.shape[2])


def migrate_first(pool, mig_src, row_count):
    plan = migration_plan(pool, mig_src, row_count)
    sent = outgoing_pages(pool, plan, row_count, 0, plan["first"])
    return lax.all_to_all(sent, "row", split_axis=0, concat_axis=0, tiled=True)


def migrate_rest(pool, mig_src, row_count, first_recv, dep):
    plan = migration_plan(pool, mig_src, row_count)
    land_dev, k1 = plan["land_dev"], plan["first"]
    my_row = lax.axis_index("row")
    mine = my_row * land_dev + jnp.arange(land_dev, dtype=jnp.int32)
    src_mine = plan["src_row"][mine]
    rank_mine = plan["rank"][mine]
    pool_dep, _ = lax.optimization_barrier((pool, dep))
    sizes = [0, land_dev - k1] if land_dev > k1 else [0]

    def branch(size):
        def run(pool_b, recv1):
            if size == 0:
                both = recv1
            else:
                sent = outgoing_pages(pool_b, plan, row_count, k1, size)
                recv2 = lax.all_to_all(sent, "row", split_axis=0, concat_axis=0, tiled=True)
                both = jnp.concatenate([recv1, recv2], axis=1)
            width = k1 + size
            flat = both.reshape(row_count * width, both.shape[2], both.shape[3])
            return jnp.take(flat, src_mine * width + jnp.clip(rank_mine, 0, width - 1), axis=0)
        return run

    need = jnp.maximum(plan["most"] - k1, 0)
    index = jnp.sum((jnp.array(sizes, jnp.int32) < need).astype(jnp.int32))
    return lax.switch(index, [branch(b) for b in sizes], pool_dep, first_recv)


def on_device(xn, w_qkv, w_out, pool, page_table, lengths, mig_src, deal):
    heads_here = w_out.shape[0] // HEAD_DIM
    rows_all = xn.shape[0] * lax.axis_size("col")
    row_count = lax.axis_size("row")
    req_row = rows_all // row_count
    inverse = jnp.zeros((rows_all,), jnp.int32).at[deal].set(jnp.arange(rows_all, dtype=jnp.int32))
    gathered = lax.all_gather(xn, "col", axis=0, tiled=True)
    chosen = inverse
    heads3 = w_qkv.reshape(w_qkv.shape[0], heads_here, 3, HEAD_DIM)
    w_perm = jnp.concatenate(
        [heads3[:, :, :2].reshape(w_qkv.shape[0], -1), heads3[:, :, 2].reshape(w_qkv.shape[0], -1)],
        axis=1)
    partial = jnp.dot(jnp.take(gathered, chosen, axis=0), w_perm,
                      preferred_element_type=jnp.float32).astype(jnp.bfloat16)
    parts = lax.all_to_all(partial, "row", split_axis=0, concat_axis=0, tiled=True)
    projected = jnp.sum(parts.reshape(row_count, req_row, -1).astype(jnp.float32), axis=0)
    qk_lanes = heads_here * 2 * HEAD_DIM
    value_new = projected[:, qk_lanes:].astype(jnp.bfloat16)
    first = migrate_first(pool, mig_src, row_count)
    mixed, landed = attend(projected[:, :qk_lanes], value_new, page_table, lengths, pool,
                           lambda dep: migrate_rest(pool, mig_src, row_count, first, dep))
    mixed = mixed.reshape(req_row, heads_here * HEAD_DIM)
    mixed_all = lax.all_gather(mixed, "row", axis=0, tiled=True)
    chosen = deal
    col_count = lax.axis_size("col")
    partial = jnp.dot(
        jnp.take(mixed_all, chosen, axis=0), w_out, preferred_element_type=jnp.float32
    ).astype(jnp.bfloat16)
    parts = lax.all_to_all(partial, "col", split_axis=0, concat_axis=0, tiled=True)
    attended = jnp.sum(
        parts.reshape(col_count, rows_all // col_count, -1).astype(jnp.float32), axis=0
    ).astype(jnp.bfloat16)
    return (attended, landed)


def solution(mesh):
    placed = (
        P("col", "row"),
        P("row", "col"),
        P("col", "row"),
        P("row", None, "col"),
        P("row", None),
        P("row"),
        P(),
        P(),
    )
    return jax.shard_map(
        on_device,
        mesh=mesh,
        in_specs=placed,
        out_specs=(P("col", "row"), P("row", None, "col")),
        check_vma=False,
    )
```

```python
import functools

import jax
import jax.numpy as jnp
from jax import lax
from jax.experimental import pallas as pl
from jax.experimental.pallas import tpu as pltpu
from jax.sharding import PartitionSpec as P

HEAD_DIM = 64
PAGE = 64


theta_base = 130000.0
neg_large = -1e30


def rotate(values, positions):
    half = values.shape[-1] // 2
    freqs = theta_base ** (-(jnp.arange(half, dtype=jnp.float32) * 2.0 / values.shape[-1]))
    angles = positions.astype(jnp.float32)[:, None, None] * freqs[None, None, :]
    cosine = jnp.cos(angles)
    sine = jnp.sin(angles)
    first = values[..., :half]
    second = values[..., half:]
    return jnp.concatenate(
        [first * cosine - second * sine, second * cosine + first * sine], axis=-1
    )


def page_scores(page_of, flat, scores, qrow, start, count, length, maxp):
    rows = qrow.shape[0]
    pos = lax.broadcasted_iota(jnp.int32, (rows, PAGE), 1)

    def one(k):
        j = flat[start + k] % maxp
        s = lax.dot_general(
            qrow, page_of(start + k), (((1,), (1,)), ((), ())),
            preferred_element_type=jnp.float32,
        ) * 0.125
        s = jnp.where(j * PAGE + pos < length, s, neg_large)
        scores[k] = s
        return s

    def two(k2, top):
        s0 = one(2 * k2)
        s1 = one(2 * k2 + 1)
        return jnp.maximum(top, jnp.maximum(s0, s1))

    top = lax.fori_loop(0, count // 2, two, jnp.full((rows, PAGE), neg_large, jnp.float32))
    top = lax.fori_loop(count // 2 * 2, count, lambda k, t: jnp.maximum(t, one(k)), top)
    return jnp.max(top, axis=1, keepdims=True)


def page_values(page_of, flat, scores, top, start, count, length, maxp, lanes):
    rows = top.shape[0]
    pos = lax.broadcasted_iota(jnp.int32, (rows, PAGE), 1)

    def one(k):
        j = flat[start + k] % maxp
        e = jnp.where(j * PAGE + pos < length, jnp.exp(scores[k] - top), 0.0)
        w = e.astype(jnp.bfloat16)
        return e, jnp.dot(w, page_of(start + k), preferred_element_type=jnp.float32)

    def two(k2, carry):
        total, numer = carry
        e0, n0 = one(2 * k2)
        e1, n1 = one(2 * k2 + 1)
        return total + (e0 + e1), numer + (n0 + n1)

    def single(k, carry):
        total, numer = carry
        e0, n0 = one(k)
        return total + e0, numer + n0

    init = (jnp.zeros((rows, PAGE), jnp.float32), jnp.zeros((rows, lanes), jnp.float32))
    carry = lax.fori_loop(0, count // 2, two, init)
    total, numer = lax.fori_loop(count // 2 * 2, count, single, carry)
    return jnp.sum(total, axis=1, keepdims=True), numer


def build_list(tbl, lens, pool_n, maxp, reqs, flat, starts, listed, landing):
    def req(r, carry):
        n, nl = carry
        starts[r] = n
        count = (lens[r] + PAGE - 1) // PAGE

        def page(j, n):
            e = r * maxp + j
            flat[n] = e
            keep = (tbl[e] >= pool_n) if landing else (tbl[e] < pool_n)
            return n + keep.astype(jnp.int32)

        n2 = lax.fori_loop(0, count, page, n)
        listed[nl] = r
        return n2, nl + (n2 > n).astype(jnp.int32)

    n, nl = lax.fori_loop(0, reqs, req, (0, 0))
    starts[reqs] = n
    return n, nl


def query_rows(qwide_ref, r, rows):
    lanes = qwide_ref.shape[2]
    wide = jnp.broadcast_to(qwide_ref[r], (rows, lanes))
    head = lax.broadcasted_iota(jnp.int32, (rows, lanes), 0)
    lane = lax.broadcasted_iota(jnp.int32, (rows, lanes), 1)
    return jnp.where(head == lane // 128, wide, 0.0).astype(jnp.bfloat16)


def pool_kernel(tbl, lens, qrow_ref, snew_ref, pool_ref,
                m_ref, l_ref, n_ref, scores, flat, starts, listed):
    reqs, rows, lanes = snew_ref.shape[0], snew_ref.shape[1], pool_ref.shape[2]
    maxp = scores.shape[0]
    pool_n = pool_ref.shape[0]
    build_list(tbl, lens, pool_n, maxp, reqs, flat, starts, listed, False)
    page_of = lambda f: pool_ref[jnp.clip(tbl[flat[f]], 0, pool_n - 1)]

    def request(r, carry):
        start = starts[r]
        count = starts[r + 1] - start
        length = lens[r]
        snew = snew_ref[r][:, :1]
        top = page_scores(page_of, flat, scores, query_rows(qrow_ref, r, rows), start, count,
                          length, maxp)
        top = jnp.maximum(top, snew)
        total, numer = page_values(page_of, flat, scores, top, start, count, length, maxp,
                                   lanes)
        m_ref[r] = jnp.broadcast_to(top, (rows, 128))
        l_ref[r] = jnp.broadcast_to(total, (rows, 128))
        n_ref[r] = numer
        return carry

    lax.fori_loop(0, reqs, request, 0)


def land_kernel(tbl, lens, qrow_ref, m_in, l_in, n_in, land_ref, pool_n_ref,
                m_ref, l_ref, n_ref, scores, flat, starts, listed):
    reqs, rows, lanes = m_in.shape[0], m_in.shape[1], land_ref.shape[2]
    maxp = scores.shape[0]
    pool_n = pool_n_ref.shape[0]
    land_n = land_ref.shape[0]
    _, listed_n = build_list(tbl, lens, pool_n, maxp, reqs, flat, starts, listed, True)
    m_ref[...] = m_in[...]
    l_ref[...] = l_in[...]
    n_ref[...] = n_in[...]
    page_of = lambda f: land_ref[jnp.clip(tbl[flat[f]] - pool_n, 0, land_n - 1)]

    def request(k, carry):
        r = listed[k]
        start = starts[r]
        count = starts[r + 1] - start
        length = lens[r]
        top_a = m_in[r][:, :1]
        top_b = page_scores(page_of, flat, scores, query_rows(qrow_ref, r, rows), start, count,
                            length, maxp)
        top = jnp.maximum(top_a, top_b)
        total, numer = page_values(page_of, flat, scores, top, start, count, length, maxp,
                                   lanes)
        scale = jnp.exp(top_a - top)
        m_ref[r] = jnp.broadcast_to(top, (rows, 128))
        l_ref[r] = jnp.broadcast_to(total + l_in[r][:, :1] * scale, (rows, 128))
        n_ref[r] = numer + n_in[r] * scale
        return carry

    lax.fori_loop(0, listed_n, request, 0)


def attend(qk, value_new, table, lens, pool, landed_fn):
    req_count = qk.shape[0]
    lanes = pool.shape[2]
    heads_here = lanes // (2 * HEAD_DIM)
    maxp = table.shape[1]
    pool_n = pool.shape[0]
    rows = 8
    lane = jnp.arange(lanes, dtype=jnp.int32)
    qwide = jnp.where((lane % 128 < HEAD_DIM)[None, :], qk.astype(jnp.float32), 0.0)
    qwide = qwide.reshape(req_count, 1, lanes)
    grouped = qk.astype(jnp.float32).reshape(req_count, heads_here, 2 * HEAD_DIM)
    score_new = jnp.sum(grouped[..., :HEAD_DIM] * grouped[..., HEAD_DIM:], axis=-1) * 0.125
    vf = value_new.astype(jnp.float32).reshape(req_count, heads_here, HEAD_DIM)
    snew = jnp.zeros((req_count, rows, 128), jnp.float32) + jnp.pad(
        score_new, ((0, 0), (0, rows - heads_here)))[:, :, None]
    tbl = table.reshape(-1)

    full = lambda shape: pl.BlockSpec(shape, lambda i, *_: (0,) * len(shape))
    big = (req_count, rows, lanes)
    small = (req_count, rows, 128)
    wide = (req_count, 1, lanes)
    scratch = [
        pltpu.VMEM((maxp, rows, PAGE), jnp.float32),
        pltpu.SMEM((req_count * maxp,), jnp.int32),
        pltpu.SMEM((req_count + 1,), jnp.int32),
        pltpu.SMEM((req_count,), jnp.int32),
    ]
    params = pltpu.CompilerParams(
        dimension_semantics=("arbitrary",), vmem_limit_bytes=60 * 1024 * 1024)
    state = [
        jax.ShapeDtypeStruct(small, jnp.float32),
        jax.ShapeDtypeStruct(small, jnp.float32),
        jax.ShapeDtypeStruct(big, jnp.float32),
    ]
    m_a, l_a, n_a = pl.pallas_call(
        pool_kernel,
        grid_spec=pltpu.PrefetchScalarGridSpec(
            num_scalar_prefetch=2,
            grid=(1,),
            in_specs=[full(wide), full(small), pl.BlockSpec(memory_space=pltpu.VMEM)],
            out_specs=[full(small), full(small), full(big)],
            scratch_shapes=scratch,
        ),
        out_shape=state,
        compiler_params=params,
    )(tbl, lens, qwide, snew, pool)

    landed = landed_fn(n_a)
    m_b, l_b, n_b = pl.pallas_call(
        land_kernel,
        grid_spec=pltpu.PrefetchScalarGridSpec(
            num_scalar_prefetch=2,
            grid=(1,),
            in_specs=[full(wide), full(small), full(small), full(big),
                      pl.BlockSpec(memory_space=pltpu.VMEM), pl.BlockSpec(memory_space=pl.ANY)],
            out_specs=[full(small), full(small), full(big)],
            scratch_shapes=scratch,
        ),
        out_shape=state,
        compiler_params=params,
    )(tbl, lens, qwide, m_a, l_a, n_a, landed, pool)
    top = m_b[:, :heads_here, :1]
    e_new = jnp.exp(score_new[:, :, None] - top)
    w_new = e_new.astype(jnp.bfloat16).astype(jnp.float32)
    numer = n_b[:, :heads_here].reshape(req_count, heads_here, heads_here, 2, HEAD_DIM)
    numer = jnp.stack([numer[:, h, h, 1] for h in range(heads_here)], axis=1)
    picked = ((numer + w_new * vf) / (l_b[:, :heads_here, :1] + e_new)).astype(jnp.bfloat16)
    return picked, landed


def migration_plan(pool, mig_src, row_count):
    pool_dev = pool.shape[0]
    land_all = mig_src.shape[0]
    land_dev = land_all // row_count
    src_row = jnp.clip(mig_src // pool_dev, 0, row_count - 1)
    local_page = jnp.clip(mig_src - src_row * pool_dev, 0, pool_dev - 1)
    dst_row = jnp.arange(land_all, dtype=jnp.int32) // land_dev
    onehot = (src_row[:, None] == jnp.arange(row_count, dtype=jnp.int32)[None, :]).astype(jnp.int32)
    csum = jnp.cumsum(onehot.reshape(row_count, land_dev, row_count), axis=1)
    csum = csum.reshape(land_all, row_count)
    rank = jnp.sum(csum * onehot, axis=1) - 1
    return dict(src_row=src_row, local_page=local_page, dst_row=dst_row, rank=rank,
                most=jnp.max(csum), land_dev=land_dev, first=max(1, (land_dev * 5 + 7) // 8))


def outgoing_pages(pool, plan, row_count, lo, size):
    my_row = lax.axis_index("row")
    rank = plan["rank"]
    sel = (plan["src_row"] == my_row) & (rank >= lo) & (rank < lo + size)
    where = jnp.where(sel, plan["dst_row"] * size + (rank - lo), row_count * size)
    idx = jnp.zeros((row_count * size,), jnp.int32).at[where].set(plan["local_page"], mode="drop")
    return jnp.take(pool, idx, axis=0).reshape(row_count, size, pool.shape[1], pool.shape[2])


def migrate_first(pool, mig_src, row_count):
    plan = migration_plan(pool, mig_src, row_count)
    sent = outgoing_pages(pool, plan, row_count, 0, plan["first"])
    return lax.all_to_all(sent, "row", split_axis=0, concat_axis=0, tiled=True)


def migrate_rest(pool, mig_src, row_count, first_recv, dep):
    plan = migration_plan(pool, mig_src, row_count)
    land_dev, k1 = plan["land_dev"], plan["first"]
    my_row = lax.axis_index("row")
    mine = my_row * land_dev + jnp.arange(land_dev, dtype=jnp.int32)
    src_mine = plan["src_row"][mine]
    rank_mine = plan["rank"][mine]
    pool_dep, _ = lax.optimization_barrier((pool, dep))
    sizes = [0, land_dev - k1] if land_dev > k1 else [0]

    def branch(size):
        def run(pool_b, recv1):
            if size == 0:
                both = recv1
            else:
                sent = outgoing_pages(pool_b, plan, row_count, k1, size)
                recv2 = lax.all_to_all(sent, "row", split_axis=0, concat_axis=0, tiled=True)
                both = jnp.concatenate([recv1, recv2], axis=1)
            width = k1 + size
            flat = both.reshape(row_count * width, both.shape[2], both.shape[3])
            return jnp.take(flat, src_mine * width + jnp.clip(rank_mine, 0, width - 1), axis=0)
        return run

    need = jnp.maximum(plan["most"] - k1, 0)
    index = jnp.sum((jnp.array(sizes, jnp.int32) < need).astype(jnp.int32))
    return lax.switch(index, [branch(b) for b in sizes], pool_dep, first_recv)


def on_device(xn, w_qkv, w_out, pool, page_table, lengths, mig_src, deal):
    heads_here = w_out.shape[0] // HEAD_DIM
    rows_all = xn.shape[0] * lax.axis_size("col")
    row_count = lax.axis_size("row")
    req_row = rows_all // row_count
    inverse = jnp.zeros((rows_all,), jnp.int32).at[deal].set(jnp.arange(rows_all, dtype=jnp.int32))
    gathered = lax.all_gather(xn, "col", axis=0, tiled=True)
    chosen = inverse
    heads3 = w_qkv.reshape(w_qkv.shape[0], heads_here, 3, HEAD_DIM)
    w_perm = jnp.concatenate(
        [heads3[:, :, :2].reshape(w_qkv.shape[0], -1), heads3[:, :, 2].reshape(w_qkv.shape[0], -1)],
        axis=1)
    partial = jnp.dot(jnp.take(gathered, chosen, axis=0), w_perm,
                      preferred_element_type=jnp.float32).astype(jnp.bfloat16)
    parts = lax.all_to_all(partial, "row", split_axis=0, concat_axis=0, tiled=True)
    projected = jnp.sum(parts.reshape(row_count, req_row, -1).astype(jnp.float32), axis=0)
    qk_lanes = heads_here * 2 * HEAD_DIM
    x = projected[:, :qk_lanes]
    lane = jnp.arange(qk_lanes, dtype=jnp.int32)
    within = lane % HEAD_DIM
    half = HEAD_DIM // 2
    freqs = theta_base ** (-(jnp.arange(half, dtype=jnp.float32) * 2.0 / HEAD_DIM))
    angles = lengths.astype(jnp.float32)[:, None] * freqs[None, :]
    cosine = jnp.tile(jnp.cos(angles), (1, qk_lanes // half))
    sine = jnp.tile(jnp.sin(angles), (1, qk_lanes // half))
    ahead = jnp.roll(x, -half, axis=1)
    behind = jnp.roll(x, half, axis=1)
    rotated = jnp.where((within < half)[None, :], x * cosine - ahead * sine,
                        x * cosine + behind * sine)
    qk = rotated.astype(jnp.bfloat16)
    value_new = projected[:, qk_lanes:].astype(jnp.bfloat16)
    first = migrate_first(pool, mig_src, row_count)
    mixed, landed = attend(qk, value_new, page_table, lengths, pool,
                           lambda dep: migrate_rest(pool, mig_src, row_count, first, dep))
    mixed = mixed.reshape(req_row, heads_here * HEAD_DIM)
    mixed_all = lax.all_gather(mixed, "row", axis=0, tiled=True)
    chosen = deal
    col_count = lax.axis_size("col")
    partial = jnp.dot(
        jnp.take(mixed_all, chosen, axis=0), w_out, preferred_element_type=jnp.float32
    ).astype(jnp.bfloat16)
    parts = lax.all_to_all(partial, "col", split_axis=0, concat_axis=0, tiled=True)
    attended = jnp.sum(
        parts.reshape(col_count, rows_all // col_count, -1).astype(jnp.float32), axis=0
    ).astype(jnp.bfloat16)
    return (attended, landed)


def solution(mesh):
    placed = (
        P("col", "row"),
        P("row", "col"),
        P("col", "row"),
        P("row", None, "col"),
        P("row", None),
        P("row"),
        P(),
        P(),
    )
    return jax.shard_map(
        on_device,
        mesh=mesh,
        in_specs=placed,
        out_specs=(P("col", "row"), P("row", None, "col")),
        check_vma=False,
    )
```

```python
import functools

import jax
import jax.numpy as jnp
from jax import lax
from jax.experimental import pallas as pl
from jax.experimental.pallas import tpu as pltpu
from jax.sharding import PartitionSpec as P

HEAD_DIM = 64
PAGE = 64


theta_base = 130000.0
neg_large = -1e30


def rotate(values, positions):
    half = values.shape[-1] // 2
    freqs = theta_base ** (-(jnp.arange(half, dtype=jnp.float32) * 2.0 / values.shape[-1]))
    angles = positions.astype(jnp.float32)[:, None, None] * freqs[None, None, :]
    cosine = jnp.cos(angles)
    sine = jnp.sin(angles)
    first = values[..., :half]
    second = values[..., half:]
    return jnp.concatenate(
        [first * cosine - second * sine, second * cosine + first * sine], axis=-1
    )


def page_scores(page_of, flat, scores, qrow, start, count, length, maxp):
    rows = qrow.shape[0]
    pos = lax.broadcasted_iota(jnp.int32, (rows, PAGE), 1)

    def one(k):
        j = flat[start + k] % maxp
        s = lax.dot_general(
            qrow, page_of(start + k), (((1,), (1,)), ((), ())),
            preferred_element_type=jnp.float32,
        ) * 0.125
        s = jnp.where(j * PAGE + pos < length, s, neg_large)
        scores[k] = s
        return s

    def two(k2, top):
        s0 = one(2 * k2)
        s1 = one(2 * k2 + 1)
        return jnp.maximum(top, jnp.maximum(s0, s1))

    top = lax.fori_loop(0, count // 2, two, jnp.full((rows, PAGE), neg_large, jnp.float32))
    top = lax.fori_loop(count // 2 * 2, count, lambda k, t: jnp.maximum(t, one(k)), top)
    return jnp.max(top, axis=1, keepdims=True)


def page_values(page_of, flat, scores, top, start, count, length, maxp, lanes):
    rows = top.shape[0]
    pos = lax.broadcasted_iota(jnp.int32, (rows, PAGE), 1)

    def one(k):
        j = flat[start + k] % maxp
        e = jnp.where(j * PAGE + pos < length, jnp.exp(scores[k] - top), 0.0)
        w = e.astype(jnp.bfloat16)
        return e, jnp.dot(w, page_of(start + k), preferred_element_type=jnp.float32)

    def two(k2, carry):
        total, numer = carry
        e0, n0 = one(2 * k2)
        e1, n1 = one(2 * k2 + 1)
        return total + (e0 + e1), numer + (n0 + n1)

    def single(k, carry):
        total, numer = carry
        e0, n0 = one(k)
        return total + e0, numer + n0

    init = (jnp.zeros((rows, PAGE), jnp.float32), jnp.zeros((rows, lanes), jnp.float32))
    carry = lax.fori_loop(0, count // 2, two, init)
    total, numer = lax.fori_loop(count // 2 * 2, count, single, carry)
    return jnp.sum(total, axis=1, keepdims=True), numer


def build_list(tbl, lens, pool_n, maxp, reqs, flat, starts, listed, landing):
    def req(r, carry):
        n, nl = carry
        starts[r] = n
        count = (lens[r] + PAGE - 1) // PAGE

        def page(j, n):
            e = r * maxp + j
            flat[n] = e
            keep = (tbl[e] >= pool_n) if landing else (tbl[e] < pool_n)
            return n + keep.astype(jnp.int32)

        n2 = lax.fori_loop(0, count, page, n)
        listed[nl] = r
        return n2, nl + (n2 > n).astype(jnp.int32)

    n, nl = lax.fori_loop(0, reqs, req, (0, 0))
    starts[reqs] = n
    return n, nl


def query_rows(qwide_ref, r, rows):
    lanes = qwide_ref.shape[2]
    wide = jnp.broadcast_to(qwide_ref[r], (rows, lanes))
    head = lax.broadcasted_iota(jnp.int32, (rows, lanes), 0)
    lane = lax.broadcasted_iota(jnp.int32, (rows, lanes), 1)
    return jnp.where(head == lane // 128, wide, 0.0).astype(jnp.bfloat16)


def own_block(values):
    rows, lanes = values.shape
    head = lax.broadcasted_iota(jnp.int32, (rows, lanes), 0)
    lane = lax.broadcasted_iota(jnp.int32, (rows, lanes), 1)
    return jnp.sum(jnp.where(head == lane // 128, values, 0.0), axis=0, keepdims=True)


def pool_kernel(tbl, lens, qrow_ref, snew_ref, pool_ref,
                m_ref, l_ref, n_ref, scores, flat, starts, listed):
    reqs, rows, lanes = snew_ref.shape[0], snew_ref.shape[1], pool_ref.shape[2]
    maxp = scores.shape[0]
    pool_n = pool_ref.shape[0]
    build_list(tbl, lens, pool_n, maxp, reqs, flat, starts, listed, False)
    page_of = lambda f: pool_ref[jnp.clip(tbl[flat[f]], 0, pool_n - 1)]

    def request(r, carry):
        start = starts[r]
        count = starts[r + 1] - start
        length = lens[r]
        snew = snew_ref[r][:, :1]
        top = page_scores(page_of, flat, scores, query_rows(qrow_ref, r, rows), start, count,
                          length, maxp)
        top = jnp.maximum(top, snew)
        total, numer = page_values(page_of, flat, scores, top, start, count, length, maxp,
                                   lanes)
        m_ref[r] = jnp.broadcast_to(top, (rows, 128))
        l_ref[r] = jnp.broadcast_to(total, (rows, 128))
        n_ref[r] = own_block(numer)
        return carry

    lax.fori_loop(0, reqs, request, 0)


def land_kernel(tbl, lens, qrow_ref, m_in, l_in, n_in, land_ref, pool_n_ref,
                m_ref, l_ref, n_ref, scores, flat, starts, listed):
    reqs, rows, lanes = m_in.shape[0], m_in.shape[1], land_ref.shape[2]
    maxp = scores.shape[0]
    pool_n = pool_n_ref.shape[0]
    land_n = land_ref.shape[0]
    _, listed_n = build_list(tbl, lens, pool_n, maxp, reqs, flat, starts, listed, True)
    m_ref[...] = m_in[...]
    l_ref[...] = l_in[...]
    n_ref[...] = n_in[...]
    page_of = lambda f: land_ref[jnp.clip(tbl[flat[f]] - pool_n, 0, land_n - 1)]

    def request(k, carry):
        r = listed[k]
        start = starts[r]
        count = starts[r + 1] - start
        length = lens[r]
        top_a = m_in[r][:, :1]
        top_b = page_scores(page_of, flat, scores, query_rows(qrow_ref, r, rows), start, count,
                            length, maxp)
        top = jnp.maximum(top_a, top_b)
        total, numer = page_values(page_of, flat, scores, top, start, count, length, maxp,
                                   lanes)
        scale = jnp.exp(top_a - top)
        m_ref[r] = jnp.broadcast_to(top, (rows, 128))
        l_ref[r] = jnp.broadcast_to(total + l_in[r][:, :1] * scale, (rows, 128))
        n_ref[r] = own_block(numer) + n_in[r] * own_block(jnp.broadcast_to(scale, numer.shape))
        return carry

    lax.fori_loop(0, listed_n, request, 0)


def attend(qk, value_new, table, lens, pool, landed_fn):
    req_count = qk.shape[0]
    lanes = pool.shape[2]
    heads_here = lanes // (2 * HEAD_DIM)
    maxp = table.shape[1]
    pool_n = pool.shape[0]
    rows = 8
    lane = jnp.arange(lanes, dtype=jnp.int32)
    qwide = jnp.where((lane % 128 < HEAD_DIM)[None, :], qk.astype(jnp.float32), 0.0)
    qwide = qwide.reshape(req_count, 1, lanes)
    grouped = qk.astype(jnp.float32).reshape(req_count, heads_here, 2 * HEAD_DIM)
    score_new = jnp.sum(grouped[..., :HEAD_DIM] * grouped[..., HEAD_DIM:], axis=-1) * 0.125
    vf = value_new.astype(jnp.float32).reshape(req_count, heads_here, HEAD_DIM)
    snew = jnp.zeros((req_count, rows, 128), jnp.float32) + jnp.pad(
        score_new, ((0, 0), (0, rows - heads_here)))[:, :, None]
    tbl = table.reshape(-1)

    full = lambda shape: pl.BlockSpec(shape, lambda i, *_: (0,) * len(shape))
    big = (req_count, rows, lanes)
    small = (req_count, rows, 128)
    wide = (req_count, 1, lanes)
    scratch = [
        pltpu.VMEM((maxp, rows, PAGE), jnp.float32),
        pltpu.SMEM((req_count * maxp,), jnp.int32),
        pltpu.SMEM((req_count + 1,), jnp.int32),
        pltpu.SMEM((req_count,), jnp.int32),
    ]
    params = pltpu.CompilerParams(
        dimension_semantics=("arbitrary",), vmem_limit_bytes=60 * 1024 * 1024)
    state = [
        jax.ShapeDtypeStruct(small, jnp.float32),
        jax.ShapeDtypeStruct(small, jnp.float32),
        jax.ShapeDtypeStruct(wide, jnp.float32),
    ]
    m_a, l_a, n_a = pl.pallas_call(
        pool_kernel,
        grid_spec=pltpu.PrefetchScalarGridSpec(
            num_scalar_prefetch=2,
            grid=(1,),
            in_specs=[full(wide), full(small), pl.BlockSpec(memory_space=pltpu.VMEM)],
            out_specs=[full(small), full(small), full(wide)],
            scratch_shapes=scratch,
        ),
        out_shape=state,
        compiler_params=params,
    )(tbl, lens, qwide, snew, pool)

    landed = landed_fn(n_a)
    m_b, l_b, n_b = pl.pallas_call(
        land_kernel,
        grid_spec=pltpu.PrefetchScalarGridSpec(
            num_scalar_prefetch=2,
            grid=(1,),
            in_specs=[full(wide), full(small), full(small), full(wide),
                      pl.BlockSpec(memory_space=pltpu.VMEM), pl.BlockSpec(memory_space=pl.ANY)],
            out_specs=[full(small), full(small), full(wide)],
            scratch_shapes=scratch,
        ),
        out_shape=state,
        compiler_params=params,
    )(tbl, lens, qwide, m_a, l_a, n_a, landed, pool)
    top = m_b[:, :heads_here, :1]
    e_new = jnp.exp(score_new[:, :, None] - top)
    w_new = e_new.astype(jnp.bfloat16).astype(jnp.float32)
    numer = n_b.reshape(req_count, heads_here, 2, HEAD_DIM)[:, :, 1]
    picked = ((numer + w_new * vf) / (l_b[:, :heads_here, :1] + e_new)).astype(jnp.bfloat16)
    return picked, landed


def migration_plan(pool, mig_src, row_count):
    pool_dev = pool.shape[0]
    land_all = mig_src.shape[0]
    land_dev = land_all // row_count
    src_row = jnp.clip(mig_src // pool_dev, 0, row_count - 1)
    local_page = jnp.clip(mig_src - src_row * pool_dev, 0, pool_dev - 1)
    dst_row = jnp.arange(land_all, dtype=jnp.int32) // land_dev
    onehot = (src_row[:, None] == jnp.arange(row_count, dtype=jnp.int32)[None, :]).astype(jnp.int32)
    csum = jnp.cumsum(onehot.reshape(row_count, land_dev, row_count), axis=1)
    csum = csum.reshape(land_all, row_count)
    rank = jnp.sum(csum * onehot, axis=1) - 1
    return dict(src_row=src_row, local_page=local_page, dst_row=dst_row, rank=rank,
                most=jnp.max(csum), land_dev=land_dev, first=max(1, (land_dev * 5 + 7) // 8))


def outgoing_pages(pool, plan, row_count, lo, size):
    my_row = lax.axis_index("row")
    rank = plan["rank"]
    sel = (plan["src_row"] == my_row) & (rank >= lo) & (rank < lo + size)
    where = jnp.where(sel, plan["dst_row"] * size + (rank - lo), row_count * size)
    idx = jnp.zeros((row_count * size,), jnp.int32).at[where].set(plan["local_page"], mode="drop")
    return jnp.take(pool, idx, axis=0).reshape(row_count, size, pool.shape[1], pool.shape[2])


def migrate_first(pool, mig_src, row_count):
    plan = migration_plan(pool, mig_src, row_count)
    sent = outgoing_pages(pool, plan, row_count, 0, plan["first"])
    return lax.all_to_all(sent, "row", split_axis=0, concat_axis=0, tiled=True)


def migrate_rest(pool, mig_src, row_count, first_recv, dep):
    plan = migration_plan(pool, mig_src, row_count)
    land_dev, k1 = plan["land_dev"], plan["first"]
    my_row = lax.axis_index("row")
    mine = my_row * land_dev + jnp.arange(land_dev, dtype=jnp.int32)
    src_mine = plan["src_row"][mine]
    rank_mine = plan["rank"][mine]
    pool_dep, _ = lax.optimization_barrier((pool, dep))
    sizes = [0, land_dev - k1] if land_dev > k1 else [0]

    def branch(size):
        def run(pool_b, recv1):
            if size == 0:
                both = recv1
            else:
                sent = outgoing_pages(pool_b, plan, row_count, k1, size)
                recv2 = lax.all_to_all(sent, "row", split_axis=0, concat_axis=0, tiled=True)
                both = jnp.concatenate([recv1, recv2], axis=1)
            width = k1 + size
            flat = both.reshape(row_count * width, both.shape[2], both.shape[3])
            return jnp.take(flat, src_mine * width + jnp.clip(rank_mine, 0, width - 1), axis=0)
        return run

    need = jnp.maximum(plan["most"] - k1, 0)
    index = jnp.sum((jnp.array(sizes, jnp.int32) < need).astype(jnp.int32))
    return lax.switch(index, [branch(b) for b in sizes], pool_dep, first_recv)


def on_device(xn, w_qkv, w_out, pool, page_table, lengths, mig_src, deal):
    heads_here = w_out.shape[0] // HEAD_DIM
    rows_all = xn.shape[0] * lax.axis_size("col")
    row_count = lax.axis_size("row")
    req_row = rows_all // row_count
    inverse = jnp.zeros((rows_all,), jnp.int32).at[deal].set(jnp.arange(rows_all, dtype=jnp.int32))
    gathered = lax.all_gather(xn, "col", axis=0, tiled=True)
    chosen = inverse
    heads3 = w_qkv.reshape(w_qkv.shape[0], heads_here, 3, HEAD_DIM)
    w_perm = jnp.concatenate(
        [heads3[:, :, :2].reshape(w_qkv.shape[0], -1), heads3[:, :, 2].reshape(w_qkv.shape[0], -1)],
        axis=1)
    partial = jnp.dot(jnp.take(gathered, chosen, axis=0), w_perm,
                      preferred_element_type=jnp.float32).astype(jnp.bfloat16)
    parts = lax.all_to_all(partial, "row", split_axis=0, concat_axis=0, tiled=True)
    projected = jnp.sum(parts.reshape(row_count, req_row, -1).astype(jnp.float32), axis=0)
    qk_lanes = heads_here * 2 * HEAD_DIM
    x = projected[:, :qk_lanes]
    lane = jnp.arange(qk_lanes, dtype=jnp.int32)
    within = lane % HEAD_DIM
    half = HEAD_DIM // 2
    freqs = theta_base ** (-(jnp.arange(half, dtype=jnp.float32) * 2.0 / HEAD_DIM))
    angles = lengths.astype(jnp.float32)[:, None] * freqs[None, :]
    cosine = jnp.tile(jnp.cos(angles), (1, qk_lanes // half))
    sine = jnp.tile(jnp.sin(angles), (1, qk_lanes // half))
    ahead = jnp.roll(x, -half, axis=1)
    behind = jnp.roll(x, half, axis=1)
    rotated = jnp.where((within < half)[None, :], x * cosine - ahead * sine,
                        x * cosine + behind * sine)
    qk = rotated.astype(jnp.bfloat16)
    value_new = projected[:, qk_lanes:].astype(jnp.bfloat16)
    first = migrate_first(pool, mig_src, row_count)
    mixed, landed = attend(qk, value_new, page_table, lengths, pool,
                           lambda dep: migrate_rest(pool, mig_src, row_count, first, dep))
    mixed = mixed.reshape(req_row, heads_here * HEAD_DIM)
    mixed_all = lax.all_gather(mixed, "row", axis=0, tiled=True)
    chosen = deal
    col_count = lax.axis_size("col")
    partial = jnp.dot(
        jnp.take(mixed_all, chosen, axis=0), w_out, preferred_element_type=jnp.float32
    ).astype(jnp.bfloat16)
    parts = lax.all_to_all(partial, "col", split_axis=0, concat_axis=0, tiled=True)
    attended = jnp.sum(
        parts.reshape(col_count, rows_all // col_count, -1).astype(jnp.float32), axis=0
    ).astype(jnp.bfloat16)
    return (attended, landed)


def solution(mesh):
    placed = (
        P("col", "row"),
        P("row", "col"),
        P("col", "row"),
        P("row", None, "col"),
        P("row", None),
        P("row"),
        P(),
        P(),
    )
    return jax.shard_map(
        on_device,
        mesh=mesh,
        in_specs=placed,
        out_specs=(P("col", "row"), P("row", None, "col")),
        check_vma=False,
    )
```

```python
import functools

import jax
import jax.numpy as jnp
from jax import lax
from jax.experimental import pallas as pl
from jax.experimental.pallas import tpu as pltpu
from jax.sharding import PartitionSpec as P

HEAD_DIM = 64
PAGE = 64


theta_base = 130000.0
neg_large = -1e30


def rotate(values, positions):
    half = values.shape[-1] // 2
    freqs = theta_base ** (-(jnp.arange(half, dtype=jnp.float32) * 2.0 / values.shape[-1]))
    angles = positions.astype(jnp.float32)[:, None, None] * freqs[None, None, :]
    cosine = jnp.cos(angles)
    sine = jnp.sin(angles)
    first = values[..., :half]
    second = values[..., half:]
    return jnp.concatenate(
        [first * cosine - second * sine, second * cosine + first * sine], axis=-1
    )


def page_scores(page_of, flat, scores, qrow, start, count, length, maxp):
    rows = qrow.shape[0]
    pos = lax.broadcasted_iota(jnp.int32, (rows, PAGE), 1)

    def one(k):
        j = flat[start + k] % maxp
        s = lax.dot_general(
            qrow, page_of(start + k), (((1,), (1,)), ((), ())),
            preferred_element_type=jnp.float32,
        ) * 0.125
        s = jnp.where(j * PAGE + pos < length, s, neg_large)
        scores[k] = s
        return s

    def two(k2, top):
        s0 = one(2 * k2)
        s1 = one(2 * k2 + 1)
        return jnp.maximum(top, jnp.maximum(s0, s1))

    top = lax.fori_loop(0, count // 2, two, jnp.full((rows, PAGE), neg_large, jnp.float32))
    top = lax.fori_loop(count // 2 * 2, count, lambda k, t: jnp.maximum(t, one(k)), top)
    return jnp.max(top, axis=1, keepdims=True)


def page_values(page_of, flat, scores, top, start, count, length, maxp, lanes):
    rows = top.shape[0]
    pos = lax.broadcasted_iota(jnp.int32, (rows, PAGE), 1)

    def one(k):
        j = flat[start + k] % maxp
        e = jnp.where(j * PAGE + pos < length, jnp.exp(scores[k] - top), 0.0)
        w = e.astype(jnp.bfloat16)
        return e, jnp.dot(w, page_of(start + k), preferred_element_type=jnp.float32)

    def two(k2, carry):
        total, numer = carry
        e0, n0 = one(2 * k2)
        e1, n1 = one(2 * k2 + 1)
        return total + (e0 + e1), numer + (n0 + n1)

    def single(k, carry):
        total, numer = carry
        e0, n0 = one(k)
        return total + e0, numer + n0

    init = (jnp.zeros((rows, PAGE), jnp.float32), jnp.zeros((rows, lanes), jnp.float32))
    carry = lax.fori_loop(0, count // 2, two, init)
    total, numer = lax.fori_loop(count // 2 * 2, count, single, carry)
    return jnp.sum(total, axis=1, keepdims=True), numer


def build_list(tbl, lens, pool_n, maxp, reqs, flat, starts, listed, landing):
    def req(r, carry):
        n, nl = carry
        starts[r] = n
        count = (lens[r] + PAGE - 1) // PAGE

        def page(j, n):
            e = r * maxp + j
            flat[n] = e
            keep = (tbl[e] >= pool_n) if landing else (tbl[e] < pool_n)
            return n + keep.astype(jnp.int32)

        n2 = lax.fori_loop(0, count, page, n)
        listed[nl] = r
        return n2, nl + (n2 > n).astype(jnp.int32)

    n, nl = lax.fori_loop(0, reqs, req, (0, 0))
    starts[reqs] = n
    return n, nl


def query_rows(qwide_ref, r, rows):
    lanes = qwide_ref.shape[2]
    wide = jnp.broadcast_to(qwide_ref[r], (rows, lanes))
    head = lax.broadcasted_iota(jnp.int32, (rows, lanes), 0)
    lane = lax.broadcasted_iota(jnp.int32, (rows, lanes), 1)
    return jnp.where(head == lane // 128, wide, 0.0).astype(jnp.bfloat16)


def pool_kernel(tbl, lens, qrow_ref, snew_ref, pool_ref,
                m_ref, l_ref, n_ref, scores, flat, starts, listed):
    reqs, rows, lanes = snew_ref.shape[0], snew_ref.shape[1], pool_ref.shape[2]
    maxp = scores.shape[0]
    pool_n = pool_ref.shape[0]
    build_list(tbl, lens, pool_n, maxp, reqs, flat, starts, listed, False)
    page_of = lambda f: pool_ref[jnp.clip(tbl[flat[f]], 0, pool_n - 1)]

    def request(r, carry):
        start = starts[r]
        count = starts[r + 1] - start
        length = lens[r]
        snew = snew_ref[r][:, :1]
        top = page_scores(page_of, flat, scores, query_rows(qrow_ref, r, rows), start, count,
                          length, maxp)
        top = jnp.maximum(top, snew)
        total, numer = page_values(page_of, flat, scores, top, start, count, length, maxp,
                                   lanes)
        m_ref[r] = jnp.broadcast_to(top, (rows, 128))
        l_ref[r] = jnp.broadcast_to(total, (rows, 128))
        n_ref[r] = numer
        return carry

    lax.fori_loop(0, reqs, request, 0)


def land_kernel(tbl, lens, qrow_ref, m_in, l_in, n_in, land_ref, pool_n_ref,
                m_ref, l_ref, n_ref, scores, flat, starts, listed):
    reqs, rows, lanes = m_in.shape[0], m_in.shape[1], land_ref.shape[2]
    maxp = scores.shape[0]
    pool_n = pool_n_ref.shape[0]
    land_n = land_ref.shape[0]
    _, listed_n = build_list(tbl, lens, pool_n, maxp, reqs, flat, starts, listed, True)
    m_ref[...] = m_in[...]
    l_ref[...] = l_in[...]
    n_ref[...] = n_in[...]
    page_of = lambda f: land_ref[jnp.clip(tbl[flat[f]] - pool_n, 0, land_n - 1)]

    def request(k, carry):
        r = listed[k]
        start = starts[r]
        count = starts[r + 1] - start
        length = lens[r]
        top_a = m_in[r][:, :1]
        top_b = page_scores(page_of, flat, scores, query_rows(qrow_ref, r, rows), start, count,
                            length, maxp)
        top = jnp.maximum(top_a, top_b)
        total, numer = page_values(page_of, flat, scores, top, start, count, length, maxp,
                                   lanes)
        scale = jnp.exp(top_a - top)
        m_ref[r] = jnp.broadcast_to(top, (rows, 128))
        l_ref[r] = jnp.broadcast_to(total + l_in[r][:, :1] * scale, (rows, 128))
        n_ref[r] = numer + n_in[r] * scale
        return carry

    lax.fori_loop(0, listed_n, request, 0)


def attend(qk, value_new, table, lens, pool, landed_fn):
    req_count = qk.shape[0]
    lanes = pool.shape[2]
    heads_here = lanes // (2 * HEAD_DIM)
    maxp = table.shape[1]
    pool_n = pool.shape[0]
    rows = 8
    lane = jnp.arange(lanes, dtype=jnp.int32)
    qwide = jnp.where((lane % 128 < HEAD_DIM)[None, :], qk.astype(jnp.float32), 0.0)
    qwide = qwide.reshape(req_count, 1, lanes)
    grouped = qk.astype(jnp.float32).reshape(req_count, heads_here, 2 * HEAD_DIM)
    score_new = jnp.sum(grouped[..., :HEAD_DIM] * grouped[..., HEAD_DIM:], axis=-1) * 0.125
    vf = value_new.astype(jnp.float32).reshape(req_count, heads_here, HEAD_DIM)
    snew = jnp.zeros((req_count, rows, 128), jnp.float32) + jnp.pad(
        score_new, ((0, 0), (0, rows - heads_here)))[:, :, None]
    tbl = table.reshape(-1)

    full = lambda shape: pl.BlockSpec(shape, lambda i, *_: (0,) * len(shape))
    big = (req_count, rows, lanes)
    small = (req_count, rows, 128)
    wide = (req_count, 1, lanes)
    scratch = [
        pltpu.VMEM((maxp, rows, PAGE), jnp.float32),
        pltpu.SMEM((req_count * maxp,), jnp.int32),
        pltpu.SMEM((req_count + 1,), jnp.int32),
        pltpu.SMEM((req_count,), jnp.int32),
    ]
    params = pltpu.CompilerParams(
        dimension_semantics=("arbitrary",), vmem_limit_bytes=60 * 1024 * 1024)
    state = [
        jax.ShapeDtypeStruct(small, jnp.float32),
        jax.ShapeDtypeStruct(small, jnp.float32),
        jax.ShapeDtypeStruct(big, jnp.float32),
    ]
    m_a, l_a, n_a = pl.pallas_call(
        pool_kernel,
        grid_spec=pltpu.PrefetchScalarGridSpec(
            num_scalar_prefetch=2,
            grid=(1,),
            in_specs=[full(wide), full(small), pl.BlockSpec(memory_space=pltpu.VMEM)],
            out_specs=[full(small), full(small), full(big)],
            scratch_shapes=scratch,
        ),
        out_shape=state,
        compiler_params=params,
    )(tbl, lens, qwide, snew, pool)

    landed = landed_fn(n_a)
    m_b, l_b, n_b = pl.pallas_call(
        land_kernel,
        grid_spec=pltpu.PrefetchScalarGridSpec(
            num_scalar_prefetch=2,
            grid=(1,),
            in_specs=[full(wide), full(small), full(small), full(big),
                      pl.BlockSpec(memory_space=pltpu.VMEM), pl.BlockSpec(memory_space=pl.ANY)],
            out_specs=[full(small), full(small), full(big)],
            scratch_shapes=scratch,
        ),
        out_shape=state,
        compiler_params=params,
    )(tbl, lens, qwide, m_a, l_a, n_a, landed, pool)
    top = m_b[:, :heads_here, :1]
    e_new = jnp.exp(score_new[:, :, None] - top)
    w_new = e_new.astype(jnp.bfloat16).astype(jnp.float32)
    numer = n_b[:, :heads_here].reshape(req_count, heads_here, heads_here, 2, HEAD_DIM)
    numer = jnp.stack([numer[:, h, h, 1] for h in range(heads_here)], axis=1)
    picked = ((numer + w_new * vf) / (l_b[:, :heads_here, :1] + e_new)).astype(jnp.bfloat16)
    return picked, landed


def migration_plan(pool, mig_src, row_count):
    pool_dev = pool.shape[0]
    land_all = mig_src.shape[0]
    land_dev = land_all // row_count
    src_row = jnp.clip(mig_src // pool_dev, 0, row_count - 1)
    local_page = jnp.clip(mig_src - src_row * pool_dev, 0, pool_dev - 1)
    dst_row = jnp.arange(land_all, dtype=jnp.int32) // land_dev
    onehot = (src_row[:, None] == jnp.arange(row_count, dtype=jnp.int32)[None, :]).astype(jnp.int32)
    csum = jnp.cumsum(onehot.reshape(row_count, land_dev, row_count), axis=1)
    csum = csum.reshape(land_all, row_count)
    rank = jnp.sum(csum * onehot, axis=1) - 1
    return dict(src_row=src_row, local_page=local_page, dst_row=dst_row, rank=rank,
                most=jnp.max(csum), land_dev=land_dev, first=max(1, (land_dev * 5 + 7) // 8))


def gather_kernel(idx_ref, pool_ref, out_ref, sems):
    count = out_ref.shape[0]
    pool_n = pool_ref.shape[0]

    def start(i, carry):
        src = jnp.clip(idx_ref[i], 0, pool_n - 1)
        pltpu.make_async_copy(pool_ref.at[src], out_ref.at[i], sems.at[i]).start()
        return carry

    def wait(i, carry):
        pltpu.make_async_copy(pool_ref.at[0], out_ref.at[i], sems.at[i]).wait()
        return carry

    lax.fori_loop(0, count, start, 0)
    lax.fori_loop(0, count, wait, 0)


def outgoing_pages(pool, plan, row_count, lo, size):
    my_row = lax.axis_index("row")
    rank = plan["rank"]
    sel = (plan["src_row"] == my_row) & (rank >= lo) & (rank < lo + size)
    where = jnp.where(sel, plan["dst_row"] * size + (rank - lo), row_count * size)
    idx = jnp.zeros((row_count * size,), jnp.int32).at[where].set(plan["local_page"], mode="drop")
    count = row_count * size
    pages = pl.pallas_call(
        gather_kernel,
        grid_spec=pltpu.PrefetchScalarGridSpec(
            num_scalar_prefetch=1,
            grid=(1,),
            in_specs=[pl.BlockSpec(memory_space=pl.ANY)],
            out_specs=pl.BlockSpec((count,) + pool.shape[1:], lambda i, *_: (0, 0, 0)),
            scratch_shapes=[pltpu.SemaphoreType.DMA((count,))],
        ),
        out_shape=jax.ShapeDtypeStruct((count,) + pool.shape[1:], pool.dtype),
        compiler_params=pltpu.CompilerParams(vmem_limit_bytes=32 * 1024 * 1024),
    )(idx, pool)
    return pages.reshape(row_count, size, pool.shape[1], pool.shape[2])


def migrate_first(pool, mig_src, row_count):
    plan = migration_plan(pool, mig_src, row_count)
    sent = outgoing_pages(pool, plan, row_count, 0, plan["first"])
    return lax.all_to_all(sent, "row", split_axis=0, concat_axis=0, tiled=True)


def migrate_rest(pool, mig_src, row_count, first_recv, dep):
    plan = migration_plan(pool, mig_src, row_count)
    land_dev, k1 = plan["land_dev"], plan["first"]
    my_row = lax.axis_index("row")
    mine = my_row * land_dev + jnp.arange(land_dev, dtype=jnp.int32)
    src_mine = plan["src_row"][mine]
    rank_mine = plan["rank"][mine]
    pool_dep, _ = lax.optimization_barrier((pool, dep))
    sizes = [0, land_dev - k1] if land_dev > k1 else [0]

    def branch(size):
        def run(pool_b, recv1):
            if size == 0:
                both = recv1
            else:
                sent = outgoing_pages(pool_b, plan, row_count, k1, size)
                recv2 = lax.all_to_all(sent, "row", split_axis=0, concat_axis=0, tiled=True)
                both = jnp.concatenate([recv1, recv2], axis=1)
            width = k1 + size
            flat = both.reshape(row_count * width, both.shape[2], both.shape[3])
            return jnp.take(flat, src_mine * width + jnp.clip(rank_mine, 0, width - 1), axis=0)
        return run

    need = jnp.maximum(plan["most"] - k1, 0)
    index = jnp.sum((jnp.array(sizes, jnp.int32) < need).astype(jnp.int32))
    return lax.switch(index, [branch(b) for b in sizes], pool_dep, first_recv)


def on_device(xn, w_qkv, w_out, pool, page_table, lengths, mig_src, deal):
    heads_here = w_out.shape[0] // HEAD_DIM
    rows_all = xn.shape[0] * lax.axis_size("col")
    row_count = lax.axis_size("row")
    req_row = rows_all // row_count
    inverse = jnp.zeros((rows_all,), jnp.int32).at[deal].set(jnp.arange(rows_all, dtype=jnp.int32))
    gathered = lax.all_gather(xn, "col", axis=0, tiled=True)
    chosen = inverse
    heads3 = w_qkv.reshape(w_qkv.shape[0], heads_here, 3, HEAD_DIM)
    w_perm = jnp.concatenate(
        [heads3[:, :, :2].reshape(w_qkv.shape[0], -1), heads3[:, :, 2].reshape(w_qkv.shape[0], -1)],
        axis=1)
    partial = jnp.dot(jnp.take(gathered, chosen, axis=0), w_perm,
                      preferred_element_type=jnp.float32).astype(jnp.bfloat16)
    parts = lax.all_to_all(partial, "row", split_axis=0, concat_axis=0, tiled=True)
    projected = jnp.sum(parts.reshape(row_count, req_row, -1).astype(jnp.float32), axis=0)
    qk_lanes = heads_here * 2 * HEAD_DIM
    x = projected[:, :qk_lanes]
    lane = jnp.arange(qk_lanes, dtype=jnp.int32)
    within = lane % HEAD_DIM
    half = HEAD_DIM // 2
    freqs = theta_base ** (-(jnp.arange(half, dtype=jnp.float32) * 2.0 / HEAD_DIM))
    angles = lengths.astype(jnp.float32)[:, None] * freqs[None, :]
    cosine = jnp.tile(jnp.cos(angles), (1, qk_lanes // half))
    sine = jnp.tile(jnp.sin(angles), (1, qk_lanes // half))
    ahead = jnp.roll(x, -half, axis=1)
    behind = jnp.roll(x, half, axis=1)
    rotated = jnp.where((within < half)[None, :], x * cosine - ahead * sine,
                        x * cosine + behind * sine)
    qk = rotated.astype(jnp.bfloat16)
    value_new = projected[:, qk_lanes:].astype(jnp.bfloat16)
    first = migrate_first(pool, mig_src, row_count)
    mixed, landed = attend(qk, value_new, page_table, lengths, pool,
                           lambda dep: migrate_rest(pool, mig_src, row_count, first, dep))
    mixed = mixed.reshape(req_row, heads_here * HEAD_DIM)
    mixed_all = lax.all_gather(mixed, "row", axis=0, tiled=True)
    chosen = deal
    col_count = lax.axis_size("col")
    partial = jnp.dot(
        jnp.take(mixed_all, chosen, axis=0), w_out, preferred_element_type=jnp.float32
    ).astype(jnp.bfloat16)
    parts = lax.all_to_all(partial, "col", split_axis=0, concat_axis=0, tiled=True)
    attended = jnp.sum(
        parts.reshape(col_count, rows_all // col_count, -1).astype(jnp.float32), axis=0
    ).astype(jnp.bfloat16)
    return (attended, landed)


def solution(mesh):
    placed = (
        P("col", "row"),
        P("row", "col"),
        P("col", "row"),
        P("row", None, "col"),
        P("row", None),
        P("row"),
        P(),
        P(),
    )
    return jax.shard_map(
        on_device,
        mesh=mesh,
        in_specs=placed,
        out_specs=(P("col", "row"), P("row", None, "col")),
        check_vma=False,
    )
```

```python
import functools

import jax
import jax.numpy as jnp
from jax import lax
from jax.experimental import pallas as pl
from jax.experimental.pallas import tpu as pltpu
from jax.sharding import PartitionSpec as P

HEAD_DIM = 64
PAGE = 64


theta_base = 130000.0
neg_large = -1e30


def rotate(values, positions):
    half = values.shape[-1] // 2
    freqs = theta_base ** (-(jnp.arange(half, dtype=jnp.float32) * 2.0 / values.shape[-1]))
    angles = positions.astype(jnp.float32)[:, None, None] * freqs[None, None, :]
    cosine = jnp.cos(angles)
    sine = jnp.sin(angles)
    first = values[..., :half]
    second = values[..., half:]
    return jnp.concatenate(
        [first * cosine - second * sine, second * cosine + first * sine], axis=-1
    )


def page_scores(page_of, flat, scores, qrow, start, count, length, maxp):
    rows = qrow.shape[0]
    pos = lax.broadcasted_iota(jnp.int32, (rows, PAGE), 1)

    def one(k):
        j = flat[start + k] % maxp
        s = lax.dot_general(
            qrow, page_of(start + k), (((1,), (1,)), ((), ())),
            preferred_element_type=jnp.float32,
        ) * 0.125
        s = jnp.where(j * PAGE + pos < length, s, neg_large)
        scores[k] = s
        return s

    def two(k2, top):
        s0 = one(2 * k2)
        s1 = one(2 * k2 + 1)
        return jnp.maximum(top, jnp.maximum(s0, s1))

    top = lax.fori_loop(0, count // 2, two, jnp.full((rows, PAGE), neg_large, jnp.float32))
    top = lax.fori_loop(count // 2 * 2, count, lambda k, t: jnp.maximum(t, one(k)), top)
    return jnp.max(top, axis=1, keepdims=True)


def page_values(page_of, flat, scores, top, start, count, length, maxp, lanes):
    rows = top.shape[0]
    pos = lax.broadcasted_iota(jnp.int32, (rows, PAGE), 1)

    def one(k):
        j = flat[start + k] % maxp
        e = jnp.where(j * PAGE + pos < length, jnp.exp(scores[k] - top), 0.0)
        w = e.astype(jnp.bfloat16)
        return e, jnp.dot(w, page_of(start + k), preferred_element_type=jnp.float32)

    def two(k2, carry):
        total, numer = carry
        e0, n0 = one(2 * k2)
        e1, n1 = one(2 * k2 + 1)
        return total + (e0 + e1), numer + (n0 + n1)

    def single(k, carry):
        total, numer = carry
        e0, n0 = one(k)
        return total + e0, numer + n0

    init = (jnp.zeros((rows, PAGE), jnp.float32), jnp.zeros((rows, lanes), jnp.float32))
    carry = lax.fori_loop(0, count // 2, two, init)
    total, numer = lax.fori_loop(count // 2 * 2, count, single, carry)
    return jnp.sum(total, axis=1, keepdims=True), numer


def build_list(tbl, lens, pool_n, maxp, reqs, flat, starts, listed, landing):
    def req(r, carry):
        n, nl = carry
        starts[r] = n
        count = (lens[r] + PAGE - 1) // PAGE

        def page(j, n):
            e = r * maxp + j
            flat[n] = e
            keep = (tbl[e] >= pool_n) if landing else (tbl[e] < pool_n)
            return n + keep.astype(jnp.int32)

        n2 = lax.fori_loop(0, count, page, n)
        listed[nl] = r
        return n2, nl + (n2 > n).astype(jnp.int32)

    n, nl = lax.fori_loop(0, reqs, req, (0, 0))
    starts[reqs] = n
    return n, nl


def query_rows(qwide_ref, r, rows):
    lanes = qwide_ref.shape[2]
    wide = jnp.broadcast_to(qwide_ref[r], (rows, lanes))
    head = lax.broadcasted_iota(jnp.int32, (rows, lanes), 0)
    lane = lax.broadcasted_iota(jnp.int32, (rows, lanes), 1)
    return jnp.where(head == lane // 128, wide, 0.0).astype(jnp.bfloat16)


def pool_kernel(tbl, lens, qrow_ref, snew_ref, pool_ref,
                m_ref, l_ref, n_ref, scores, flat, starts, listed):
    reqs, rows, lanes = snew_ref.shape[0], snew_ref.shape[1], pool_ref.shape[2]
    maxp = scores.shape[0]
    pool_n = pool_ref.shape[0]
    build_list(tbl, lens, pool_n, maxp, reqs, flat, starts, listed, False)
    page_of = lambda f: pool_ref[jnp.clip(tbl[flat[f]], 0, pool_n - 1)]

    def request(r, carry):
        start = starts[r]
        count = starts[r + 1] - start
        length = lens[r]
        snew = snew_ref[r][:, :1]
        top = page_scores(page_of, flat, scores, query_rows(qrow_ref, r, rows), start, count,
                          length, maxp)
        top = jnp.maximum(top, snew)
        total, numer = page_values(page_of, flat, scores, top, start, count, length, maxp,
                                   lanes)
        m_ref[r] = jnp.broadcast_to(top, (rows, 128))
        l_ref[r] = jnp.broadcast_to(total, (rows, 128))
        n_ref[r] = numer
        return carry

    lax.fori_loop(0, reqs, request, 0)


def land_kernel(tbl, lens, qrow_ref, m_in, l_in, n_in, land_ref, pool_n_ref,
                m_ref, l_ref, n_ref, scores, flat, starts, listed):
    reqs, rows, lanes = m_in.shape[0], m_in.shape[1], land_ref.shape[2]
    maxp = scores.shape[0]
    pool_n = pool_n_ref.shape[0]
    land_n = land_ref.shape[0]
    _, listed_n = build_list(tbl, lens, pool_n, maxp, reqs, flat, starts, listed, True)
    m_ref[...] = m_in[...]
    l_ref[...] = l_in[...]
    n_ref[...] = n_in[...]
    page_of = lambda f: land_ref[jnp.clip(tbl[flat[f]] - pool_n, 0, land_n - 1)]

    def request(k, carry):
        r = listed[k]
        start = starts[r]
        count = starts[r + 1] - start
        length = lens[r]
        top_a = m_in[r][:, :1]
        top_b = page_scores(page_of, flat, scores, query_rows(qrow_ref, r, rows), start, count,
                            length, maxp)
        top = jnp.maximum(top_a, top_b)
        total, numer = page_values(page_of, flat, scores, top, start, count, length, maxp,
                                   lanes)
        scale = jnp.exp(top_a - top)
        m_ref[r] = jnp.broadcast_to(top, (rows, 128))
        l_ref[r] = jnp.broadcast_to(total + l_in[r][:, :1] * scale, (rows, 128))
        n_ref[r] = numer + n_in[r] * scale
        return carry

    lax.fori_loop(0, listed_n, request, 0)


def attend(qk, value_new, table, lens, pool, landed_fn):
    req_count = qk.shape[0]
    lanes = pool.shape[2]
    heads_here = lanes // (2 * HEAD_DIM)
    maxp = table.shape[1]
    pool_n = pool.shape[0]
    rows = 8
    lane = jnp.arange(lanes, dtype=jnp.int32)
    qwide = jnp.where((lane % 128 < HEAD_DIM)[None, :], qk.astype(jnp.float32), 0.0)
    qwide = qwide.reshape(req_count, 1, lanes)
    grouped = qk.astype(jnp.float32).reshape(req_count, heads_here, 2 * HEAD_DIM)
    score_new = jnp.sum(grouped[..., :HEAD_DIM] * grouped[..., HEAD_DIM:], axis=-1) * 0.125
    vf = value_new.astype(jnp.float32).reshape(req_count, heads_here, HEAD_DIM)
    snew = jnp.zeros((req_count, rows, 128), jnp.float32) + jnp.pad(
        score_new, ((0, 0), (0, rows - heads_here)))[:, :, None]
    tbl = table.reshape(-1)

    full = lambda shape: pl.BlockSpec(shape, lambda i, *_: (0,) * len(shape))
    big = (req_count, rows, lanes)
    small = (req_count, rows, 128)
    wide = (req_count, 1, lanes)
    scratch = [
        pltpu.VMEM((maxp, rows, PAGE), jnp.float32),
        pltpu.SMEM((req_count * maxp,), jnp.int32),
        pltpu.SMEM((req_count + 1,), jnp.int32),
        pltpu.SMEM((req_count,), jnp.int32),
    ]
    params = pltpu.CompilerParams(
        dimension_semantics=("arbitrary",), vmem_limit_bytes=60 * 1024 * 1024)
    state = [
        jax.ShapeDtypeStruct(small, jnp.float32),
        jax.ShapeDtypeStruct(small, jnp.float32),
        jax.ShapeDtypeStruct(big, jnp.float32),
    ]
    m_a, l_a, n_a = pl.pallas_call(
        pool_kernel,
        grid_spec=pltpu.PrefetchScalarGridSpec(
            num_scalar_prefetch=2,
            grid=(1,),
            in_specs=[full(wide), full(small), pl.BlockSpec(memory_space=pltpu.VMEM)],
            out_specs=[full(small), full(small), full(big)],
            scratch_shapes=scratch,
        ),
        out_shape=state,
        compiler_params=params,
    )(tbl, lens, qwide, snew, pool)

    landed = landed_fn(n_a)
    m_b, l_b, n_b = pl.pallas_call(
        land_kernel,
        grid_spec=pltpu.PrefetchScalarGridSpec(
            num_scalar_prefetch=2,
            grid=(1,),
            in_specs=[full(wide), full(small), full(small), full(big),
                      pl.BlockSpec(memory_space=pltpu.VMEM), pl.BlockSpec(memory_space=pl.ANY)],
            out_specs=[full(small), full(small), full(big)],
            scratch_shapes=scratch,
        ),
        out_shape=state,
        compiler_params=params,
    )(tbl, lens, qwide, m_a, l_a, n_a, landed, pool)
    top = m_b[:, :heads_here, :1]
    e_new = jnp.exp(score_new[:, :, None] - top)
    w_new = e_new.astype(jnp.bfloat16).astype(jnp.float32)
    numer = n_b[:, :heads_here].reshape(req_count, heads_here, heads_here, 2, HEAD_DIM)
    numer = jnp.stack([numer[:, h, h, 1] for h in range(heads_here)], axis=1)
    picked = ((numer + w_new * vf) / (l_b[:, :heads_here, :1] + e_new)).astype(jnp.bfloat16)
    return picked, landed


def migration_plan(pool, mig_src, row_count):
    pool_dev = pool.shape[0]
    land_all = mig_src.shape[0]
    land_dev = land_all // row_count
    src_row = jnp.clip(mig_src // pool_dev, 0, row_count - 1)
    local_page = jnp.clip(mig_src - src_row * pool_dev, 0, pool_dev - 1)
    dst_row = jnp.arange(land_all, dtype=jnp.int32) // land_dev
    onehot = (src_row[:, None] == jnp.arange(row_count, dtype=jnp.int32)[None, :]).astype(jnp.int32)
    csum = jnp.cumsum(onehot.reshape(row_count, land_dev, row_count), axis=1)
    csum = csum.reshape(land_all, row_count)
    rank = jnp.sum(csum * onehot, axis=1) - 1
    return dict(src_row=src_row, local_page=local_page, dst_row=dst_row, rank=rank,
                most=jnp.max(csum), land_dev=land_dev, first=max(1, (land_dev * 5 + 7) // 8))


def gather_kernel(idx_ref, pool_ref, out_ref, sems):
    count = out_ref.shape[0]
    pool_n = pool_ref.shape[0]

    def start(i, carry):
        src = jnp.clip(idx_ref[i], 0, pool_n - 1)
        pltpu.make_async_copy(pool_ref.at[src], out_ref.at[i], sems.at[i]).start()
        return carry

    def wait(i, carry):
        pltpu.make_async_copy(pool_ref.at[0], out_ref.at[i], sems.at[i]).wait()
        return carry

    lax.fori_loop(0, count, start, 0)
    lax.fori_loop(0, count, wait, 0)


def outgoing_pages(pool, plan, row_count, lo, size, tied=()):
    my_row = lax.axis_index("row")
    rank = plan["rank"]
    sel = (plan["src_row"] == my_row) & (rank >= lo) & (rank < lo + size)
    where = jnp.where(sel, plan["dst_row"] * size + (rank - lo), row_count * size)
    idx = jnp.zeros((row_count * size,), jnp.int32).at[where].set(plan["local_page"], mode="drop")
    idx, _ = lax.optimization_barrier((idx, tied))
    count = row_count * size
    pages = pl.pallas_call(
        gather_kernel,
        grid_spec=pltpu.PrefetchScalarGridSpec(
            num_scalar_prefetch=1,
            grid=(1,),
            in_specs=[pl.BlockSpec(memory_space=pl.ANY)],
            out_specs=pl.BlockSpec((count,) + pool.shape[1:], lambda i, *_: (0, 0, 0)),
            scratch_shapes=[pltpu.SemaphoreType.DMA((count,))],
        ),
        out_shape=jax.ShapeDtypeStruct((count,) + pool.shape[1:], pool.dtype),
        compiler_params=pltpu.CompilerParams(vmem_limit_bytes=32 * 1024 * 1024),
    )(idx, pool)
    return pages.reshape(row_count, size, pool.shape[1], pool.shape[2])


def migrate_first(pool, mig_src, row_count, tied):
    plan = migration_plan(pool, mig_src, row_count)
    sent = outgoing_pages(pool, plan, row_count, 0, plan["first"], tied)
    return lax.all_to_all(sent, "row", split_axis=0, concat_axis=0, tiled=True)


def migrate_rest(pool, mig_src, row_count, first_recv, dep):
    plan = migration_plan(pool, mig_src, row_count)
    land_dev, k1 = plan["land_dev"], plan["first"]
    my_row = lax.axis_index("row")
    mine = my_row * land_dev + jnp.arange(land_dev, dtype=jnp.int32)
    src_mine = plan["src_row"][mine]
    rank_mine = plan["rank"][mine]
    pool_dep, _ = lax.optimization_barrier((pool, dep))
    sizes = [0, land_dev - k1] if land_dev > k1 else [0]

    def branch(size):
        def run(pool_b, recv1):
            if size == 0:
                both = recv1
            else:
                sent = outgoing_pages(pool_b, plan, row_count, k1, size)
                recv2 = lax.all_to_all(sent, "row", split_axis=0, concat_axis=0, tiled=True)
                both = jnp.concatenate([recv1, recv2], axis=1)
            width = k1 + size
            flat = both.reshape(row_count * width, both.shape[2], both.shape[3])
            return jnp.take(flat, src_mine * width + jnp.clip(rank_mine, 0, width - 1), axis=0)
        return run

    need = jnp.maximum(plan["most"] - k1, 0)
    index = jnp.sum((jnp.array(sizes, jnp.int32) < need).astype(jnp.int32))
    return lax.switch(index, [branch(b) for b in sizes], pool_dep, first_recv)


def on_device(xn, w_qkv, w_out, pool, page_table, lengths, mig_src, deal):
    heads_here = w_out.shape[0] // HEAD_DIM
    rows_all = xn.shape[0] * lax.axis_size("col")
    row_count = lax.axis_size("row")
    req_row = rows_all // row_count
    inverse = jnp.zeros((rows_all,), jnp.int32).at[deal].set(jnp.arange(rows_all, dtype=jnp.int32))
    gathered = lax.all_gather(xn, "col", axis=0, tiled=True)
    chosen = inverse
    qk_lanes = heads_here * 2 * HEAD_DIM
    half = HEAD_DIM // 2
    freqs = theta_base ** (-(jnp.arange(half, dtype=jnp.float32) * 2.0 / HEAD_DIM))
    angles = lengths.astype(jnp.float32)[:, None] * freqs[None, :]
    cosine = jnp.tile(jnp.cos(angles), (1, qk_lanes // half))
    sine = jnp.tile(jnp.sin(angles), (1, qk_lanes // half))
    heads3 = w_qkv.reshape(w_qkv.shape[0], heads_here, 3, HEAD_DIM)
    w_perm = jnp.concatenate(
        [heads3[:, :, :2].reshape(w_qkv.shape[0], -1), heads3[:, :, 2].reshape(w_qkv.shape[0], -1)],
        axis=1)
    partial = jnp.dot(jnp.take(gathered, chosen, axis=0), w_perm,
                      preferred_element_type=jnp.float32).astype(jnp.bfloat16)
    parts = lax.all_to_all(partial, "row", split_axis=0, concat_axis=0, tiled=True)
    projected = jnp.sum(parts.reshape(row_count, req_row, -1).astype(jnp.float32), axis=0)
    qk_lanes = heads_here * 2 * HEAD_DIM
    x = projected[:, :qk_lanes]
    lane = jnp.arange(qk_lanes, dtype=jnp.int32)
    within = lane % HEAD_DIM
    half = HEAD_DIM // 2
    ahead = jnp.roll(x, -half, axis=1)
    behind = jnp.roll(x, half, axis=1)
    rotated = jnp.where((within < half)[None, :], x * cosine - ahead * sine,
                        x * cosine + behind * sine)
    qk = rotated.astype(jnp.bfloat16)
    value_new = projected[:, qk_lanes:].astype(jnp.bfloat16)
    first = migrate_first(pool, mig_src, row_count, (cosine, sine))
    mixed, landed = attend(qk, value_new, page_table, lengths, pool,
                           lambda dep: migrate_rest(pool, mig_src, row_count, first, dep))
    mixed = mixed.reshape(req_row, heads_here * HEAD_DIM)
    mixed_all = lax.all_gather(mixed, "row", axis=0, tiled=True)
    chosen = deal
    col_count = lax.axis_size("col")
    partial = jnp.dot(
        jnp.take(mixed_all, chosen, axis=0), w_out, preferred_element_type=jnp.float32
    ).astype(jnp.bfloat16)
    parts = lax.all_to_all(partial, "col", split_axis=0, concat_axis=0, tiled=True)
    attended = jnp.sum(
        parts.reshape(col_count, rows_all // col_count, -1).astype(jnp.float32), axis=0
    ).astype(jnp.bfloat16)
    return (attended, landed)


def solution(mesh):
    placed = (
        P("col", "row"),
        P("row", "col"),
        P("col", "row"),
        P("row", None, "col"),
        P("row", None),
        P("row"),
        P(),
        P(),
    )
    return jax.shard_map(
        on_device,
        mesh=mesh,
        in_specs=placed,
        out_specs=(P("col", "row"), P("row", None, "col")),
        check_vma=False,
    )
```

```python
import functools

import jax
import jax.numpy as jnp
from jax import lax
from jax.experimental import pallas as pl
from jax.experimental.pallas import tpu as pltpu
from jax.sharding import PartitionSpec as P

HEAD_DIM = 64
PAGE = 64


theta_base = 130000.0
neg_large = -1e30


def rotate(values, positions):
    half = values.shape[-1] // 2
    freqs = theta_base ** (-(jnp.arange(half, dtype=jnp.float32) * 2.0 / values.shape[-1]))
    angles = positions.astype(jnp.float32)[:, None, None] * freqs[None, None, :]
    cosine = jnp.cos(angles)
    sine = jnp.sin(angles)
    first = values[..., :half]
    second = values[..., half:]
    return jnp.concatenate(
        [first * cosine - second * sine, second * cosine + first * sine], axis=-1
    )


def page_scores(page_of, flat, scores, qrow, start, count, length, maxp):
    rows = qrow.shape[0]
    pos = lax.broadcasted_iota(jnp.int32, (rows, PAGE), 1)

    def one(k):
        j = flat[start + k] % maxp
        s = lax.dot_general(
            qrow, page_of(start + k), (((1,), (1,)), ((), ())),
            preferred_element_type=jnp.float32,
        ) * 0.125
        s = jnp.where(j * PAGE + pos < length, s, neg_large)
        scores[k] = s
        return s

    def two(k2, top):
        s0 = one(2 * k2)
        s1 = one(2 * k2 + 1)
        return jnp.maximum(top, jnp.maximum(s0, s1))

    top = lax.fori_loop(0, count // 2, two, jnp.full((rows, PAGE), neg_large, jnp.float32))
    top = lax.fori_loop(count // 2 * 2, count, lambda k, t: jnp.maximum(t, one(k)), top)
    return jnp.max(top, axis=1, keepdims=True)


def page_values(page_of, flat, scores, top, start, count, length, maxp, lanes):
    rows = top.shape[0]
    pos = lax.broadcasted_iota(jnp.int32, (rows, PAGE), 1)

    def one(k):
        j = flat[start + k] % maxp
        e = jnp.where(j * PAGE + pos < length, jnp.exp(scores[k] - top), 0.0)
        w = e.astype(jnp.bfloat16)
        return e, jnp.dot(w, page_of(start + k), preferred_element_type=jnp.float32)

    def two(k2, carry):
        total, numer = carry
        e0, n0 = one(2 * k2)
        e1, n1 = one(2 * k2 + 1)
        return total + (e0 + e1), numer + (n0 + n1)

    def single(k, carry):
        total, numer = carry
        e0, n0 = one(k)
        return total + e0, numer + n0

    init = (jnp.zeros((rows, PAGE), jnp.float32), jnp.zeros((rows, lanes), jnp.float32))
    carry = lax.fori_loop(0, count // 2, two, init)
    total, numer = lax.fori_loop(count // 2 * 2, count, single, carry)
    return jnp.sum(total, axis=1, keepdims=True), numer


def build_list(tbl, lens, pool_n, maxp, reqs, flat, starts, listed, landing):
    def req(r, carry):
        n, nl = carry
        starts[r] = n
        count = (lens[r] + PAGE - 1) // PAGE

        def page(j, n):
            e = r * maxp + j
            flat[n] = e
            keep = (tbl[e] >= pool_n) if landing else (tbl[e] < pool_n)
            return n + keep.astype(jnp.int32)

        n2 = lax.fori_loop(0, count, page, n)
        listed[nl] = r
        return n2, nl + (n2 > n).astype(jnp.int32)

    n, nl = lax.fori_loop(0, reqs, req, (0, 0))
    starts[reqs] = n
    return n, nl


def query_rows(qwide_ref, r, rows):
    lanes = qwide_ref.shape[2]
    wide = jnp.broadcast_to(qwide_ref[r], (rows, lanes))
    head = lax.broadcasted_iota(jnp.int32, (rows, lanes), 0)
    lane = lax.broadcasted_iota(jnp.int32, (rows, lanes), 1)
    return jnp.where(head == lane // 128, wide, 0.0).astype(jnp.bfloat16)


def pool_kernel(tbl, lens, qrow_ref, snew_ref, pool_ref,
                m_ref, l_ref, n_ref, scores, flat, starts, listed):
    reqs, rows, lanes = snew_ref.shape[0], snew_ref.shape[1], pool_ref.shape[2]
    maxp = scores.shape[0]
    pool_n = pool_ref.shape[0]
    build_list(tbl, lens, pool_n, maxp, reqs, flat, starts, listed, False)
    page_of = lambda f: pool_ref[jnp.clip(tbl[flat[f]], 0, pool_n - 1)]

    def request(r, carry):
        start = starts[r]
        count = starts[r + 1] - start
        length = lens[r]
        snew = snew_ref[r][:, :1]
        top = page_scores(page_of, flat, scores, query_rows(qrow_ref, r, rows), start, count,
                          length, maxp)
        top = jnp.maximum(top, snew)
        total, numer = page_values(page_of, flat, scores, top, start, count, length, maxp,
                                   lanes)
        m_ref[r] = jnp.broadcast_to(top, (rows, 128))
        l_ref[r] = jnp.broadcast_to(total, (rows, 128))
        n_ref[r] = numer
        return carry

    lax.fori_loop(0, reqs, request, 0)


def land_kernel(tbl, lens, qrow_ref, m_in, l_in, n_in, land_ref, pool_n_ref,
                m_ref, l_ref, n_ref, scores, flat, starts, listed, mbuf, lbuf, nbuf, sems):
    reqs, rows, lanes = m_in.shape[0], m_in.shape[1], land_ref.shape[2]
    maxp = scores.shape[0]
    pool_n = pool_n_ref.shape[0]
    land_n = land_ref.shape[0]
    _, listed_n = build_list(tbl, lens, pool_n, maxp, reqs, flat, starts, listed, True)
    page_of = lambda f: land_ref[jnp.clip(tbl[flat[f]] - pool_n, 0, land_n - 1)]
    pairs = ((m_in, m_ref, mbuf), (l_in, l_ref, lbuf), (n_in, n_ref, nbuf))

    def request(k, carry):
        r = listed[k]
        reads = [pltpu.make_async_copy(src.at[pl.ds(r, 1)], buf, sems.at[i])
                 for i, (src, _, buf) in enumerate(pairs)]
        for c in reads:
            c.start()
        for c in reads:
            c.wait()
        start = starts[r]
        count = starts[r + 1] - start
        length = lens[r]
        top_a = mbuf[0][:, :1]
        top_b = page_scores(page_of, flat, scores, query_rows(qrow_ref, r, rows), start, count,
                            length, maxp)
        top = jnp.maximum(top_a, top_b)
        total, numer = page_values(page_of, flat, scores, top, start, count, length, maxp,
                                   lanes)
        scale = jnp.exp(top_a - top)
        l_new = total + lbuf[0][:, :1] * scale
        n_new = numer + nbuf[0] * scale
        mbuf[0] = jnp.broadcast_to(top, (rows, 128))
        lbuf[0] = jnp.broadcast_to(l_new, (rows, 128))
        nbuf[0] = n_new
        writes = [pltpu.make_async_copy(buf, dst.at[pl.ds(r, 1)], sems.at[i])
                  for i, (_, dst, buf) in enumerate(pairs)]
        for c in writes:
            c.start()
        for c in writes:
            c.wait()
        return carry

    lax.fori_loop(0, listed_n, request, 0)


def attend(qk, value_new, table, lens, pool, landed_fn):
    req_count = qk.shape[0]
    lanes = pool.shape[2]
    heads_here = lanes // (2 * HEAD_DIM)
    maxp = table.shape[1]
    pool_n = pool.shape[0]
    rows = 8
    lane = jnp.arange(lanes, dtype=jnp.int32)
    qwide = jnp.where((lane % 128 < HEAD_DIM)[None, :], qk.astype(jnp.float32), 0.0)
    qwide = qwide.reshape(req_count, 1, lanes)
    grouped = qk.astype(jnp.float32).reshape(req_count, heads_here, 2 * HEAD_DIM)
    score_new = jnp.sum(grouped[..., :HEAD_DIM] * grouped[..., HEAD_DIM:], axis=-1) * 0.125
    vf = value_new.astype(jnp.float32).reshape(req_count, heads_here, HEAD_DIM)
    snew = jnp.zeros((req_count, rows, 128), jnp.float32) + jnp.pad(
        score_new, ((0, 0), (0, rows - heads_here)))[:, :, None]
    tbl = table.reshape(-1)

    full = lambda shape: pl.BlockSpec(shape, lambda i, *_: (0,) * len(shape))
    big = (req_count, rows, lanes)
    small = (req_count, rows, 128)
    wide = (req_count, 1, lanes)
    scratch = [
        pltpu.VMEM((maxp, rows, PAGE), jnp.float32),
        pltpu.SMEM((req_count * maxp,), jnp.int32),
        pltpu.SMEM((req_count + 1,), jnp.int32),
        pltpu.SMEM((req_count,), jnp.int32),
    ]
    params = pltpu.CompilerParams(
        dimension_semantics=("arbitrary",), vmem_limit_bytes=60 * 1024 * 1024)
    state = [
        jax.ShapeDtypeStruct(small, jnp.float32),
        jax.ShapeDtypeStruct(small, jnp.float32),
        jax.ShapeDtypeStruct(big, jnp.float32),
    ]
    m_a, l_a, n_a = pl.pallas_call(
        pool_kernel,
        grid_spec=pltpu.PrefetchScalarGridSpec(
            num_scalar_prefetch=2,
            grid=(1,),
            in_specs=[full(wide), full(small), pl.BlockSpec(memory_space=pltpu.VMEM)],
            out_specs=[full(small), full(small), full(big)],
            scratch_shapes=scratch,
        ),
        out_shape=state,
        compiler_params=params,
    )(tbl, lens, qwide, snew, pool)

    landed = landed_fn(n_a)
    any_spec = pl.BlockSpec(memory_space=pl.ANY)
    m_b, l_b, n_b = pl.pallas_call(
        land_kernel,
        grid_spec=pltpu.PrefetchScalarGridSpec(
            num_scalar_prefetch=2,
            grid=(1,),
            in_specs=[full(wide), any_spec, any_spec, any_spec,
                      pl.BlockSpec(memory_space=pltpu.VMEM), any_spec],
            out_specs=[any_spec, any_spec, any_spec],
            scratch_shapes=scratch + [
                pltpu.VMEM((1, rows, 128), jnp.float32),
                pltpu.VMEM((1, rows, 128), jnp.float32),
                pltpu.VMEM((1, rows, lanes), jnp.float32),
                pltpu.SemaphoreType.DMA((3,)),
            ],
        ),
        out_shape=state,
        input_output_aliases={3: 0, 4: 1, 5: 2},
        compiler_params=params,
    )(tbl, lens, qwide, m_a, l_a, n_a, landed, pool)
    top = m_b[:, :heads_here, :1]
    e_new = jnp.exp(score_new[:, :, None] - top)
    w_new = e_new.astype(jnp.bfloat16).astype(jnp.float32)
    numer = n_b[:, :heads_here].reshape(req_count, heads_here, heads_here, 2, HEAD_DIM)
    numer = jnp.stack([numer[:, h, h, 1] for h in range(heads_here)], axis=1)
    picked = ((numer + w_new * vf) / (l_b[:, :heads_here, :1] + e_new)).astype(jnp.bfloat16)
    return picked, landed


def migration_plan(pool, mig_src, row_count):
    pool_dev = pool.shape[0]
    land_all = mig_src.shape[0]
    land_dev = land_all // row_count
    src_row = jnp.clip(mig_src // pool_dev, 0, row_count - 1)
    local_page = jnp.clip(mig_src - src_row * pool_dev, 0, pool_dev - 1)
    dst_row = jnp.arange(land_all, dtype=jnp.int32) // land_dev
    onehot = (src_row[:, None] == jnp.arange(row_count, dtype=jnp.int32)[None, :]).astype(jnp.int32)
    csum = jnp.cumsum(onehot.reshape(row_count, land_dev, row_count), axis=1)
    csum = csum.reshape(land_all, row_count)
    rank = jnp.sum(csum * onehot, axis=1) - 1
    return dict(src_row=src_row, local_page=local_page, dst_row=dst_row, rank=rank,
                most=jnp.max(csum), land_dev=land_dev, first=max(1, (land_dev * 5 + 7) // 8))


def gather_kernel(idx_ref, pool_ref, out_ref, sems):
    count = out_ref.shape[0]
    pool_n = pool_ref.shape[0]

    def start(i, carry):
        src = jnp.clip(idx_ref[i], 0, pool_n - 1)
        pltpu.make_async_copy(pool_ref.at[src], out_ref.at[i], sems.at[i]).start()
        return carry

    def wait(i, carry):
        pltpu.make_async_copy(pool_ref.at[0], out_ref.at[i], sems.at[i]).wait()
        return carry

    lax.fori_loop(0, count, start, 0)
    lax.fori_loop(0, count, wait, 0)


def outgoing_pages(pool, plan, row_count, lo, size):
    my_row = lax.axis_index("row")
    rank = plan["rank"]
    sel = (plan["src_row"] == my_row) & (rank >= lo) & (rank < lo + size)
    where = jnp.where(sel, plan["dst_row"] * size + (rank - lo), row_count * size)
    idx = jnp.zeros((row_count * size,), jnp.int32).at[where].set(plan["local_page"], mode="drop")
    count = row_count * size
    pages = pl.pallas_call(
        gather_kernel,
        grid_spec=pltpu.PrefetchScalarGridSpec(
            num_scalar_prefetch=1,
            grid=(1,),
            in_specs=[pl.BlockSpec(memory_space=pl.ANY)],
            out_specs=pl.BlockSpec((count,) + pool.shape[1:], lambda i, *_: (0, 0, 0)),
            scratch_shapes=[pltpu.SemaphoreType.DMA((count,))],
        ),
        out_shape=jax.ShapeDtypeStruct((count,) + pool.shape[1:], pool.dtype),
        compiler_params=pltpu.CompilerParams(vmem_limit_bytes=32 * 1024 * 1024),
    )(idx, pool)
    return pages.reshape(row_count, size, pool.shape[1], pool.shape[2])


def migrate_first(pool, mig_src, row_count):
    plan = migration_plan(pool, mig_src, row_count)
    sent = outgoing_pages(pool, plan, row_count, 0, plan["first"])
    return lax.all_to_all(sent, "row", split_axis=0, concat_axis=0, tiled=True)


def migrate_rest(pool, mig_src, row_count, first_recv, dep):
    plan = migration_plan(pool, mig_src, row_count)
    land_dev, k1 = plan["land_dev"], plan["first"]
    my_row = lax.axis_index("row")
    mine = my_row * land_dev + jnp.arange(land_dev, dtype=jnp.int32)
    src_mine = plan["src_row"][mine]
    rank_mine = plan["rank"][mine]
    pool_dep, _ = lax.optimization_barrier((pool, dep))
    sizes = [0, land_dev - k1] if land_dev > k1 else [0]

    def branch(size):
        def run(pool_b, recv1):
            if size == 0:
                both = recv1
            else:
                sent = outgoing_pages(pool_b, plan, row_count, k1, size)
                recv2 = lax.all_to_all(sent, "row", split_axis=0, concat_axis=0, tiled=True)
                both = jnp.concatenate([recv1, recv2], axis=1)
            width = k1 + size
            flat = both.reshape(row_count * width, both.shape[2], both.shape[3])
            return jnp.take(flat, src_mine * width + jnp.clip(rank_mine, 0, width - 1), axis=0)
        return run

    need = jnp.maximum(plan["most"] - k1, 0)
    index = jnp.sum((jnp.array(sizes, jnp.int32) < need).astype(jnp.int32))
    return lax.switch(index, [branch(b) for b in sizes], pool_dep, first_recv)


def on_device(xn, w_qkv, w_out, pool, page_table, lengths, mig_src, deal):
    heads_here = w_out.shape[0] // HEAD_DIM
    rows_all = xn.shape[0] * lax.axis_size("col")
    row_count = lax.axis_size("row")
    req_row = rows_all // row_count
    inverse = jnp.zeros((rows_all,), jnp.int32).at[deal].set(jnp.arange(rows_all, dtype=jnp.int32))
    gathered = lax.all_gather(xn, "col", axis=0, tiled=True)
    chosen = inverse
    heads3 = w_qkv.reshape(w_qkv.shape[0], heads_here, 3, HEAD_DIM)
    w_perm = jnp.concatenate(
        [heads3[:, :, :2].reshape(w_qkv.shape[0], -1), heads3[:, :, 2].reshape(w_qkv.shape[0], -1)],
        axis=1)
    partial = jnp.dot(jnp.take(gathered, chosen, axis=0), w_perm,
                      preferred_element_type=jnp.float32).astype(jnp.bfloat16)
    parts = lax.all_to_all(partial, "row", split_axis=0, concat_axis=0, tiled=True)
    projected = jnp.sum(parts.reshape(row_count, req_row, -1).astype(jnp.float32), axis=0)
    qk_lanes = heads_here * 2 * HEAD_DIM
    x = projected[:, :qk_lanes]
    lane = jnp.arange(qk_lanes, dtype=jnp.int32)
    within = lane % HEAD_DIM
    half = HEAD_DIM // 2
    freqs = theta_base ** (-(jnp.arange(half, dtype=jnp.float32) * 2.0 / HEAD_DIM))
    angles = lengths.astype(jnp.float32)[:, None] * freqs[None, :]
    cosine = jnp.tile(jnp.cos(angles), (1, qk_lanes // half))
    sine = jnp.tile(jnp.sin(angles), (1, qk_lanes // half))
    ahead = jnp.roll(x, -half, axis=1)
    behind = jnp.roll(x, half, axis=1)
    rotated = jnp.where((within < half)[None, :], x * cosine - ahead * sine,
                        x * cosine + behind * sine)
    qk = rotated.astype(jnp.bfloat16)
    value_new = projected[:, qk_lanes:].astype(jnp.bfloat16)
    first = migrate_first(pool, mig_src, row_count)
    mixed, landed = attend(qk, value_new, page_table, lengths, pool,
                           lambda dep: migrate_rest(pool, mig_src, row_count, first, dep))
    mixed = mixed.reshape(req_row, heads_here * HEAD_DIM)
    mixed_all = lax.all_gather(mixed, "row", axis=0, tiled=True)
    chosen = deal
    col_count = lax.axis_size("col")
    partial = jnp.dot(
        jnp.take(mixed_all, chosen, axis=0), w_out, preferred_element_type=jnp.float32
    ).astype(jnp.bfloat16)
    parts = lax.all_to_all(partial, "col", split_axis=0, concat_axis=0, tiled=True)
    attended = jnp.sum(
        parts.reshape(col_count, rows_all // col_count, -1).astype(jnp.float32), axis=0
    ).astype(jnp.bfloat16)
    return (attended, landed)


def solution(mesh):
    placed = (
        P("col", "row"),
        P("row", "col"),
        P("col", "row"),
        P("row", None, "col"),
        P("row", None),
        P("row"),
        P(),
        P(),
    )
    return jax.shard_map(
        on_device,
        mesh=mesh,
        in_specs=placed,
        out_specs=(P("col", "row"), P("row", None, "col")),
        check_vma=False,
    )
```

```python
import functools

import jax
import jax.numpy as jnp
from jax import lax
from jax.experimental import pallas as pl
from jax.experimental.pallas import tpu as pltpu
from jax.sharding import PartitionSpec as P

HEAD_DIM = 64
PAGE = 64


theta_base = 130000.0
neg_large = -1e30


def rotate(values, positions):
    half = values.shape[-1] // 2
    freqs = theta_base ** (-(jnp.arange(half, dtype=jnp.float32) * 2.0 / values.shape[-1]))
    angles = positions.astype(jnp.float32)[:, None, None] * freqs[None, None, :]
    cosine = jnp.cos(angles)
    sine = jnp.sin(angles)
    first = values[..., :half]
    second = values[..., half:]
    return jnp.concatenate(
        [first * cosine - second * sine, second * cosine + first * sine], axis=-1
    )


def page_scores(page_of, flat, scores, qrow, start, count, length, maxp):
    rows = qrow.shape[0]
    pos = lax.broadcasted_iota(jnp.int32, (rows, PAGE), 1)

    def one(k):
        j = flat[start + k] % maxp
        s = lax.dot_general(
            qrow, page_of(start + k), (((1,), (1,)), ((), ())),
            preferred_element_type=jnp.float32,
        ) * 0.125
        s = jnp.where(j * PAGE + pos < length, s, neg_large)
        scores[k] = s
        return s

    def two(k2, top):
        s0 = one(2 * k2)
        s1 = one(2 * k2 + 1)
        return jnp.maximum(top, jnp.maximum(s0, s1))

    top = lax.fori_loop(0, count // 2, two, jnp.full((rows, PAGE), neg_large, jnp.float32))
    top = lax.fori_loop(count // 2 * 2, count, lambda k, t: jnp.maximum(t, one(k)), top)
    return jnp.max(top, axis=1, keepdims=True)


def page_values(page_of, flat, scores, top, start, count, length, maxp, lanes):
    rows = top.shape[0]
    pos = lax.broadcasted_iota(jnp.int32, (rows, PAGE), 1)

    def one(k):
        j = flat[start + k] % maxp
        e = jnp.where(j * PAGE + pos < length, jnp.exp(scores[k] - top), 0.0)
        w = e.astype(jnp.bfloat16)
        return e, jnp.dot(w, page_of(start + k), preferred_element_type=jnp.float32)

    def two(k2, carry):
        total, numer = carry
        e0, n0 = one(2 * k2)
        e1, n1 = one(2 * k2 + 1)
        return total + (e0 + e1), numer + (n0 + n1)

    def single(k, carry):
        total, numer = carry
        e0, n0 = one(k)
        return total + e0, numer + n0

    init = (jnp.zeros((rows, PAGE), jnp.float32), jnp.zeros((rows, lanes), jnp.float32))
    carry = lax.fori_loop(0, count // 2, two, init)
    total, numer = lax.fori_loop(count // 2 * 2, count, single, carry)
    return jnp.sum(total, axis=1, keepdims=True), numer


def build_list(tbl, lens, pool_n, maxp, reqs, flat, starts, listed, landing):
    def req(r, carry):
        n, nl = carry
        starts[r] = n
        count = (lens[r] + PAGE - 1) // PAGE

        def page(j, n):
            e = r * maxp + j
            flat[n] = e
            keep = (tbl[e] >= pool_n) if landing else (tbl[e] < pool_n)
            return n + keep.astype(jnp.int32)

        n2 = lax.fori_loop(0, count, page, n)
        listed[nl] = r
        return n2, nl + (n2 > n).astype(jnp.int32)

    n, nl = lax.fori_loop(0, reqs, req, (0, 0))
    starts[reqs] = n
    return n, nl


def query_rows(qwide_ref, r, rows):
    lanes = qwide_ref.shape[2]
    wide = jnp.broadcast_to(qwide_ref[r], (rows, lanes))
    head = lax.broadcasted_iota(jnp.int32, (rows, lanes), 0)
    lane = lax.broadcasted_iota(jnp.int32, (rows, lanes), 1)
    return jnp.where(head == lane // 128, wide, 0.0).astype(jnp.bfloat16)


def pool_kernel(tbl, lens, qrow_ref, snew_ref, pool_ref,
                m_ref, l_ref, n_ref, scores, flat, starts, listed):
    reqs, rows, lanes = snew_ref.shape[0], snew_ref.shape[1], pool_ref.shape[2]
    maxp = scores.shape[0]
    pool_n = pool_ref.shape[0]
    build_list(tbl, lens, pool_n, maxp, reqs, flat, starts, listed, False)
    page_of = lambda f: pool_ref[jnp.clip(tbl[flat[f]], 0, pool_n - 1)]

    def request(r, carry):
        start = starts[r]
        count = starts[r + 1] - start
        length = lens[r]
        snew = snew_ref[r][:, :1]
        top = page_scores(page_of, flat, scores, query_rows(qrow_ref, r, rows), start, count,
                          length, maxp)
        top = jnp.maximum(top, snew)
        total, numer = page_values(page_of, flat, scores, top, start, count, length, maxp,
                                   lanes)
        m_ref[r] = jnp.broadcast_to(top, (rows, 128))
        l_ref[r] = jnp.broadcast_to(total, (rows, 128))
        n_ref[r] = numer
        return carry

    lax.fori_loop(0, reqs, request, 0)


def land_kernel(tbl, lens, qrow_ref, m_in, l_in, n_in, land_ref, pool_n_ref,
                m_ref, l_ref, n_ref, scores, flat, starts, listed):
    reqs, rows, lanes = m_in.shape[0], m_in.shape[1], land_ref.shape[2]
    maxp = scores.shape[0]
    pool_n = pool_n_ref.shape[0]
    land_n = land_ref.shape[0]
    _, listed_n = build_list(tbl, lens, pool_n, maxp, reqs, flat, starts, listed, True)
    m_ref[...] = m_in[...]
    l_ref[...] = l_in[...]
    n_ref[...] = n_in[...]
    page_of = lambda f: land_ref[jnp.clip(tbl[flat[f]] - pool_n, 0, land_n - 1)]

    def request(k, carry):
        r = listed[k]
        start = starts[r]
        count = starts[r + 1] - start
        length = lens[r]
        top_a = m_in[r][:, :1]
        top_b = page_scores(page_of, flat, scores, query_rows(qrow_ref, r, rows), start, count,
                            length, maxp)
        top = jnp.maximum(top_a, top_b)
        total, numer = page_values(page_of, flat, scores, top, start, count, length, maxp,
                                   lanes)
        scale = jnp.exp(top_a - top)
        m_ref[r] = jnp.broadcast_to(top, (rows, 128))
        l_ref[r] = jnp.broadcast_to(total + l_in[r][:, :1] * scale, (rows, 128))
        n_ref[r] = numer + n_in[r] * scale
        return carry

    lax.fori_loop(0, listed_n, request, 0)


def attend(qk, value_new, table, lens, pool, landed_fn):
    req_count = qk.shape[0]
    lanes = pool.shape[2]
    heads_here = lanes // (2 * HEAD_DIM)
    maxp = table.shape[1]
    pool_n = pool.shape[0]
    rows = 8
    lane = jnp.arange(lanes, dtype=jnp.int32)
    qwide = jnp.where((lane % 128 < HEAD_DIM)[None, :], qk.astype(jnp.float32), 0.0)
    qwide = qwide.reshape(req_count, 1, lanes)
    grouped = qk.astype(jnp.float32).reshape(req_count, heads_here, 2 * HEAD_DIM)
    score_new = jnp.sum(grouped[..., :HEAD_DIM] * grouped[..., HEAD_DIM:], axis=-1) * 0.125
    vf = value_new.astype(jnp.float32).reshape(req_count, heads_here, HEAD_DIM)
    snew = jnp.zeros((req_count, rows, 128), jnp.float32) + jnp.pad(
        score_new, ((0, 0), (0, rows - heads_here)))[:, :, None]
    tbl = table.reshape(-1)

    full = lambda shape: pl.BlockSpec(shape, lambda i, *_: (0,) * len(shape))
    big = (req_count, rows, lanes)
    small = (req_count, rows, 128)
    wide = (req_count, 1, lanes)
    scratch = [
        pltpu.VMEM((maxp, rows, PAGE), jnp.float32),
        pltpu.SMEM((req_count * maxp,), jnp.int32),
        pltpu.SMEM((req_count + 1,), jnp.int32),
        pltpu.SMEM((req_count,), jnp.int32),
    ]
    params = pltpu.CompilerParams(
        dimension_semantics=("arbitrary",), vmem_limit_bytes=60 * 1024 * 1024)
    state = [
        jax.ShapeDtypeStruct(small, jnp.float32),
        jax.ShapeDtypeStruct(small, jnp.float32),
        jax.ShapeDtypeStruct(big, jnp.float32),
    ]
    m_a, l_a, n_a = pl.pallas_call(
        pool_kernel,
        grid_spec=pltpu.PrefetchScalarGridSpec(
            num_scalar_prefetch=2,
            grid=(1,),
            in_specs=[full(wide), full(small), pl.BlockSpec(memory_space=pltpu.VMEM)],
            out_specs=[full(small), full(small), full(big)],
            scratch_shapes=scratch,
        ),
        out_shape=state,
        compiler_params=params,
    )(tbl, lens, qwide, snew, pool)

    landed = landed_fn(n_a)
    m_b, l_b, n_b = pl.pallas_call(
        land_kernel,
        grid_spec=pltpu.PrefetchScalarGridSpec(
            num_scalar_prefetch=2,
            grid=(1,),
            in_specs=[full(wide), full(small), full(small), full(big),
                      pl.BlockSpec(memory_space=pltpu.VMEM), pl.BlockSpec(memory_space=pl.ANY)],
            out_specs=[full(small), full(small), full(big)],
            scratch_shapes=scratch,
        ),
        out_shape=state,
        compiler_params=params,
    )(tbl, lens, qwide, m_a, l_a, n_a, landed, pool)
    top = m_b[:, :heads_here, :1]
    e_new = jnp.exp(score_new[:, :, None] - top)
    w_new = e_new.astype(jnp.bfloat16).astype(jnp.float32)
    numer = n_b[:, :heads_here].reshape(req_count, heads_here, heads_here, 2, HEAD_DIM)
    numer = jnp.stack([numer[:, h, h, 1] for h in range(heads_here)], axis=1)
    picked = ((numer + w_new * vf) / (l_b[:, :heads_here, :1] + e_new)).astype(jnp.bfloat16)
    return picked, landed


def migration_plan(pool, mig_src, row_count):
    pool_dev = pool.shape[0]
    land_all = mig_src.shape[0]
    land_dev = land_all // row_count
    src_row = jnp.clip(mig_src // pool_dev, 0, row_count - 1)
    local_page = jnp.clip(mig_src - src_row * pool_dev, 0, pool_dev - 1)
    dst_row = jnp.arange(land_all, dtype=jnp.int32) // land_dev
    onehot = (src_row[:, None] == jnp.arange(row_count, dtype=jnp.int32)[None, :]).astype(jnp.int32)
    csum = jnp.cumsum(onehot.reshape(row_count, land_dev, row_count), axis=1)
    csum = csum.reshape(land_all, row_count)
    rank = jnp.sum(csum * onehot, axis=1) - 1
    return dict(src_row=src_row, local_page=local_page, dst_row=dst_row, rank=rank,
                most=jnp.max(csum), land_dev=land_dev, first=max(1, (land_dev * 5 + 7) // 8))


def gather_kernel(idx_ref, pool_ref, out_ref, sems):
    count = out_ref.shape[0]
    pool_n = pool_ref.shape[0]

    def start(i, carry):
        src = jnp.clip(idx_ref[i], 0, pool_n - 1)
        pltpu.make_async_copy(pool_ref.at[src], out_ref.at[i], sems.at[i]).start()
        return carry

    def wait(i, carry):
        pltpu.make_async_copy(pool_ref.at[0], out_ref.at[i], sems.at[i]).wait()
        return carry

    lax.fori_loop(0, count, start, 0)
    lax.fori_loop(0, count, wait, 0)


def outgoing_pages(pool, plan, row_count, lo, size):
    my_row = lax.axis_index("row")
    rank = plan["rank"]
    sel = (plan["src_row"] == my_row) & (rank >= lo) & (rank < lo + size)
    where = jnp.where(sel, plan["dst_row"] * size + (rank - lo), row_count * size)
    idx = jnp.zeros((row_count * size,), jnp.int32).at[where].set(plan["local_page"], mode="drop")
    count = row_count * size
    pages = pl.pallas_call(
        gather_kernel,
        grid_spec=pltpu.PrefetchScalarGridSpec(
            num_scalar_prefetch=1,
            grid=(1,),
            in_specs=[pl.BlockSpec(memory_space=pl.ANY)],
            out_specs=pl.BlockSpec((count,) + pool.shape[1:], lambda i, *_: (0, 0, 0)),
            scratch_shapes=[pltpu.SemaphoreType.DMA((count,))],
        ),
        out_shape=jax.ShapeDtypeStruct((count,) + pool.shape[1:], pool.dtype),
        compiler_params=pltpu.CompilerParams(vmem_limit_bytes=32 * 1024 * 1024),
    )(idx, pool)
    return pages.reshape(row_count, size, pool.shape[1], pool.shape[2])


def migrate_first(pool, mig_src, row_count):
    plan = migration_plan(pool, mig_src, row_count)
    sent = outgoing_pages(pool, plan, row_count, 0, plan["first"])
    return lax.all_to_all(sent, "row", split_axis=0, concat_axis=0, tiled=True)


def migrate_rest(pool, mig_src, row_count, first_recv, dep):
    plan = migration_plan(pool, mig_src, row_count)
    land_dev, k1 = plan["land_dev"], plan["first"]
    my_row = lax.axis_index("row")
    mine = my_row * land_dev + jnp.arange(land_dev, dtype=jnp.int32)
    src_mine = plan["src_row"][mine]
    rank_mine = plan["rank"][mine]
    pool_dep, _ = lax.optimization_barrier((pool, dep))
    sizes = [0, land_dev - k1] if land_dev > k1 else [0]

    def branch(size):
        def run(pool_b, recv1):
            if size == 0:
                both = recv1
            else:
                sent = outgoing_pages(pool_b, plan, row_count, k1, size)
                recv2 = lax.all_to_all(sent, "row", split_axis=0, concat_axis=0, tiled=True)
                both = jnp.concatenate([recv1, recv2], axis=1)
            width = k1 + size
            flat = both.reshape(row_count * width, both.shape[2], both.shape[3])
            return jnp.take(flat, src_mine * width + jnp.clip(rank_mine, 0, width - 1), axis=0)
        return run

    need = jnp.maximum(plan["most"] - k1, 0)
    index = jnp.sum((jnp.array(sizes, jnp.int32) < need).astype(jnp.int32))
    return lax.switch(index, [branch(b) for b in sizes], pool_dep, first_recv)


def on_device(xn, w_qkv, w_out, pool, page_table, lengths, mig_src, deal):
    heads_here = w_out.shape[0] // HEAD_DIM
    rows_all = xn.shape[0] * lax.axis_size("col")
    row_count = lax.axis_size("row")
    req_row = rows_all // row_count
    inverse = jnp.zeros((rows_all,), jnp.int32).at[deal].set(jnp.arange(rows_all, dtype=jnp.int32))
    gathered = lax.all_gather(xn, "col", axis=0, tiled=True)
    chosen = inverse
    heads3 = w_qkv.reshape(w_qkv.shape[0], heads_here, 3, HEAD_DIM)
    w_perm = jnp.concatenate(
        [heads3[:, :, :2].reshape(w_qkv.shape[0], -1), heads3[:, :, 2].reshape(w_qkv.shape[0], -1)],
        axis=1)
    partial = jnp.dot(jnp.take(gathered, chosen, axis=0), w_perm,
                      preferred_element_type=jnp.float32).astype(jnp.bfloat16)
    parts = lax.all_to_all(partial, "row", split_axis=0, concat_axis=0, tiled=True)
    projected = jnp.sum(parts.reshape(row_count, req_row, -1).astype(jnp.float32), axis=0)
    qk_lanes = heads_here * 2 * HEAD_DIM
    x = projected[:, :qk_lanes]
    lane = jnp.arange(qk_lanes, dtype=jnp.int32)
    within = lane % HEAD_DIM
    half = HEAD_DIM // 2
    freqs = theta_base ** (-(jnp.arange(half, dtype=jnp.float32) * 2.0 / HEAD_DIM))
    angles = lengths.astype(jnp.float32)[:, None] * freqs[None, :]
    narrow = lax.optimization_barrier(
        (jnp.tile(jnp.cos(angles), (1, 128 // half)), jnp.tile(jnp.sin(angles), (1, 128 // half))))
    cosine = jnp.tile(narrow[0], (1, qk_lanes // 128))
    sine = jnp.tile(narrow[1], (1, qk_lanes // 128))
    ahead = jnp.roll(x, -half, axis=1)
    behind = jnp.roll(x, half, axis=1)
    rotated = jnp.where((within < half)[None, :], x * cosine - ahead * sine,
                        x * cosine + behind * sine)
    qk = rotated.astype(jnp.bfloat16)
    value_new = projected[:, qk_lanes:].astype(jnp.bfloat16)
    first = migrate_first(pool, mig_src, row_count)
    mixed, landed = attend(qk, value_new, page_table, lengths, pool,
                           lambda dep: migrate_rest(pool, mig_src, row_count, first, dep))
    mixed = mixed.reshape(req_row, heads_here * HEAD_DIM)
    mixed_all = lax.all_gather(mixed, "row", axis=0, tiled=True)
    chosen = deal
    col_count = lax.axis_size("col")
    partial = jnp.dot(
        jnp.take(mixed_all, chosen, axis=0), w_out, preferred_element_type=jnp.float32
    ).astype(jnp.bfloat16)
    parts = lax.all_to_all(partial, "col", split_axis=0, concat_axis=0, tiled=True)
    attended = jnp.sum(
        parts.reshape(col_count, rows_all // col_count, -1).astype(jnp.float32), axis=0
    ).astype(jnp.bfloat16)
    return (attended, landed)


def solution(mesh):
    placed = (
        P("col", "row"),
        P("row", "col"),
        P("col", "row"),
        P("row", None, "col"),
        P("row", None),
        P("row"),
        P(),
        P(),
    )
    return jax.shard_map(
        on_device,
        mesh=mesh,
        in_specs=placed,
        out_specs=(P("col", "row"), P("row", None, "col")),
        check_vma=False,
    )
```

```python
import functools

import jax
import jax.numpy as jnp
from jax import lax
from jax.experimental import pallas as pl
from jax.experimental.pallas import tpu as pltpu
from jax.sharding import PartitionSpec as P

HEAD_DIM = 64
PAGE = 64


theta_base = 130000.0
neg_large = -1e30


def rotate(values, positions):
    half = values.shape[-1] // 2
    freqs = theta_base ** (-(jnp.arange(half, dtype=jnp.float32) * 2.0 / values.shape[-1]))
    angles = positions.astype(jnp.float32)[:, None, None] * freqs[None, None, :]
    cosine = jnp.cos(angles)
    sine = jnp.sin(angles)
    first = values[..., :half]
    second = values[..., half:]
    return jnp.concatenate(
        [first * cosine - second * sine, second * cosine + first * sine], axis=-1
    )


def page_scores(page_of, flat, scores, qrow, start, count, length, maxp):
    rows = qrow.shape[0]
    pos = lax.broadcasted_iota(jnp.int32, (rows, PAGE), 1)

    def one(k):
        j = flat[start + k] % maxp
        s = lax.dot_general(
            qrow, page_of(start + k), (((1,), (1,)), ((), ())),
            preferred_element_type=jnp.float32,
        ) * 0.125
        s = jnp.where(j * PAGE + pos < length, s, neg_large)
        scores[k] = s
        return s

    def four(k4, top):
        s0 = one(4 * k4)
        s1 = one(4 * k4 + 1)
        s2 = one(4 * k4 + 2)
        s3 = one(4 * k4 + 3)
        return jnp.maximum(top, jnp.maximum(jnp.maximum(s0, s1), jnp.maximum(s2, s3)))

    top = lax.fori_loop(0, count // 4, four, jnp.full((rows, PAGE), neg_large, jnp.float32))
    top = lax.fori_loop(count // 4 * 4, count, lambda k, t: jnp.maximum(t, one(k)), top)
    return jnp.max(top, axis=1, keepdims=True)


def page_values(page_of, flat, scores, top, start, count, length, maxp, lanes):
    rows = top.shape[0]
    pos = lax.broadcasted_iota(jnp.int32, (rows, PAGE), 1)

    def one(k):
        j = flat[start + k] % maxp
        e = jnp.where(j * PAGE + pos < length, jnp.exp(scores[k] - top), 0.0)
        w = e.astype(jnp.bfloat16)
        return e, jnp.dot(w, page_of(start + k), preferred_element_type=jnp.float32)

    def four(k4, carry):
        total, numer = carry
        e0, n0 = one(4 * k4)
        e1, n1 = one(4 * k4 + 1)
        e2, n2 = one(4 * k4 + 2)
        e3, n3 = one(4 * k4 + 3)
        return total + ((e0 + e1) + (e2 + e3)), numer + ((n0 + n1) + (n2 + n3))

    def single(k, carry):
        total, numer = carry
        e0, n0 = one(k)
        return total + e0, numer + n0

    init = (jnp.zeros((rows, PAGE), jnp.float32), jnp.zeros((rows, lanes), jnp.float32))
    carry = lax.fori_loop(0, count // 4, four, init)
    total, numer = lax.fori_loop(count // 4 * 4, count, single, carry)
    return jnp.sum(total, axis=1, keepdims=True), numer


def build_list(tbl, lens, pool_n, maxp, reqs, flat, starts, listed, landing):
    def req(r, carry):
        n, nl = carry
        starts[r] = n
        count = (lens[r] + PAGE - 1) // PAGE

        def page(j, n):
            e = r * maxp + j
            flat[n] = e
            keep = (tbl[e] >= pool_n) if landing else (tbl[e] < pool_n)
            return n + keep.astype(jnp.int32)

        n2 = lax.fori_loop(0, count, page, n)
        listed[nl] = r
        return n2, nl + (n2 > n).astype(jnp.int32)

    n, nl = lax.fori_loop(0, reqs, req, (0, 0))
    starts[reqs] = n
    return n, nl


def query_rows(qwide_ref, r, rows):
    lanes = qwide_ref.shape[2]
    wide = jnp.broadcast_to(qwide_ref[r], (rows, lanes))
    head = lax.broadcasted_iota(jnp.int32, (rows, lanes), 0)
    lane = lax.broadcasted_iota(jnp.int32, (rows, lanes), 1)
    return jnp.where(head == lane // 128, wide, 0.0).astype(jnp.bfloat16)


def pool_kernel(tbl, lens, qrow_ref, snew_ref, pool_ref,
                m_ref, l_ref, n_ref, scores, flat, starts, listed):
    reqs, rows, lanes = snew_ref.shape[0], snew_ref.shape[1], pool_ref.shape[2]
    maxp = scores.shape[0]
    pool_n = pool_ref.shape[0]
    build_list(tbl, lens, pool_n, maxp, reqs, flat, starts, listed, False)
    page_of = lambda f: pool_ref[jnp.clip(tbl[flat[f]], 0, pool_n - 1)]

    def request(r, carry):
        start = starts[r]
        count = starts[r + 1] - start
        length = lens[r]
        snew = snew_ref[r][:, :1]
        top = page_scores(page_of, flat, scores, query_rows(qrow_ref, r, rows), start, count,
                          length, maxp)
        top = jnp.maximum(top, snew)
        total, numer = page_values(page_of, flat, scores, top, start, count, length, maxp,
                                   lanes)
        m_ref[r] = jnp.broadcast_to(top, (rows, 128))
        l_ref[r] = jnp.broadcast_to(total, (rows, 128))
        n_ref[r] = numer
        return carry

    lax.fori_loop(0, reqs, request, 0)


def land_kernel(tbl, lens, qrow_ref, m_in, l_in, n_in, land_ref, pool_n_ref,
                m_ref, l_ref, n_ref, scores, flat, starts, listed):
    reqs, rows, lanes = m_in.shape[0], m_in.shape[1], land_ref.shape[2]
    maxp = scores.shape[0]
    pool_n = pool_n_ref.shape[0]
    land_n = land_ref.shape[0]
    _, listed_n = build_list(tbl, lens, pool_n, maxp, reqs, flat, starts, listed, True)
    m_ref[...] = m_in[...]
    l_ref[...] = l_in[...]
    n_ref[...] = n_in[...]
    page_of = lambda f: land_ref[jnp.clip(tbl[flat[f]] - pool_n, 0, land_n - 1)]

    def request(k, carry):
        r = listed[k]
        start = starts[r]
        count = starts[r + 1] - start
        length = lens[r]
        top_a = m_in[r][:, :1]
        top_b = page_scores(page_of, flat, scores, query_rows(qrow_ref, r, rows), start, count,
                            length, maxp)
        top = jnp.maximum(top_a, top_b)
        total, numer = page_values(page_of, flat, scores, top, start, count, length, maxp,
                                   lanes)
        scale = jnp.exp(top_a - top)
        m_ref[r] = jnp.broadcast_to(top, (rows, 128))
        l_ref[r] = jnp.broadcast_to(total + l_in[r][:, :1] * scale, (rows, 128))
        n_ref[r] = numer + n_in[r] * scale
        return carry

    lax.fori_loop(0, listed_n, request, 0)


def attend(qk, value_new, table, lens, pool, landed_fn):
    req_count = qk.shape[0]
    lanes = pool.shape[2]
    heads_here = lanes // (2 * HEAD_DIM)
    maxp = table.shape[1]
    pool_n = pool.shape[0]
    rows = 8
    lane = jnp.arange(lanes, dtype=jnp.int32)
    qwide = jnp.where((lane % 128 < HEAD_DIM)[None, :], qk.astype(jnp.float32), 0.0)
    qwide = qwide.reshape(req_count, 1, lanes)
    grouped = qk.astype(jnp.float32).reshape(req_count, heads_here, 2 * HEAD_DIM)
    score_new = jnp.sum(grouped[..., :HEAD_DIM] * grouped[..., HEAD_DIM:], axis=-1) * 0.125
    vf = value_new.astype(jnp.float32).reshape(req_count, heads_here, HEAD_DIM)
    snew = jnp.zeros((req_count, rows, 128), jnp.float32) + jnp.pad(
        score_new, ((0, 0), (0, rows - heads_here)))[:, :, None]
    tbl = table.reshape(-1)

    full = lambda shape: pl.BlockSpec(shape, lambda i, *_: (0,) * len(shape))
    big = (req_count, rows, lanes)
    small = (req_count, rows, 128)
    wide = (req_count, 1, lanes)
    scratch = [
        pltpu.VMEM((maxp, rows, PAGE), jnp.float32),
        pltpu.SMEM((req_count * maxp,), jnp.int32),
        pltpu.SMEM((req_count + 1,), jnp.int32),
        pltpu.SMEM((req_count,), jnp.int32),
    ]
    params = pltpu.CompilerParams(
        dimension_semantics=("arbitrary",), vmem_limit_bytes=60 * 1024 * 1024)
    state = [
        jax.ShapeDtypeStruct(small, jnp.float32),
        jax.ShapeDtypeStruct(small, jnp.float32),
        jax.ShapeDtypeStruct(big, jnp.float32),
    ]
    m_a, l_a, n_a = pl.pallas_call(
        pool_kernel,
        grid_spec=pltpu.PrefetchScalarGridSpec(
            num_scalar_prefetch=2,
            grid=(1,),
            in_specs=[full(wide), full(small), pl.BlockSpec(memory_space=pltpu.VMEM)],
            out_specs=[full(small), full(small), full(big)],
            scratch_shapes=scratch,
        ),
        out_shape=state,
        compiler_params=params,
    )(tbl, lens, qwide, snew, pool)

    landed = landed_fn(n_a)
    m_b, l_b, n_b = pl.pallas_call(
        land_kernel,
        grid_spec=pltpu.PrefetchScalarGridSpec(
            num_scalar_prefetch=2,
            grid=(1,),
            in_specs=[full(wide), full(small), full(small), full(big),
                      pl.BlockSpec(memory_space=pltpu.VMEM), pl.BlockSpec(memory_space=pl.ANY)],
            out_specs=[full(small), full(small), full(big)],
            scratch_shapes=scratch,
        ),
        out_shape=state,
        compiler_params=params,
    )(tbl, lens, qwide, m_a, l_a, n_a, landed, pool)
    top = m_b[:, :heads_here, :1]
    e_new = jnp.exp(score_new[:, :, None] - top)
    w_new = e_new.astype(jnp.bfloat16).astype(jnp.float32)
    numer = n_b[:, :heads_here].reshape(req_count, heads_here, heads_here, 2, HEAD_DIM)
    numer = jnp.stack([numer[:, h, h, 1] for h in range(heads_here)], axis=1)
    picked = ((numer + w_new * vf) / (l_b[:, :heads_here, :1] + e_new)).astype(jnp.bfloat16)
    return picked, landed


def migration_plan(pool, mig_src, row_count):
    pool_dev = pool.shape[0]
    land_all = mig_src.shape[0]
    land_dev = land_all // row_count
    src_row = jnp.clip(mig_src // pool_dev, 0, row_count - 1)
    local_page = jnp.clip(mig_src - src_row * pool_dev, 0, pool_dev - 1)
    dst_row = jnp.arange(land_all, dtype=jnp.int32) // land_dev
    onehot = (src_row[:, None] == jnp.arange(row_count, dtype=jnp.int32)[None, :]).astype(jnp.int32)
    csum = jnp.cumsum(onehot.reshape(row_count, land_dev, row_count), axis=1)
    csum = csum.reshape(land_all, row_count)
    rank = jnp.sum(csum * onehot, axis=1) - 1
    return dict(src_row=src_row, local_page=local_page, dst_row=dst_row, rank=rank,
                most=jnp.max(csum), land_dev=land_dev, first=max(1, (land_dev * 5 + 7) // 8))


def gather_kernel(idx_ref, pool_ref, out_ref, sems):
    count = out_ref.shape[0]
    pool_n = pool_ref.shape[0]

    def start(i, carry):
        src = jnp.clip(idx_ref[i], 0, pool_n - 1)
        pltpu.make_async_copy(pool_ref.at[src], out_ref.at[i], sems.at[i]).start()
        return carry

    def wait(i, carry):
        pltpu.make_async_copy(pool_ref.at[0], out_ref.at[i], sems.at[i]).wait()
        return carry

    lax.fori_loop(0, count, start, 0)
    lax.fori_loop(0, count, wait, 0)


def outgoing_pages(pool, plan, row_count, lo, size):
    my_row = lax.axis_index("row")
    rank = plan["rank"]
    sel = (plan["src_row"] == my_row) & (rank >= lo) & (rank < lo + size)
    where = jnp.where(sel, plan["dst_row"] * size + (rank - lo), row_count * size)
    idx = jnp.zeros((row_count * size,), jnp.int32).at[where].set(plan["local_page"], mode="drop")
    count = row_count * size
    pages = pl.pallas_call(
        gather_kernel,
        grid_spec=pltpu.PrefetchScalarGridSpec(
            num_scalar_prefetch=1,
            grid=(1,),
            in_specs=[pl.BlockSpec(memory_space=pl.ANY)],
            out_specs=pl.BlockSpec((count,) + pool.shape[1:], lambda i, *_: (0, 0, 0)),
            scratch_shapes=[pltpu.SemaphoreType.DMA((count,))],
        ),
        out_shape=jax.ShapeDtypeStruct((count,) + pool.shape[1:], pool.dtype),
        compiler_params=pltpu.CompilerParams(vmem_limit_bytes=32 * 1024 * 1024),
    )(idx, pool)
    return pages.reshape(row_count, size, pool.shape[1], pool.shape[2])


def migrate_first(pool, mig_src, row_count):
    plan = migration_plan(pool, mig_src, row_count)
    sent = outgoing_pages(pool, plan, row_count, 0, plan["first"])
    return lax.all_to_all(sent, "row", split_axis=0, concat_axis=0, tiled=True)


def migrate_rest(pool, mig_src, row_count, first_recv, dep):
    plan = migration_plan(pool, mig_src, row_count)
    land_dev, k1 = plan["land_dev"], plan["first"]
    my_row = lax.axis_index("row")
    mine = my_row * land_dev + jnp.arange(land_dev, dtype=jnp.int32)
    src_mine = plan["src_row"][mine]
    rank_mine = plan["rank"][mine]
    pool_dep, _ = lax.optimization_barrier((pool, dep))
    sizes = [0, land_dev - k1] if land_dev > k1 else [0]

    def branch(size):
        def run(pool_b, recv1):
            if size == 0:
                both = recv1
            else:
                sent = outgoing_pages(pool_b, plan, row_count, k1, size)
                recv2 = lax.all_to_all(sent, "row", split_axis=0, concat_axis=0, tiled=True)
                both = jnp.concatenate([recv1, recv2], axis=1)
            width = k1 + size
            flat = both.reshape(row_count * width, both.shape[2], both.shape[3])
            return jnp.take(flat, src_mine * width + jnp.clip(rank_mine, 0, width - 1), axis=0)
        return run

    need = jnp.maximum(plan["most"] - k1, 0)
    index = jnp.sum((jnp.array(sizes, jnp.int32) < need).astype(jnp.int32))
    return lax.switch(index, [branch(b) for b in sizes], pool_dep, first_recv)


def on_device(xn, w_qkv, w_out, pool, page_table, lengths, mig_src, deal):
    heads_here = w_out.shape[0] // HEAD_DIM
    rows_all = xn.shape[0] * lax.axis_size("col")
    row_count = lax.axis_size("row")
    req_row = rows_all // row_count
    inverse = jnp.zeros((rows_all,), jnp.int32).at[deal].set(jnp.arange(rows_all, dtype=jnp.int32))
    gathered = lax.all_gather(xn, "col", axis=0, tiled=True)
    chosen = inverse
    heads3 = w_qkv.reshape(w_qkv.shape[0], heads_here, 3, HEAD_DIM)
    w_perm = jnp.concatenate(
        [heads3[:, :, :2].reshape(w_qkv.shape[0], -1), heads3[:, :, 2].reshape(w_qkv.shape[0], -1)],
        axis=1)
    partial = jnp.dot(jnp.take(gathered, chosen, axis=0), w_perm,
                      preferred_element_type=jnp.float32).astype(jnp.bfloat16)
    parts = lax.all_to_all(partial, "row", split_axis=0, concat_axis=0, tiled=True)
    projected = jnp.sum(parts.reshape(row_count, req_row, -1).astype(jnp.float32), axis=0)
    qk_lanes = heads_here * 2 * HEAD_DIM
    x = projected[:, :qk_lanes]
    lane = jnp.arange(qk_lanes, dtype=jnp.int32)
    within = lane % HEAD_DIM
    half = HEAD_DIM // 2
    freqs = theta_base ** (-(jnp.arange(half, dtype=jnp.float32) * 2.0 / HEAD_DIM))
    angles = lengths.astype(jnp.float32)[:, None] * freqs[None, :]
    cosine = jnp.tile(jnp.cos(angles), (1, qk_lanes // half))
    sine = jnp.tile(jnp.sin(angles), (1, qk_lanes // half))
    ahead = jnp.roll(x, -half, axis=1)
    behind = jnp.roll(x, half, axis=1)
    rotated = jnp.where((within < half)[None, :], x * cosine - ahead * sine,
                        x * cosine + behind * sine)
    qk = rotated.astype(jnp.bfloat16)
    value_new = projected[:, qk_lanes:].astype(jnp.bfloat16)
    first = migrate_first(pool, mig_src, row_count)
    mixed, landed = attend(qk, value_new, page_table, lengths, pool,
                           lambda dep: migrate_rest(pool, mig_src, row_count, first, dep))
    mixed = mixed.reshape(req_row, heads_here * HEAD_DIM)
    mixed_all = lax.all_gather(mixed, "row", axis=0, tiled=True)
    chosen = deal
    col_count = lax.axis_size("col")
    partial = jnp.dot(
        jnp.take(mixed_all, chosen, axis=0), w_out, preferred_element_type=jnp.float32
    ).astype(jnp.bfloat16)
    parts = lax.all_to_all(partial, "col", split_axis=0, concat_axis=0, tiled=True)
    attended = jnp.sum(
        parts.reshape(col_count, rows_all // col_count, -1).astype(jnp.float32), axis=0
    ).astype(jnp.bfloat16)
    return (attended, landed)


def solution(mesh):
    placed = (
        P("col", "row"),
        P("row", "col"),
        P("col", "row"),
        P("row", None, "col"),
        P("row", None),
        P("row"),
        P(),
        P(),
    )
    return jax.shard_map(
        on_device,
        mesh=mesh,
        in_specs=placed,
        out_specs=(P("col", "row"), P("row", None, "col")),
        check_vma=False,
    )
```

```python
import functools

import jax
import jax.numpy as jnp
from jax import lax
from jax.experimental import pallas as pl
from jax.experimental.pallas import tpu as pltpu
from jax.sharding import PartitionSpec as P

HEAD_DIM = 64
PAGE = 64


theta_base = 130000.0
neg_large = -1e30


def rotate(values, positions):
    half = values.shape[-1] // 2
    freqs = theta_base ** (-(jnp.arange(half, dtype=jnp.float32) * 2.0 / values.shape[-1]))
    angles = positions.astype(jnp.float32)[:, None, None] * freqs[None, None, :]
    cosine = jnp.cos(angles)
    sine = jnp.sin(angles)
    first = values[..., :half]
    second = values[..., half:]
    return jnp.concatenate(
        [first * cosine - second * sine, second * cosine + first * sine], axis=-1
    )


def page_scores(page_of, flat, scores, qrow, start, count, length, maxp):
    rows = qrow.shape[0]
    pos = lax.broadcasted_iota(jnp.int32, (rows, PAGE), 1)

    def one(k):
        j = flat[start + k] % maxp
        s = lax.dot_general(
            qrow, page_of(start + k), (((1,), (1,)), ((), ())),
            preferred_element_type=jnp.float32,
        ) * 0.125
        s = jnp.where(j * PAGE + pos < length, s, neg_large)
        scores[k] = s
        return s

    def two(k2, top):
        s0 = one(2 * k2)
        s1 = one(2 * k2 + 1)
        return jnp.maximum(top, jnp.maximum(s0, s1))

    top = lax.fori_loop(0, count // 2, two, jnp.full((rows, PAGE), neg_large, jnp.float32))
    top = lax.fori_loop(count // 2 * 2, count, lambda k, t: jnp.maximum(t, one(k)), top)
    return jnp.max(top, axis=1, keepdims=True)


def page_values(page_of, flat, scores, top, start, count, length, maxp, lanes):
    rows = top.shape[0]
    pos = lax.broadcasted_iota(jnp.int32, (rows, PAGE), 1)

    def one(k):
        j = flat[start + k] % maxp
        e = jnp.exp(scores[k] - top)
        w = e.astype(jnp.bfloat16)
        return e, jnp.dot(w, page_of(start + k), preferred_element_type=jnp.float32)

    def two(k2, carry):
        total, numer = carry
        e0, n0 = one(2 * k2)
        e1, n1 = one(2 * k2 + 1)
        return total + (e0 + e1), numer + (n0 + n1)

    def single(k, carry):
        total, numer = carry
        e0, n0 = one(k)
        return total + e0, numer + n0

    init = (jnp.zeros((rows, PAGE), jnp.float32), jnp.zeros((rows, lanes), jnp.float32))
    carry = lax.fori_loop(0, count // 2, two, init)
    total, numer = lax.fori_loop(count // 2 * 2, count, single, carry)
    return jnp.sum(total, axis=1, keepdims=True), numer


def build_list(tbl, lens, pool_n, maxp, reqs, flat, starts, listed, landing):
    def req(r, carry):
        n, nl = carry
        starts[r] = n
        count = (lens[r] + PAGE - 1) // PAGE

        def page(j, n):
            e = r * maxp + j
            flat[n] = e
            keep = (tbl[e] >= pool_n) if landing else (tbl[e] < pool_n)
            return n + keep.astype(jnp.int32)

        n2 = lax.fori_loop(0, count, page, n)
        listed[nl] = r
        return n2, nl + (n2 > n).astype(jnp.int32)

    n, nl = lax.fori_loop(0, reqs, req, (0, 0))
    starts[reqs] = n
    return n, nl


def query_rows(qwide_ref, r, rows):
    lanes = qwide_ref.shape[2]
    wide = jnp.broadcast_to(qwide_ref[r], (rows, lanes))
    head = lax.broadcasted_iota(jnp.int32, (rows, lanes), 0)
    lane = lax.broadcasted_iota(jnp.int32, (rows, lanes), 1)
    return jnp.where(head == lane // 128, wide, 0.0).astype(jnp.bfloat16)


def pool_kernel(tbl, lens, qrow_ref, snew_ref, pool_ref,
                m_ref, l_ref, n_ref, scores, flat, starts, listed):
    reqs, rows, lanes = snew_ref.shape[0], snew_ref.shape[1], pool_ref.shape[2]
    maxp = scores.shape[0]
    pool_n = pool_ref.shape[0]
    build_list(tbl, lens, pool_n, maxp, reqs, flat, starts, listed, False)
    page_of = lambda f: pool_ref[jnp.clip(tbl[flat[f]], 0, pool_n - 1)]

    def request(r, carry):
        start = starts[r]
        count = starts[r + 1] - start
        length = lens[r]
        snew = snew_ref[r][:, :1]
        top = page_scores(page_of, flat, scores, query_rows(qrow_ref, r, rows), start, count,
                          length, maxp)
        top = jnp.maximum(top, snew)
        total, numer = page_values(page_of, flat, scores, top, start, count, length, maxp,
                                   lanes)
        m_ref[r] = jnp.broadcast_to(top, (rows, 128))
        l_ref[r] = jnp.broadcast_to(total, (rows, 128))
        n_ref[r] = numer
        return carry

    lax.fori_loop(0, reqs, request, 0)


def land_kernel(tbl, lens, qrow_ref, m_in, l_in, n_in, land_ref, pool_n_ref,
                m_ref, l_ref, n_ref, scores, flat, starts, listed):
    reqs, rows, lanes = m_in.shape[0], m_in.shape[1], land_ref.shape[2]
    maxp = scores.shape[0]
    pool_n = pool_n_ref.shape[0]
    land_n = land_ref.shape[0]
    _, listed_n = build_list(tbl, lens, pool_n, maxp, reqs, flat, starts, listed, True)
    m_ref[...] = m_in[...]
    l_ref[...] = l_in[...]
    n_ref[...] = n_in[...]
    page_of = lambda f: land_ref[jnp.clip(tbl[flat[f]] - pool_n, 0, land_n - 1)]

    def request(k, carry):
        r = listed[k]
        start = starts[r]
        count = starts[r + 1] - start
        length = lens[r]
        top_a = m_in[r][:, :1]
        top_b = page_scores(page_of, flat, scores, query_rows(qrow_ref, r, rows), start, count,
                            length, maxp)
        top = jnp.maximum(top_a, top_b)
        total, numer = page_values(page_of, flat, scores, top, start, count, length, maxp,
                                   lanes)
        scale = jnp.exp(top_a - top)
        m_ref[r] = jnp.broadcast_to(top, (rows, 128))
        l_ref[r] = jnp.broadcast_to(total + l_in[r][:, :1] * scale, (rows, 128))
        n_ref[r] = numer + n_in[r] * scale
        return carry

    lax.fori_loop(0, listed_n, request, 0)


def attend(qk, value_new, table, lens, pool, landed_fn):
    req_count = qk.shape[0]
    lanes = pool.shape[2]
    heads_here = lanes // (2 * HEAD_DIM)
    maxp = table.shape[1]
    pool_n = pool.shape[0]
    rows = 8
    lane = jnp.arange(lanes, dtype=jnp.int32)
    qwide = jnp.where((lane % 128 < HEAD_DIM)[None, :], qk.astype(jnp.float32), 0.0)
    qwide = qwide.reshape(req_count, 1, lanes)
    grouped = qk.astype(jnp.float32).reshape(req_count, heads_here, 2 * HEAD_DIM)
    score_new = jnp.sum(grouped[..., :HEAD_DIM] * grouped[..., HEAD_DIM:], axis=-1) * 0.125
    vf = value_new.astype(jnp.float32).reshape(req_count, heads_here, HEAD_DIM)
    snew = jnp.zeros((req_count, rows, 128), jnp.float32) + jnp.pad(
        score_new, ((0, 0), (0, rows - heads_here)))[:, :, None]
    tbl = table.reshape(-1)

    full = lambda shape: pl.BlockSpec(shape, lambda i, *_: (0,) * len(shape))
    big = (req_count, rows, lanes)
    small = (req_count, rows, 128)
    wide = (req_count, 1, lanes)
    scratch = [
        pltpu.VMEM((maxp, rows, PAGE), jnp.float32),
        pltpu.SMEM((req_count * maxp,), jnp.int32),
        pltpu.SMEM((req_count + 1,), jnp.int32),
        pltpu.SMEM((req_count,), jnp.int32),
    ]
    params = pltpu.CompilerParams(
        dimension_semantics=("arbitrary",), vmem_limit_bytes=60 * 1024 * 1024)
    state = [
        jax.ShapeDtypeStruct(small, jnp.float32),
        jax.ShapeDtypeStruct(small, jnp.float32),
        jax.ShapeDtypeStruct(big, jnp.float32),
    ]
    m_a, l_a, n_a = pl.pallas_call(
        pool_kernel,
        grid_spec=pltpu.PrefetchScalarGridSpec(
            num_scalar_prefetch=2,
            grid=(1,),
            in_specs=[full(wide), full(small), pl.BlockSpec(memory_space=pltpu.VMEM)],
            out_specs=[full(small), full(small), full(big)],
            scratch_shapes=scratch,
        ),
        out_shape=state,
        compiler_params=params,
    )(tbl, lens, qwide, snew, pool)

    landed = landed_fn(n_a)
    m_b, l_b, n_b = pl.pallas_call(
        land_kernel,
        grid_spec=pltpu.PrefetchScalarGridSpec(
            num_scalar_prefetch=2,
            grid=(1,),
            in_specs=[full(wide), full(small), full(small), full(big),
                      pl.BlockSpec(memory_space=pltpu.VMEM), pl.BlockSpec(memory_space=pl.ANY)],
            out_specs=[full(small), full(small), full(big)],
            scratch_shapes=scratch,
        ),
        out_shape=state,
        compiler_params=params,
    )(tbl, lens, qwide, m_a, l_a, n_a, landed, pool)
    top = m_b[:, :heads_here, :1]
    e_new = jnp.exp(score_new[:, :, None] - top)
    w_new = e_new.astype(jnp.bfloat16).astype(jnp.float32)
    numer = n_b[:, :heads_here].reshape(req_count, heads_here, heads_here, 2, HEAD_DIM)
    numer = jnp.stack([numer[:, h, h, 1] for h in range(heads_here)], axis=1)
    picked = ((numer + w_new * vf) / (l_b[:, :heads_here, :1] + e_new)).astype(jnp.bfloat16)
    return picked, landed


def migration_plan(pool, mig_src, row_count):
    pool_dev = pool.shape[0]
    land_all = mig_src.shape[0]
    land_dev = land_all // row_count
    src_row = jnp.clip(mig_src // pool_dev, 0, row_count - 1)
    local_page = jnp.clip(mig_src - src_row * pool_dev, 0, pool_dev - 1)
    dst_row = jnp.arange(land_all, dtype=jnp.int32) // land_dev
    onehot = (src_row[:, None] == jnp.arange(row_count, dtype=jnp.int32)[None, :]).astype(jnp.int32)
    csum = jnp.cumsum(onehot.reshape(row_count, land_dev, row_count), axis=1)
    csum = csum.reshape(land_all, row_count)
    rank = jnp.sum(csum * onehot, axis=1) - 1
    return dict(src_row=src_row, local_page=local_page, dst_row=dst_row, rank=rank,
                most=jnp.max(csum), land_dev=land_dev, first=max(1, (land_dev * 5 + 7) // 8))


def gather_kernel(idx_ref, pool_ref, out_ref, sems):
    count = out_ref.shape[0]
    pool_n = pool_ref.shape[0]

    def start(i, carry):
        src = jnp.clip(idx_ref[i], 0, pool_n - 1)
        pltpu.make_async_copy(pool_ref.at[src], out_ref.at[i], sems.at[i]).start()
        return carry

    def wait(i, carry):
        pltpu.make_async_copy(pool_ref.at[0], out_ref.at[i], sems.at[i]).wait()
        return carry

    lax.fori_loop(0, count, start, 0)
    lax.fori_loop(0, count, wait, 0)


def outgoing_pages(pool, plan, row_count, lo, size):
    my_row = lax.axis_index("row")
    rank = plan["rank"]
    sel = (plan["src_row"] == my_row) & (rank >= lo) & (rank < lo + size)
    where = jnp.where(sel, plan["dst_row"] * size + (rank - lo), row_count * size)
    idx = jnp.zeros((row_count * size,), jnp.int32).at[where].set(plan["local_page"], mode="drop")
    count = row_count * size
    pages = pl.pallas_call(
        gather_kernel,
        grid_spec=pltpu.PrefetchScalarGridSpec(
            num_scalar_prefetch=1,
            grid=(1,),
            in_specs=[pl.BlockSpec(memory_space=pl.ANY)],
            out_specs=pl.BlockSpec((count,) + pool.shape[1:], lambda i, *_: (0, 0, 0)),
            scratch_shapes=[pltpu.SemaphoreType.DMA((count,))],
        ),
        out_shape=jax.ShapeDtypeStruct((count,) + pool.shape[1:], pool.dtype),
        compiler_params=pltpu.CompilerParams(vmem_limit_bytes=32 * 1024 * 1024),
    )(idx, pool)
    return pages.reshape(row_count, size, pool.shape[1], pool.shape[2])


def migrate_first(pool, mig_src, row_count):
    plan = migration_plan(pool, mig_src, row_count)
    sent = outgoing_pages(pool, plan, row_count, 0, plan["first"])
    return lax.all_to_all(sent, "row", split_axis=0, concat_axis=0, tiled=True)


def migrate_rest(pool, mig_src, row_count, first_recv, dep):
    plan = migration_plan(pool, mig_src, row_count)
    land_dev, k1 = plan["land_dev"], plan["first"]
    my_row = lax.axis_index("row")
    mine = my_row * land_dev + jnp.arange(land_dev, dtype=jnp.int32)
    src_mine = plan["src_row"][mine]
    rank_mine = plan["rank"][mine]
    pool_dep, _ = lax.optimization_barrier((pool, dep))
    sizes = [0, land_dev - k1] if land_dev > k1 else [0]

    def branch(size):
        def run(pool_b, recv1):
            if size == 0:
                both = recv1
            else:
                sent = outgoing_pages(pool_b, plan, row_count, k1, size)
                recv2 = lax.all_to_all(sent, "row", split_axis=0, concat_axis=0, tiled=True)
                both = jnp.concatenate([recv1, recv2], axis=1)
            width = k1 + size
            flat = both.reshape(row_count * width, both.shape[2], both.shape[3])
            return jnp.take(flat, src_mine * width + jnp.clip(rank_mine, 0, width - 1), axis=0)
        return run

    need = jnp.maximum(plan["most"] - k1, 0)
    index = jnp.sum((jnp.array(sizes, jnp.int32) < need).astype(jnp.int32))
    return lax.switch(index, [branch(b) for b in sizes], pool_dep, first_recv)


def on_device(xn, w_qkv, w_out, pool, page_table, lengths, mig_src, deal):
    heads_here = w_out.shape[0] // HEAD_DIM
    rows_all = xn.shape[0] * lax.axis_size("col")
    row_count = lax.axis_size("row")
    req_row = rows_all // row_count
    inverse = jnp.zeros((rows_all,), jnp.int32).at[deal].set(jnp.arange(rows_all, dtype=jnp.int32))
    gathered = lax.all_gather(xn, "col", axis=0, tiled=True)
    chosen = inverse
    heads3 = w_qkv.reshape(w_qkv.shape[0], heads_here, 3, HEAD_DIM)
    w_perm = jnp.concatenate(
        [heads3[:, :, :2].reshape(w_qkv.shape[0], -1), heads3[:, :, 2].reshape(w_qkv.shape[0], -1)],
        axis=1)
    partial = jnp.dot(jnp.take(gathered, chosen, axis=0), w_perm,
                      preferred_element_type=jnp.float32).astype(jnp.bfloat16)
    parts = lax.all_to_all(partial, "row", split_axis=0, concat_axis=0, tiled=True)
    projected = jnp.sum(parts.reshape(row_count, req_row, -1).astype(jnp.float32), axis=0)
    qk_lanes = heads_here * 2 * HEAD_DIM
    x = projected[:, :qk_lanes]
    lane = jnp.arange(qk_lanes, dtype=jnp.int32)
    within = lane % HEAD_DIM
    half = HEAD_DIM // 2
    freqs = theta_base ** (-(jnp.arange(half, dtype=jnp.float32) * 2.0 / HEAD_DIM))
    angles = lengths.astype(jnp.float32)[:, None] * freqs[None, :]
    cosine = jnp.tile(jnp.cos(angles), (1, qk_lanes // half))
    sine = jnp.tile(jnp.sin(angles), (1, qk_lanes // half))
    ahead = jnp.roll(x, -half, axis=1)
    behind = jnp.roll(x, half, axis=1)
    rotated = jnp.where((within < half)[None, :], x * cosine - ahead * sine,
                        x * cosine + behind * sine)
    qk = rotated.astype(jnp.bfloat16)
    value_new = projected[:, qk_lanes:].astype(jnp.bfloat16)
    first = migrate_first(pool, mig_src, row_count)
    mixed, landed = attend(qk, value_new, page_table, lengths, pool,
                           lambda dep: migrate_rest(pool, mig_src, row_count, first, dep))
    mixed = mixed.reshape(req_row, heads_here * HEAD_DIM)
    mixed_all = lax.all_gather(mixed, "row", axis=0, tiled=True)
    chosen = deal
    col_count = lax.axis_size("col")
    partial = jnp.dot(
        jnp.take(mixed_all, chosen, axis=0), w_out, preferred_element_type=jnp.float32
    ).astype(jnp.bfloat16)
    parts = lax.all_to_all(partial, "col", split_axis=0, concat_axis=0, tiled=True)
    attended = jnp.sum(
        parts.reshape(col_count, rows_all // col_count, -1).astype(jnp.float32), axis=0
    ).astype(jnp.bfloat16)
    return (attended, landed)


def solution(mesh):
    placed = (
        P("col", "row"),
        P("row", "col"),
        P("col", "row"),
        P("row", None, "col"),
        P("row", None),
        P("row"),
        P(),
        P(),
    )
    return jax.shard_map(
        on_device,
        mesh=mesh,
        in_specs=placed,
        out_specs=(P("col", "row"), P("row", None, "col")),
        check_vma=False,
    )
```

```python
import functools

import jax
import jax.numpy as jnp
from jax import lax
from jax.experimental import pallas as pl
from jax.experimental.pallas import tpu as pltpu
from jax.sharding import PartitionSpec as P

HEAD_DIM = 64
PAGE = 64


theta_base = 130000.0
neg_large = -1e30


def rotate(values, positions):
    half = values.shape[-1] // 2
    freqs = theta_base ** (-(jnp.arange(half, dtype=jnp.float32) * 2.0 / values.shape[-1]))
    angles = positions.astype(jnp.float32)[:, None, None] * freqs[None, None, :]
    cosine = jnp.cos(angles)
    sine = jnp.sin(angles)
    first = values[..., :half]
    second = values[..., half:]
    return jnp.concatenate(
        [first * cosine - second * sine, second * cosine + first * sine], axis=-1
    )


def page_scores(page_of, flat, scores, qrow, start, count, length, maxp):
    rows = qrow.shape[0]
    pos = lax.broadcasted_iota(jnp.int32, (rows, PAGE), 1)

    def one(k):
        j = flat[start + k] % maxp
        s = lax.dot_general(
            qrow, page_of(start + k), (((1,), (1,)), ((), ())),
            preferred_element_type=jnp.float32,
        ) * 0.125
        s = jnp.where(j * PAGE + pos < length, s, neg_large)
        scores[k] = s
        return s

    def two(k2, top):
        s0 = one(2 * k2)
        s1 = one(2 * k2 + 1)
        return jnp.maximum(top, jnp.maximum(s0, s1))

    top = lax.fori_loop(0, count // 2, two, jnp.full((rows, PAGE), neg_large, jnp.float32))
    top = lax.fori_loop(count // 2 * 2, count, lambda k, t: jnp.maximum(t, one(k)), top)
    return jnp.max(top, axis=1, keepdims=True)


def page_values(page_of, flat, scores, top, start, count, length, maxp, lanes):
    rows = top.shape[0]
    pos = lax.broadcasted_iota(jnp.int32, (rows, PAGE), 1)

    def one(k):
        j = flat[start + k] % maxp
        e = jnp.where(j * PAGE + pos < length, jnp.exp(scores[k] - top), 0.0)
        w = e.astype(jnp.bfloat16)
        return e, jnp.dot(w, page_of(start + k), preferred_element_type=jnp.float32)

    def two(k2, carry):
        total, numer = carry
        e0, n0 = one(2 * k2)
        e1, n1 = one(2 * k2 + 1)
        return total + (e0 + e1), numer + (n0 + n1)

    def single(k, carry):
        total, numer = carry
        e0, n0 = one(k)
        return total + e0, numer + n0

    init = (jnp.zeros((rows, PAGE), jnp.float32), jnp.zeros((rows, lanes), jnp.float32))
    total, numer = lax.fori_loop(0, count, single, init)
    return jnp.sum(total, axis=1, keepdims=True), numer


def build_list(tbl, lens, pool_n, maxp, reqs, flat, starts, listed, landing):
    def req(r, carry):
        n, nl = carry
        starts[r] = n
        count = (lens[r] + PAGE - 1) // PAGE

        def page(j, n):
            e = r * maxp + j
            flat[n] = e
            keep = (tbl[e] >= pool_n) if landing else (tbl[e] < pool_n)
            return n + keep.astype(jnp.int32)

        n2 = lax.fori_loop(0, count, page, n)
        listed[nl] = r
        return n2, nl + (n2 > n).astype(jnp.int32)

    n, nl = lax.fori_loop(0, reqs, req, (0, 0))
    starts[reqs] = n
    return n, nl


def query_rows(qwide_ref, r, rows):
    lanes = qwide_ref.shape[2]
    wide = jnp.broadcast_to(qwide_ref[r], (rows, lanes))
    head = lax.broadcasted_iota(jnp.int32, (rows, lanes), 0)
    lane = lax.broadcasted_iota(jnp.int32, (rows, lanes), 1)
    return jnp.where(head == lane // 128, wide, 0.0).astype(jnp.bfloat16)


def pool_kernel(tbl, lens, qrow_ref, snew_ref, pool_ref,
                m_ref, l_ref, n_ref, scores, flat, starts, listed):
    reqs, rows, lanes = snew_ref.shape[0], snew_ref.shape[1], pool_ref.shape[2]
    maxp = scores.shape[0]
    pool_n = pool_ref.shape[0]
    build_list(tbl, lens, pool_n, maxp, reqs, flat, starts, listed, False)
    page_of = lambda f: pool_ref[jnp.clip(tbl[flat[f]], 0, pool_n - 1)]

    def request(r, carry):
        start = starts[r]
        count = starts[r + 1] - start
        length = lens[r]
        snew = snew_ref[r][:, :1]
        top = page_scores(page_of, flat, scores, query_rows(qrow_ref, r, rows), start, count,
                          length, maxp)
        top = jnp.maximum(top, snew)
        total, numer = page_values(page_of, flat, scores, top, start, count, length, maxp,
                                   lanes)
        m_ref[r] = jnp.broadcast_to(top, (rows, 128))
        l_ref[r] = jnp.broadcast_to(total, (rows, 128))
        n_ref[r] = numer
        return carry

    lax.fori_loop(0, reqs, request, 0)


def land_kernel(tbl, lens, qrow_ref, m_in, l_in, n_in, land_ref, pool_n_ref,
                m_ref, l_ref, n_ref, scores, flat, starts, listed):
    reqs, rows, lanes = m_in.shape[0], m_in.shape[1], land_ref.shape[2]
    maxp = scores.shape[0]
    pool_n = pool_n_ref.shape[0]
    land_n = land_ref.shape[0]
    _, listed_n = build_list(tbl, lens, pool_n, maxp, reqs, flat, starts, listed, True)
    m_ref[...] = m_in[...]
    l_ref[...] = l_in[...]
    n_ref[...] = n_in[...]
    page_of = lambda f: land_ref[jnp.clip(tbl[flat[f]] - pool_n, 0, land_n - 1)]

    def request(k, carry):
        r = listed[k]
        start = starts[r]
        count = starts[r + 1] - start
        length = lens[r]
        top_a = m_in[r][:, :1]
        top_b = page_scores(page_of, flat, scores, query_rows(qrow_ref, r, rows), start, count,
                            length, maxp)
        top = jnp.maximum(top_a, top_b)
        total, numer = page_values(page_of, flat, scores, top, start, count, length, maxp,
                                   lanes)
        scale = jnp.exp(top_a - top)
        m_ref[r] = jnp.broadcast_to(top, (rows, 128))
        l_ref[r] = jnp.broadcast_to(total + l_in[r][:, :1] * scale, (rows, 128))
        n_ref[r] = numer + n_in[r] * scale
        return carry

    lax.fori_loop(0, listed_n, request, 0)


def attend(qk, value_new, table, lens, pool, landed_fn):
    req_count = qk.shape[0]
    lanes = pool.shape[2]
    heads_here = lanes // (2 * HEAD_DIM)
    maxp = table.shape[1]
    pool_n = pool.shape[0]
    rows = 8
    lane = jnp.arange(lanes, dtype=jnp.int32)
    qwide = jnp.where((lane % 128 < HEAD_DIM)[None, :], qk.astype(jnp.float32), 0.0)
    qwide = qwide.reshape(req_count, 1, lanes)
    grouped = qk.astype(jnp.float32).reshape(req_count, heads_here, 2 * HEAD_DIM)
    score_new = jnp.sum(grouped[..., :HEAD_DIM] * grouped[..., HEAD_DIM:], axis=-1) * 0.125
    vf = value_new.astype(jnp.float32).reshape(req_count, heads_here, HEAD_DIM)
    snew = jnp.zeros((req_count, rows, 128), jnp.float32) + jnp.pad(
        score_new, ((0, 0), (0, rows - heads_here)))[:, :, None]
    tbl = table.reshape(-1)

    full = lambda shape: pl.BlockSpec(shape, lambda i, *_: (0,) * len(shape))
    big = (req_count, rows, lanes)
    small = (req_count, rows, 128)
    wide = (req_count, 1, lanes)
    scratch = [
        pltpu.VMEM((maxp, rows, PAGE), jnp.float32),
        pltpu.SMEM((req_count * maxp,), jnp.int32),
        pltpu.SMEM((req_count + 1,), jnp.int32),
        pltpu.SMEM((req_count,), jnp.int32),
    ]
    params = pltpu.CompilerParams(
        dimension_semantics=("arbitrary",), vmem_limit_bytes=60 * 1024 * 1024)
    state = [
        jax.ShapeDtypeStruct(small, jnp.float32),
        jax.ShapeDtypeStruct(small, jnp.float32),
        jax.ShapeDtypeStruct(big, jnp.float32),
    ]
    m_a, l_a, n_a = pl.pallas_call(
        pool_kernel,
        grid_spec=pltpu.PrefetchScalarGridSpec(
            num_scalar_prefetch=2,
            grid=(1,),
            in_specs=[full(wide), full(small), pl.BlockSpec(memory_space=pltpu.VMEM)],
            out_specs=[full(small), full(small), full(big)],
            scratch_shapes=scratch,
        ),
        out_shape=state,
        compiler_params=params,
    )(tbl, lens, qwide, snew, pool)

    landed = landed_fn(n_a)
    m_b, l_b, n_b = pl.pallas_call(
        land_kernel,
        grid_spec=pltpu.PrefetchScalarGridSpec(
            num_scalar_prefetch=2,
            grid=(1,),
            in_specs=[full(wide), full(small), full(small), full(big),
                      pl.BlockSpec(memory_space=pltpu.VMEM), pl.BlockSpec(memory_space=pl.ANY)],
            out_specs=[full(small), full(small), full(big)],
            scratch_shapes=scratch,
        ),
        out_shape=state,
        compiler_params=params,
    )(tbl, lens, qwide, m_a, l_a, n_a, landed, pool)
    top = m_b[:, :heads_here, :1]
    e_new = jnp.exp(score_new[:, :, None] - top)
    w_new = e_new.astype(jnp.bfloat16).astype(jnp.float32)
    numer = n_b[:, :heads_here].reshape(req_count, heads_here, heads_here, 2, HEAD_DIM)
    numer = jnp.stack([numer[:, h, h, 1] for h in range(heads_here)], axis=1)
    picked = ((numer + w_new * vf) / (l_b[:, :heads_here, :1] + e_new)).astype(jnp.bfloat16)
    return picked, landed


def migration_plan(pool, mig_src, row_count):
    pool_dev = pool.shape[0]
    land_all = mig_src.shape[0]
    land_dev = land_all // row_count
    src_row = jnp.clip(mig_src // pool_dev, 0, row_count - 1)
    local_page = jnp.clip(mig_src - src_row * pool_dev, 0, pool_dev - 1)
    dst_row = jnp.arange(land_all, dtype=jnp.int32) // land_dev
    onehot = (src_row[:, None] == jnp.arange(row_count, dtype=jnp.int32)[None, :]).astype(jnp.int32)
    csum = jnp.cumsum(onehot.reshape(row_count, land_dev, row_count), axis=1)
    csum = csum.reshape(land_all, row_count)
    rank = jnp.sum(csum * onehot, axis=1) - 1
    return dict(src_row=src_row, local_page=local_page, dst_row=dst_row, rank=rank,
                most=jnp.max(csum), land_dev=land_dev, first=max(1, (land_dev * 5 + 7) // 8))


def gather_kernel(idx_ref, pool_ref, out_ref, sems):
    count = out_ref.shape[0]
    pool_n = pool_ref.shape[0]

    def start(i, carry):
        src = jnp.clip(idx_ref[i], 0, pool_n - 1)
        pltpu.make_async_copy(pool_ref.at[src], out_ref.at[i], sems.at[i]).start()
        return carry

    def wait(i, carry):
        pltpu.make_async_copy(pool_ref.at[0], out_ref.at[i], sems.at[i]).wait()
        return carry

    lax.fori_loop(0, count, start, 0)
    lax.fori_loop(0, count, wait, 0)


def outgoing_pages(pool, plan, row_count, lo, size):
    my_row = lax.axis_index("row")
    rank = plan["rank"]
    sel = (plan["src_row"] == my_row) & (rank >= lo) & (rank < lo + size)
    where = jnp.where(sel, plan["dst_row"] * size + (rank - lo), row_count * size)
    idx = jnp.zeros((row_count * size,), jnp.int32).at[where].set(plan["local_page"], mode="drop")
    count = row_count * size
    pages = pl.pallas_call(
        gather_kernel,
        grid_spec=pltpu.PrefetchScalarGridSpec(
            num_scalar_prefetch=1,
            grid=(1,),
            in_specs=[pl.BlockSpec(memory_space=pl.ANY)],
            out_specs=pl.BlockSpec((count,) + pool.shape[1:], lambda i, *_: (0, 0, 0)),
            scratch_shapes=[pltpu.SemaphoreType.DMA((count,))],
        ),
        out_shape=jax.ShapeDtypeStruct((count,) + pool.shape[1:], pool.dtype),
        compiler_params=pltpu.CompilerParams(vmem_limit_bytes=32 * 1024 * 1024),
    )(idx, pool)
    return pages.reshape(row_count, size, pool.shape[1], pool.shape[2])


def migrate_first(pool, mig_src, row_count):
    plan = migration_plan(pool, mig_src, row_count)
    sent = outgoing_pages(pool, plan, row_count, 0, plan["first"])
    return lax.all_to_all(sent, "row", split_axis=0, concat_axis=0, tiled=True)


def migrate_rest(pool, mig_src, row_count, first_recv, dep):
    plan = migration_plan(pool, mig_src, row_count)
    land_dev, k1 = plan["land_dev"], plan["first"]
    my_row = lax.axis_index("row")
    mine = my_row * land_dev + jnp.arange(land_dev, dtype=jnp.int32)
    src_mine = plan["src_row"][mine]
    rank_mine = plan["rank"][mine]
    pool_dep, _ = lax.optimization_barrier((pool, dep))
    sizes = [0, land_dev - k1] if land_dev > k1 else [0]

    def branch(size):
        def run(pool_b, recv1):
            if size == 0:
                both = recv1
            else:
                sent = outgoing_pages(pool_b, plan, row_count, k1, size)
                recv2 = lax.all_to_all(sent, "row", split_axis=0, concat_axis=0, tiled=True)
                both = jnp.concatenate([recv1, recv2], axis=1)
            width = k1 + size
            flat = both.reshape(row_count * width, both.shape[2], both.shape[3])
            return jnp.take(flat, src_mine * width + jnp.clip(rank_mine, 0, width - 1), axis=0)
        return run

    need = jnp.maximum(plan["most"] - k1, 0)
    index = jnp.sum((jnp.array(sizes, jnp.int32) < need).astype(jnp.int32))
    return lax.switch(index, [branch(b) for b in sizes], pool_dep, first_recv)


def on_device(xn, w_qkv, w_out, pool, page_table, lengths, mig_src, deal):
    heads_here = w_out.shape[0] // HEAD_DIM
    rows_all = xn.shape[0] * lax.axis_size("col")
    row_count = lax.axis_size("row")
    req_row = rows_all // row_count
    inverse = jnp.zeros((rows_all,), jnp.int32).at[deal].set(jnp.arange(rows_all, dtype=jnp.int32))
    gathered = lax.all_gather(xn, "col", axis=0, tiled=True)
    chosen = inverse
    heads3 = w_qkv.reshape(w_qkv.shape[0], heads_here, 3, HEAD_DIM)
    w_perm = jnp.concatenate(
        [heads3[:, :, :2].reshape(w_qkv.shape[0], -1), heads3[:, :, 2].reshape(w_qkv.shape[0], -1)],
        axis=1)
    partial = jnp.dot(jnp.take(gathered, chosen, axis=0), w_perm,
                      preferred_element_type=jnp.float32).astype(jnp.bfloat16)
    parts = lax.all_to_all(partial, "row", split_axis=0, concat_axis=0, tiled=True)
    projected = jnp.sum(parts.reshape(row_count, req_row, -1).astype(jnp.float32), axis=0)
    qk_lanes = heads_here * 2 * HEAD_DIM
    x = projected[:, :qk_lanes]
    lane = jnp.arange(qk_lanes, dtype=jnp.int32)
    within = lane % HEAD_DIM
    half = HEAD_DIM // 2
    freqs = theta_base ** (-(jnp.arange(half, dtype=jnp.float32) * 2.0 / HEAD_DIM))
    angles = lengths.astype(jnp.float32)[:, None] * freqs[None, :]
    cosine = jnp.tile(jnp.cos(angles), (1, qk_lanes // half))
    sine = jnp.tile(jnp.sin(angles), (1, qk_lanes // half))
    ahead = jnp.roll(x, -half, axis=1)
    behind = jnp.roll(x, half, axis=1)
    rotated = jnp.where((within < half)[None, :], x * cosine - ahead * sine,
                        x * cosine + behind * sine)
    qk = rotated.astype(jnp.bfloat16)
    value_new = projected[:, qk_lanes:].astype(jnp.bfloat16)
    first = migrate_first(pool, mig_src, row_count)
    mixed, landed = attend(qk, value_new, page_table, lengths, pool,
                           lambda dep: migrate_rest(pool, mig_src, row_count, first, dep))
    mixed = mixed.reshape(req_row, heads_here * HEAD_DIM)
    mixed_all = lax.all_gather(mixed, "row", axis=0, tiled=True)
    chosen = deal
    col_count = lax.axis_size("col")
    partial = jnp.dot(
        jnp.take(mixed_all, chosen, axis=0), w_out, preferred_element_type=jnp.float32
    ).astype(jnp.bfloat16)
    parts = lax.all_to_all(partial, "col", split_axis=0, concat_axis=0, tiled=True)
    attended = jnp.sum(
        parts.reshape(col_count, rows_all // col_count, -1).astype(jnp.float32), axis=0
    ).astype(jnp.bfloat16)
    return (attended, landed)


def solution(mesh):
    placed = (
        P("col", "row"),
        P("row", "col"),
        P("col", "row"),
        P("row", None, "col"),
        P("row", None),
        P("row"),
        P(),
        P(),
    )
    return jax.shard_map(
        on_device,
        mesh=mesh,
        in_specs=placed,
        out_specs=(P("col", "row"), P("row", None, "col")),
        check_vma=False,
    )
```
